32 devices in a mesh: row: 8 (over y, x, core), col: 4 (over z).
Axes of the slice: x: 2, y: 2, z: 4, core: 2. Of those that a mesh axis runs over, the one named last changes fastest.
Arguments:
- pair_rep: bfloat16 [128, 128, 128], P(('row', 'col')), may hold values from -16 to 16
- tile_mask: int32 [1, 1], replicated, may hold values from 0 to 1, as said below
- chain_ids: int32 [128], replicated, may hold values from 0 to 3, never falling along the last dimension, each value on 1 to 64 neighbouring positions
- chain_bias: float32 [2, 4], replicated, may hold values from -6 to 6
- row_project: bfloat16 [128, 512], replicated, may hold values from -0.5 to 0.5
- row_bias_proj: bfloat16 [128, 4], replicated, may hold values from -36 to 36
- row_output: bfloat16 [128, 128], replicated, may hold values from -0.5 to 0.5
- col_project: bfloat16 [128, 512], replicated, may hold values from -0.5 to 0.5
- col_bias_proj: bfloat16 [128, 4], replicated, may hold values from -36 to 36
- col_output: bfloat16 [128, 128], replicated, may hold values from -0.5 to 0.5
- tri_left: bfloat16 [128, 256], replicated, may hold values from -0.5 to 0.5
- tri_right: bfloat16 [128, 256], replicated, may hold values from -0.5 to 0.5
- tri_gate: bfloat16 [128, 128], replicated, may hold values from -0.5 to 0.5
- tri_output: bfloat16 [128, 128], replicated, may hold values from -1.5 to 1.5
Outputs:
- pair_out: bfloat16 [128, 128, 128], P('row', 'col')
The draws below stay inside these ranges and needn't reach their ends.
Inputs may be any that keep to these rules, and one draw needn't show every extreme that they name: `tile_mask`: every diagonal entry is 1. `chain_ids`: chain numbers never fall along the residues.
All inputs are finite; a program needn't handle non-finite values.
Results may differ from the reference program's by a relative error of at most 0.018.
Values may be sent and summed in bfloat16 or wider, within the bound.
No kernel may reach another device: no remote copies, remote signals or barrier semaphores. Data moves between devices by JAX's collectives and lax.ppermute only.
A program may use at most 64 MiB of HBM per device.

```python
import math
import jax
import jax.numpy as jnp
import numpy as np
from jax import lax

C = 128
HEADS = 4
HEAD_DIM = 32
TILE = 128
CHAINS = 4
RES = 128
TILES = 1


def bias_weights(key):
    row_part = jax.random.truncated_normal(jax.random.fold_in(key, 17), -3.0, 3.0, (C, HEADS), jnp.float32) * (0.75 * C ** (-0.5))
    col_part = jax.random.truncated_normal(jax.random.fold_in(key, 29), -3.0, 3.0, (C, HEADS), jnp.float32) * (0.75 * C ** (-0.5))
    return (row_part, col_part)


def draw_row_bias_proj(key, part):
    return bias_weights(key)[0].astype(jnp.bfloat16)


def draw_col_bias_proj(key, part):
    return bias_weights(key)[1].astype(jnp.bfloat16)


def draw_pair_rep(key, part):
    values = jax.random.truncated_normal(jax.random.fold_in(key, 3), -4.0, 4.0, (RES, RES, C), jnp.float32)
    return values.astype(jnp.bfloat16)


def draw_tile_mask(key, part):
    density = jax.random.randint(jax.random.fold_in(key, 41), (TILES, 1), 0, 2)
    rolled = jax.random.randint(jax.random.fold_in(key, 43), (TILES, TILES), 0, 8)
    diagonal = jnp.arange(TILES)[:, None] == jnp.arange(TILES)[None, :]
    return jnp.where(diagonal, 1, (rolled < density).astype(jnp.int32)).astype(jnp.int32)


def length_profile(number_of, total, bound, skew):
    portions = [(1 << 20) // math.isqrt(standing ** skew) + 1 for standing in range(2, number_of + 1)]
    rest, given = total - bound - (number_of - 1), [1] * (number_of - 1)
    while rest > 0:
        free = [i for i in range(number_of - 1) if given[i] < bound]
        pool, budget = sum([portions[i] for i in free]), rest
        for i in free:
            extra = min(bound - given[i], max(1, budget * portions[i] // pool), rest)
            given[i] = given[i] + extra
            rest = rest - extra
    return np.array([bound] + given)


def uneven(key, number_of, total, bound, lean):
    if number_of == 2:
        one = jax.random.randint(key, (), max(1, total - bound), min(bound, total - 1) + 1)
        return jnp.stack([one, total - one])
    lengths = jnp.asarray(length_profile(number_of, total, bound, lean), jnp.int32)
    twos = (number_of - 1) // 2
    giver, receiver = lengths[1:1 + 2 * twos:2], lengths[2:2 + 2 * twos:2]
    slack = jnp.minimum(giver - 1, bound - receiver)
    shifted = jax.random.randint(jax.random.fold_in(key, 1), (twos,), 0, 1 << 20) % (slack + 1)
    lengths = lengths.at[1:1 + 2 * twos:2].set(giver - shifted).at[2:2 + 2 * twos:2].set(receiver + shifted)
    return lengths[jax.random.permutation(jax.random.fold_in(key, 2), number_of)]


def bell_draw(rng, shape, scale, reach, dtype=jnp.bfloat16):
    result = scale * jax.random.normal(rng, shape, jnp.float32)
    return jnp.clip(result, min=-reach, max=reach).astype(dtype)


def setup_inputs(seed: int = 0) -> dict:
    seeds = jax.random.split(jax.random.key(seed), 15)
    pair_rep = draw_pair_rep(jax.random.fold_in(seeds[14], 71), 0)
    tile_mask = draw_tile_mask(jax.random.fold_in(seeds[14], 71), 0)
    chain_ids = jnp.searchsorted(jnp.cumsum(uneven(seeds[2], CHAINS, RES, RES // 2, 1)), jnp.arange(RES), side="right").astype(jnp.int32)
    chain_bias = bell_draw(seeds[3], (2, HEADS), 1.5, 6.0, jnp.float32)
    row_project = bell_draw(seeds[4], (C, 4 * C), C ** -0.5, 0.5)
    row_bias_proj = draw_row_bias_proj(jax.random.fold_in(seeds[14], 71), 0)
    row_output = bell_draw(seeds[6], (C, C), C ** -0.5, 0.5)
    col_project = bell_draw(seeds[7], (C, 4 * C), C ** -0.5, 0.5)
    col_bias_proj = draw_col_bias_proj(jax.random.fold_in(seeds[14], 71), 0)
    col_output = bell_draw(seeds[9], (C, C), C ** -0.5, 0.5)
    tri_left = bell_draw(seeds[10], (C, 2 * C), C ** -0.5, 0.5)
    tri_right = bell_draw(seeds[11], (C, 2 * C), C ** -0.5, 0.5)
    tri_gate = bell_draw(seeds[12], (C, C), C ** -0.5, 0.5)
    tri_output = bell_draw(seeds[13], (C, C), (C / 9) ** -0.5, 1.5)
    return {"pair_rep": pair_rep, "tile_mask": tile_mask, "chain_ids": chain_ids, "chain_bias": chain_bias, "row_project": row_project, "row_bias_proj": row_bias_proj, "row_output": row_output, "col_project": col_project, "col_bias_proj": col_bias_proj, "col_output": col_output, "tri_left": tri_left, "tri_right": tri_right, "tri_gate": tri_gate, "tri_output": tri_output}


def layer_norm(values):
    values = values.astype(jnp.float32)
    center = values - lax.optimization_barrier(jnp.mean(values, axis=-1, keepdims=True))
    spread = lax.optimization_barrier(jnp.mean(center * center, axis=-1, keepdims=True))
    return center * lax.rsqrt(spread + 1e-05)

def triangle_attention(pair_in, allowed, chain_ids, chain_add, project, bias_proj, output):
    normed = layer_norm(pair_in).astype(jnp.bfloat16)
    flat_rows = normed.reshape(RES * RES, C)
    projected = jnp.dot(flat_rows, project, preferred_element_type=jnp.float32).reshape(RES, RES, 4 * C)
    queries = projected[..., :C].astype(jnp.bfloat16).reshape(RES, RES, HEADS, HEAD_DIM)
    key_rows = projected[..., C:2 * C].astype(jnp.bfloat16).reshape(RES, RES, HEADS, HEAD_DIM)
    value_rows = projected[..., 2 * C:3 * C].astype(jnp.bfloat16).reshape(RES, RES, HEADS, HEAD_DIM)
    bias_all = jnp.dot(flat_rows, bias_proj, preferred_element_type=jnp.float32).reshape(RES, RES, HEADS).transpose(2, 0, 1)
    same_chain = (chain_ids[:, None] == chain_ids[None, :]).astype(jnp.float32)

    def one_line(inputs):
        query_line, key_line, value_line, usable = inputs
        scores = jnp.einsum('qhd,khd->hqk', query_line.astype(jnp.float32), key_line.astype(jnp.float32)) * HEAD_DIM ** (-0.5)
        scores = scores + bias_all
        scores = scores + chain_add[:, None, None] * same_chain[None]
        scores = jnp.where(usable[None, None, :], scores, -1000000000.0)
        row_peak = lax.optimization_barrier(jnp.max(scores, axis=-1, keepdims=True))
        weights = jnp.exp(scores - row_peak)
        attention = (weights / lax.optimization_barrier(jnp.sum(weights, axis=-1, keepdims=True))).astype(jnp.bfloat16)
        mixed_rows = jnp.einsum('hqk,khd->qhd', attention.astype(jnp.float32), value_line.astype(jnp.float32))
        return mixed_rows.reshape(RES, C)
    mixed_all = lax.map(one_line, (queries, key_rows, value_rows, allowed))
    gated = (mixed_all * jax.nn.sigmoid(projected[..., 3 * C:])).astype(jnp.bfloat16)
    update = jnp.dot(gated.reshape(RES * RES, C), output, preferred_element_type=jnp.float32).reshape(RES, RES, C)
    return (pair_in.astype(jnp.float32) + update).astype(jnp.bfloat16)

def reference(pair_rep, tile_mask, chain_ids, chain_bias, row_project, row_bias_proj, row_output, col_project, col_bias_proj, col_output, tri_left, tri_right, tri_gate, tri_output):
    allowed = jnp.repeat(jnp.repeat(tile_mask, TILE, axis=0), TILE, axis=1) > 0
    first_pair = triangle_attention(pair_rep, allowed, chain_ids, chain_bias[0], row_project, row_bias_proj, row_output)
    flipped = triangle_attention(first_pair.transpose(1, 0, 2), allowed.T, chain_ids, chain_bias[1], col_project, col_bias_proj, col_output)
    second_pair = flipped.transpose(1, 0, 2)
    normed = layer_norm(second_pair).astype(jnp.bfloat16)
    flat_rows = normed.reshape(RES * RES, C)
    mask_float = allowed.astype(jnp.float32)
    left_proj = jnp.dot(flat_rows, tri_left, preferred_element_type=jnp.float32).reshape(RES, RES, 2 * C)
    right_proj = jnp.dot(flat_rows, tri_right, preferred_element_type=jnp.float32).reshape(RES, RES, 2 * C)
    left_act = (jax.nn.sigmoid(left_proj[..., C:]) * left_proj[..., :C] * mask_float[..., None]).astype(jnp.bfloat16)
    right_act = (jax.nn.sigmoid(right_proj[..., C:]) * right_proj[..., :C] * mask_float[..., None]).astype(jnp.bfloat16)
    product_sum = jnp.einsum('ikc,jkc->ijc', left_act.astype(jnp.float32), right_act.astype(jnp.float32))
    centered = layer_norm(product_sum).astype(jnp.bfloat16)
    gate_values = jax.nn.sigmoid(jnp.dot(flat_rows, tri_gate, preferred_element_type=jnp.float32).reshape(RES, RES, C))
    update = jnp.dot(centered.reshape(RES * RES, C), tri_output, preferred_element_type=jnp.float32).reshape(RES, RES, C)
    return (second_pair.astype(jnp.float32) + gate_values * update).astype(jnp.bfloat16)
```

```python
import jax
import jax.numpy as jnp
from jax import lax
from jax.sharding import PartitionSpec as P


def layer_norm(values):
    values = values.astype(jnp.float32)
    center = values - jnp.mean(values, axis=-1, keepdims=True)
    spread = jnp.mean(center * center, axis=-1, keepdims=True)
    return center * lax.rsqrt(spread + 1e-05)


def tile_rows(positions, tile_table, length):
    tile_count = tile_table.shape[0]
    tile_width = length // tile_count
    onehot = (positions[:, None] // tile_width == jnp.arange(tile_count)[None, :]).astype(
        jnp.float32
    )
    picked = jnp.dot(onehot, tile_table.astype(jnp.float32))
    spread_out = jnp.broadcast_to(picked[:, :, None], (positions.shape[0], tile_count, tile_width))
    return spread_out.reshape(positions.shape[0], length) > 0.5


def tile_pairs(row_pos, col_pos, tile_table, length):
    tile_count = tile_table.shape[0]
    tile_width = length // tile_count
    row_hot = (row_pos[:, None] // tile_width == jnp.arange(tile_count)[None, :]).astype(
        jnp.float32
    )
    col_hot = (col_pos[:, None] // tile_width == jnp.arange(tile_count)[None, :]).astype(
        jnp.float32
    )
    return jnp.dot(jnp.dot(row_hot, tile_table.astype(jnp.float32)), col_hot.T)


def attend_lines(
    queries,
    key_rows,
    value_rows,
    gate_pre,
    bias_all,
    key_ok,
    chain_ids,
    chain_add,
    line_dim,
    flipped,
):
    line_count = queries.shape[line_dim]
    length = queries.shape[1 - line_dim]
    head_count = queries.shape[2]
    head_size = queries.shape[3]
    width_all = head_count * head_size
    query_rows = min(128, length)
    per_line = length // query_rows
    scaling = head_size ** (-0.5)

    def one_block(block_index):
        line_index = block_index // per_line
        offset = block_index % per_line * query_rows
        query_line = lax.dynamic_index_in_dim(queries, line_index, line_dim, keepdims=False)
        query_block = lax.dynamic_slice_in_dim(query_line, offset, query_rows, 0)
        key_line = lax.dynamic_index_in_dim(key_rows, line_index, line_dim, keepdims=False)
        value_line = lax.dynamic_index_in_dim(value_rows, line_index, line_dim, keepdims=False)
        scores = (
            jnp.einsum("qhd,khd->hqk", query_block, key_line, preferred_element_type=jnp.float32)
            * scaling
        )
        if flipped:
            bias_block = lax.dynamic_slice_in_dim(bias_all, offset, query_rows, 2).transpose(
                0, 2, 1
            )
        else:
            bias_block = lax.dynamic_slice_in_dim(bias_all, offset, query_rows, 1)
        scores = scores + bias_block
        chain_block = lax.dynamic_slice_in_dim(chain_ids, offset, query_rows, 0)
        same_chain = (chain_block[:, None] == chain_ids[None, :]).astype(jnp.float32)
        scores = scores + chain_add[:, None, None] * same_chain[None]
        usable = lax.dynamic_index_in_dim(key_ok, line_index, 0, keepdims=False)
        scores = jnp.where(usable[None, None, :], scores, -1000000000.0)
        row_peak = jnp.max(scores, axis=-1, keepdims=True)
        weights = jnp.exp(scores - row_peak)
        attention = (weights / jnp.sum(weights, axis=-1, keepdims=True)).astype(jnp.bfloat16)
        mixed_rows = jnp.einsum(
            "hqk,khd->qhd", attention, value_line, preferred_element_type=jnp.float32
        ).reshape(query_rows, width_all)
        gate_line = lax.dynamic_index_in_dim(gate_pre, line_index, line_dim, keepdims=False)
        gate_block = lax.dynamic_slice_in_dim(gate_line, offset, query_rows, 0)
        return (mixed_rows * jax.nn.sigmoid(gate_block)).astype(jnp.bfloat16)

    outputs = lax.map(one_block, jnp.arange(line_count * per_line, dtype=jnp.int32))
    outputs = outputs.reshape(line_count, length, width_all)
    if line_dim == 1:
        outputs = outputs.transpose(1, 0, 2)
    return outputs


def tri_acts(normed, weights, allowed):
    channels = normed.shape[-1]
    projected = jnp.dot(normed.reshape(-1, channels), weights, preferred_element_type=jnp.float32)
    projected = projected.reshape(normed.shape[0], normed.shape[1], 2 * channels)
    return (
        jax.nn.sigmoid(projected[..., channels:]) * projected[..., :channels] * allowed[..., None]
    ).astype(jnp.bfloat16)


def gather_lines(piece):
    device_count = lax.axis_size("row") * lax.axis_size("col")
    sent = jnp.broadcast_to(piece[None], (device_count,) + piece.shape)
    got = lax.all_to_all(sent, ("row", "col"), 0, 0, tiled=True)
    heads, rows_here, length = piece.shape
    return got.transpose(1, 0, 2, 3).reshape(heads, device_count * rows_here, length)


def shards(
    pair_rep,
    tile_mask,
    chain_ids,
    chain_bias,
    row_project,
    row_bias_proj,
    row_output,
    col_project,
    col_bias_proj,
    col_output,
    tri_left,
    tri_right,
    tri_gate,
    tri_output,
):
    n_row = lax.axis_size("row")
    n_col = lax.axis_size("col")
    device_count = n_row * n_col
    rows_here, length, channels = pair_rep.shape
    head_count = row_bias_proj.shape[1]
    head_size = channels // head_count
    row_index = lax.axis_index("row")
    col_index = lax.axis_index("col")
    device_index = row_index * n_col + col_index
    block_rows = length // n_row
    block_cols = length // n_col
    local_lines = device_index * rows_here + jnp.arange(rows_here, dtype=jnp.int32)
    local_cols = col_index * block_cols + row_index * rows_here + jnp.arange(rows_here, dtype=jnp.int32)
    normed = layer_norm(pair_rep).astype(jnp.bfloat16)
    flat_rows = normed.reshape(rows_here * length, channels)
    bias_rows = jnp.dot(flat_rows, row_bias_proj, preferred_element_type=jnp.float32)
    bias_rows = bias_rows.reshape(rows_here, length, head_count).transpose(2, 0, 1)
    bias_all = gather_lines(bias_rows)
    projected = jnp.dot(flat_rows, row_project, preferred_element_type=jnp.float32).reshape(
        rows_here, length, 4 * channels
    )
    qkv_rows = (
        projected[..., : 3 * channels]
        .astype(jnp.bfloat16)
        .reshape(rows_here, length, 3, head_count, head_size)
    )
    key_ok = tile_rows(local_lines, tile_mask, length)
    mixed_rows = attend_lines(
        qkv_rows[:, :, 0],
        qkv_rows[:, :, 1],
        qkv_rows[:, :, 2],
        projected[..., 3 * channels :],
        bias_all,
        key_ok,
        chain_ids,
        chain_bias[0],
        0,
        False,
    )
    update = jnp.dot(
        mixed_rows.reshape(-1, channels), row_output, preferred_element_type=jnp.float32
    ).reshape(rows_here, length, channels)
    first_pair = (pair_rep.astype(jnp.float32) + update).astype(jnp.bfloat16)
    normed_first = layer_norm(first_pair).astype(jnp.bfloat16)
    bias_next = jnp.dot(
        normed_first.reshape(-1, channels), col_bias_proj, preferred_element_type=jnp.float32
    )
    bias_next = bias_next.reshape(rows_here, length, head_count).transpose(2, 0, 1)
    bias_cols = gather_lines(bias_next)
    first_sent = (
        first_pair.reshape(rows_here, n_col, n_row, rows_here, channels)
        .transpose(0, 2, 1, 3, 4)
        .reshape(rows_here, length, channels)
    )
    columns = lax.all_to_all(first_sent, ("row", "col"), split_axis=1, concat_axis=0, tiled=True)
    normed_cols = layer_norm(columns).astype(jnp.bfloat16)
    projected_cols = jnp.dot(
        normed_cols.reshape(-1, channels), col_project, preferred_element_type=jnp.float32
    ).reshape(length, rows_here, 4 * channels)
    qkv_cols = (
        projected_cols[..., : 3 * channels]
        .astype(jnp.bfloat16)
        .reshape(length, rows_here, 3, head_count, head_size)
    )
    col_ok = tile_rows(local_cols, tile_mask.T, length)
    mixed_cols = attend_lines(
        qkv_cols[:, :, 0],
        qkv_cols[:, :, 1],
        qkv_cols[:, :, 2],
        projected_cols[..., 3 * channels :],
        bias_cols,
        col_ok,
        chain_ids,
        chain_bias[1],
        1,
        True,
    )
    update_cols = jnp.dot(
        mixed_cols.reshape(-1, channels), col_output, preferred_element_type=jnp.float32
    ).reshape(length, rows_here, channels)
    second_pair = (columns.astype(jnp.float32) + update_cols).astype(jnp.bfloat16)
    normed_second = layer_norm(second_pair).astype(jnp.bfloat16)
    edge_mask = tile_pairs(jnp.arange(length, dtype=jnp.int32), local_cols, tile_mask, length)
    left_all = tri_acts(normed_second, tri_left, edge_mask)
    right_all = tri_acts(normed_second, tri_right, edge_mask)
    raw_got = lax.all_to_all(
        second_pair.reshape(n_row, block_rows, rows_here, channels), "row", 0, 0, tiled=True
    )
    own_pair = raw_got.transpose(1, 0, 2, 3).reshape(block_rows, block_cols, channels)
    left_send = jnp.broadcast_to(
        left_all.reshape(n_row, 1, block_rows, rows_here, channels),
        (n_row, n_col, block_rows, rows_here, channels),
    )
    right_send = jnp.broadcast_to(
        right_all.reshape(1, n_col, block_cols, rows_here, channels),
        (n_row, n_col, block_cols, rows_here, channels),
    )
    outgoing = jnp.concatenate([left_send, right_send], axis=2).reshape(
        device_count, block_rows + block_cols, rows_here, channels
    )
    received = lax.all_to_all(outgoing, ("row", "col"), split_axis=0, concat_axis=0, tiled=True)
    product_sum = jnp.einsum(
        "sikc,sjkc->ijc",
        received[:, :block_rows],
        received[:, block_rows:],
        preferred_element_type=jnp.float32,
    )
    normed_own = layer_norm(own_pair).astype(jnp.bfloat16)
    gate_values = jax.nn.sigmoid(
        jnp.dot(normed_own.reshape(-1, channels), tri_gate, preferred_element_type=jnp.float32)
    ).reshape(block_rows, block_cols, channels)
    centered = layer_norm(product_sum).astype(jnp.bfloat16)
    update_tri = jnp.dot(
        centered.reshape(-1, channels), tri_output, preferred_element_type=jnp.float32
    ).reshape(block_rows, block_cols, channels)
    return (own_pair.astype(jnp.float32) + gate_values * update_tri).astype(jnp.bfloat16)


def solution(mesh):
    return jax.shard_map(
        shards,
        mesh=mesh,
        in_specs=(
            P(("row", "col"), None, None),
            P(),
            P(),
            P(),
            P(),
            P(),
            P(),
            P(),
            P(),
            P(),
            P(),
            P(),
            P(),
            P(),
        ),
        out_specs=P("row", "col", None),
        check_vma=False,
    )
```

```python
import jax
import jax.numpy as jnp
from jax import lax
from jax.sharding import PartitionSpec as P


def layer_norm(values):
    values = values.astype(jnp.float32)
    center = values - jnp.mean(values, axis=-1, keepdims=True)
    spread = jnp.mean(center * center, axis=-1, keepdims=True)
    return center * lax.rsqrt(spread + 1e-05)


def tile_rows(positions, tile_table, length):
    tile_count = tile_table.shape[0]
    tile_width = length // tile_count
    onehot = (positions[:, None] // tile_width == jnp.arange(tile_count)[None, :]).astype(
        jnp.float32
    )
    picked = jnp.dot(onehot, tile_table.astype(jnp.float32))
    spread_out = jnp.broadcast_to(picked[:, :, None], (positions.shape[0], tile_count, tile_width))
    return spread_out.reshape(positions.shape[0], length) > 0.5


def tile_pairs(row_pos, col_pos, tile_table, length):
    tile_count = tile_table.shape[0]
    tile_width = length // tile_count
    row_hot = (row_pos[:, None] // tile_width == jnp.arange(tile_count)[None, :]).astype(
        jnp.float32
    )
    col_hot = (col_pos[:, None] // tile_width == jnp.arange(tile_count)[None, :]).astype(
        jnp.float32
    )
    return jnp.dot(jnp.dot(row_hot, tile_table.astype(jnp.float32)), col_hot.T)


def attend_lines(
    queries,
    key_rows,
    value_rows,
    gate_pre,
    bias_all,
    key_ok,
    chain_ids,
    chain_add,
    line_dim,
    flipped,
):
    length = queries.shape[1 - line_dim]
    head_count = queries.shape[2]
    head_size = queries.shape[3]
    width_all = head_count * head_size
    query_rows = min(128, length)
    blocks = length // query_rows
    scaling = head_size ** (-0.5)
    spec_q = "lqhd" if line_dim == 0 else "qlhd"
    spec_k = "lkhd" if line_dim == 0 else "klhd"
    usable = key_ok[:, None, None, :]

    def one_block(offset):
        query_block = lax.dynamic_slice_in_dim(queries, offset, query_rows, 1 - line_dim)
        scores = (
            jnp.einsum(
                f"{spec_q},{spec_k}->lhqk",
                query_block,
                key_rows,
                preferred_element_type=jnp.float32,
            )
            * scaling
        )
        if flipped:
            bias_block = lax.dynamic_slice_in_dim(bias_all, offset, query_rows, 2).transpose(
                0, 2, 1
            )
        else:
            bias_block = lax.dynamic_slice_in_dim(bias_all, offset, query_rows, 1)
        scores = scores + bias_block[None]
        chain_block = lax.dynamic_slice_in_dim(chain_ids, offset, query_rows, 0)
        same_chain = (chain_block[:, None] == chain_ids[None, :]).astype(jnp.float32)
        scores = scores + (chain_add[:, None, None] * same_chain[None])[None]
        scores = jnp.where(usable, scores, -1000000000.0)
        row_peak = jnp.max(scores, axis=-1, keepdims=True)
        weights = jnp.exp(scores - row_peak)
        attention = (weights / jnp.sum(weights, axis=-1, keepdims=True)).astype(jnp.bfloat16)
        mixed_rows = jnp.einsum(
            f"lhqk,{spec_k}->{spec_q}", attention, value_rows, preferred_element_type=jnp.float32
        )
        mixed_rows = mixed_rows.reshape(mixed_rows.shape[:2] + (width_all,))
        gate_block = lax.dynamic_slice_in_dim(gate_pre, offset, query_rows, 1 - line_dim)
        return (mixed_rows * jax.nn.sigmoid(gate_block)).astype(jnp.bfloat16)

    if blocks == 1:
        return one_block(0)
    outputs = lax.map(one_block, jnp.arange(blocks, dtype=jnp.int32) * query_rows)
    if line_dim == 0:
        outputs = outputs.transpose(1, 0, 2, 3)
    return outputs.reshape(gate_pre.shape[:2] + (width_all,))


def tri_acts(normed, weights, allowed):
    channels = normed.shape[-1]
    projected = jnp.dot(normed.reshape(-1, channels), weights, preferred_element_type=jnp.float32)
    projected = projected.reshape(normed.shape[0], normed.shape[1], 2 * channels)
    return (
        jax.nn.sigmoid(projected[..., channels:]) * projected[..., :channels] * allowed[..., None]
    ).astype(jnp.bfloat16)


def gather_lines(piece):
    device_count = lax.axis_size("row") * lax.axis_size("col")
    sent = jnp.broadcast_to(piece[None], (device_count,) + piece.shape)
    got = lax.all_to_all(sent, ("row", "col"), 0, 0, tiled=True)
    heads, rows_here, length = piece.shape
    return got.transpose(1, 0, 2, 3).reshape(heads, device_count * rows_here, length)


def shards(
    pair_rep,
    tile_mask,
    chain_ids,
    chain_bias,
    row_project,
    row_bias_proj,
    row_output,
    col_project,
    col_bias_proj,
    col_output,
    tri_left,
    tri_right,
    tri_gate,
    tri_output,
):
    n_row = lax.axis_size("row")
    n_col = lax.axis_size("col")
    device_count = n_row * n_col
    rows_here, length, channels = pair_rep.shape
    head_count = row_bias_proj.shape[1]
    head_size = channels // head_count
    row_index = lax.axis_index("row")
    col_index = lax.axis_index("col")
    device_index = row_index * n_col + col_index
    block_rows = length // n_row
    block_cols = length // n_col
    local_lines = device_index * rows_here + jnp.arange(rows_here, dtype=jnp.int32)
    local_cols = col_index * block_cols + row_index * rows_here + jnp.arange(rows_here, dtype=jnp.int32)
    normed = layer_norm(pair_rep).astype(jnp.bfloat16)
    flat_rows = normed.reshape(rows_here * length, channels)
    bias_rows = jnp.dot(flat_rows, row_bias_proj, preferred_element_type=jnp.float32)
    bias_rows = bias_rows.reshape(rows_here, length, head_count).transpose(2, 0, 1)
    bias_all = gather_lines(bias_rows)
    projected = jnp.dot(flat_rows, row_project, preferred_element_type=jnp.float32).reshape(
        rows_here, length, 4 * channels
    )
    qkv_rows = (
        projected[..., : 3 * channels]
        .astype(jnp.bfloat16)
        .reshape(rows_here, length, 3, head_count, head_size)
    )
    key_ok = tile_rows(local_lines, tile_mask, length)
    mixed_rows = attend_lines(
        qkv_rows[:, :, 0],
        qkv_rows[:, :, 1],
        qkv_rows[:, :, 2],
        projected[..., 3 * channels :],
        bias_all,
        key_ok,
        chain_ids,
        chain_bias[0],
        0,
        False,
    )
    update = jnp.dot(
        mixed_rows.reshape(-1, channels), row_output, preferred_element_type=jnp.float32
    ).reshape(rows_here, length, channels)
    first_pair = (pair_rep.astype(jnp.float32) + update).astype(jnp.bfloat16)
    normed_first = layer_norm(first_pair).astype(jnp.bfloat16)
    bias_next = jnp.dot(
        normed_first.reshape(-1, channels), col_bias_proj, preferred_element_type=jnp.float32
    )
    bias_next = bias_next.reshape(rows_here, length, head_count).transpose(2, 0, 1)
    pair_chunks = (
        first_pair.reshape(rows_here, n_col, n_row, rows_here, channels)
        .transpose(2, 1, 0, 3, 4)
        .reshape(device_count, rows_here * rows_here * channels)
        .astype(jnp.float32)
    )
    bias_chunks = jnp.broadcast_to(
        bias_next.reshape(1, -1), (device_count, head_count * rows_here * length)
    )
    merged = lax.all_to_all(
        jnp.concatenate([pair_chunks, bias_chunks], axis=1), ("row", "col"), 0, 0, tiled=True
    )
    pair_size = rows_here * rows_here * channels
    columns = (
        merged[:, :pair_size].astype(jnp.bfloat16).reshape(length, rows_here, channels)
    )
    bias_cols = (
        merged[:, pair_size:]
        .reshape(device_count, head_count, rows_here, length)
        .transpose(1, 0, 2, 3)
        .reshape(head_count, length, length)
    )
    normed_cols = layer_norm(columns).astype(jnp.bfloat16)
    projected_cols = jnp.dot(
        normed_cols.reshape(-1, channels), col_project, preferred_element_type=jnp.float32
    ).reshape(length, rows_here, 4 * channels)
    qkv_cols = (
        projected_cols[..., : 3 * channels]
        .astype(jnp.bfloat16)
        .reshape(length, rows_here, 3, head_count, head_size)
    )
    col_ok = tile_rows(local_cols, tile_mask.T, length)
    mixed_cols = attend_lines(
        qkv_cols[:, :, 0],
        qkv_cols[:, :, 1],
        qkv_cols[:, :, 2],
        projected_cols[..., 3 * channels :],
        bias_cols,
        col_ok,
        chain_ids,
        chain_bias[1],
        1,
        True,
    )
    update_cols = jnp.dot(
        mixed_cols.reshape(-1, channels), col_output, preferred_element_type=jnp.float32
    ).reshape(length, rows_here, channels)
    second_pair = (columns.astype(jnp.float32) + update_cols).astype(jnp.bfloat16)
    normed_second = layer_norm(second_pair).astype(jnp.bfloat16)
    edge_mask = tile_pairs(jnp.arange(length, dtype=jnp.int32), local_cols, tile_mask, length)
    left_all = tri_acts(normed_second, tri_left, edge_mask)
    right_all = tri_acts(normed_second, tri_right, edge_mask)
    raw_got = lax.all_to_all(
        second_pair.reshape(n_row, block_rows, rows_here, channels), "row", 0, 0, tiled=True
    )
    own_pair = raw_got.transpose(1, 0, 2, 3).reshape(block_rows, block_cols, channels)
    left_send = jnp.broadcast_to(
        left_all.reshape(n_row, 1, block_rows, rows_here, channels),
        (n_row, n_col, block_rows, rows_here, channels),
    )
    right_send = jnp.broadcast_to(
        right_all.reshape(1, n_col, block_cols, rows_here, channels),
        (n_row, n_col, block_cols, rows_here, channels),
    )
    outgoing = jnp.concatenate([left_send, right_send], axis=2).reshape(
        device_count, block_rows + block_cols, rows_here, channels
    )
    received = lax.all_to_all(outgoing, ("row", "col"), split_axis=0, concat_axis=0, tiled=True)
    product_sum = jnp.einsum(
        "sikc,sjkc->ijc",
        received[:, :block_rows],
        received[:, block_rows:],
        preferred_element_type=jnp.float32,
    )
    normed_own = layer_norm(own_pair).astype(jnp.bfloat16)
    gate_values = jax.nn.sigmoid(
        jnp.dot(normed_own.reshape(-1, channels), tri_gate, preferred_element_type=jnp.float32)
    ).reshape(block_rows, block_cols, channels)
    centered = layer_norm(product_sum).astype(jnp.bfloat16)
    update_tri = jnp.dot(
        centered.reshape(-1, channels), tri_output, preferred_element_type=jnp.float32
    ).reshape(block_rows, block_cols, channels)
    return (own_pair.astype(jnp.float32) + gate_values * update_tri).astype(jnp.bfloat16)


def solution(mesh):
    return jax.shard_map(
        shards,
        mesh=mesh,
        in_specs=(
            P(("row", "col"), None, None),
            P(),
            P(),
            P(),
            P(),
            P(),
            P(),
            P(),
            P(),
            P(),
            P(),
            P(),
            P(),
            P(),
        ),
        out_specs=P("row", "col", None),
        check_vma=False,
    )
```

```python
import jax
import jax.numpy as jnp
from jax import lax
from jax.sharding import PartitionSpec as P


def layer_norm(values):
    values = values.astype(jnp.float32)
    center = values - jnp.mean(values, axis=-1, keepdims=True)
    spread = jnp.mean(center * center, axis=-1, keepdims=True)
    return center * lax.rsqrt(spread + 1e-05)


def tile_rows(positions, tile_table, length):
    tile_count = tile_table.shape[0]
    tile_width = length // tile_count
    onehot = (positions[:, None] // tile_width == jnp.arange(tile_count)[None, :]).astype(
        jnp.float32
    )
    picked = jnp.dot(onehot, tile_table.astype(jnp.float32))
    spread_out = jnp.broadcast_to(picked[:, :, None], (positions.shape[0], tile_count, tile_width))
    return spread_out.reshape(positions.shape[0], length) > 0.5


def tile_pairs(row_pos, col_pos, tile_table, length):
    tile_count = tile_table.shape[0]
    tile_width = length // tile_count
    row_hot = (row_pos[:, None] // tile_width == jnp.arange(tile_count)[None, :]).astype(
        jnp.float32
    )
    col_hot = (col_pos[:, None] // tile_width == jnp.arange(tile_count)[None, :]).astype(
        jnp.float32
    )
    return jnp.dot(jnp.dot(row_hot, tile_table.astype(jnp.float32)), col_hot.T)


def attend_lines(
    queries,
    key_rows,
    value_rows,
    gate_pre,
    bias_all,
    key_ok,
    chain_ids,
    chain_add,
    line_dim,
    flipped,
):
    length = queries.shape[1 - line_dim]
    head_count = queries.shape[2]
    head_size = queries.shape[3]
    width_all = head_count * head_size
    query_rows = min(128, length)
    blocks = length // query_rows
    scaling = head_size ** (-0.5)
    spec_q = "lqhd" if line_dim == 0 else "qlhd"
    spec_k = "lkhd" if line_dim == 0 else "klhd"
    usable = key_ok[:, None, None, :]

    def one_block(offset):
        query_block = lax.dynamic_slice_in_dim(queries, offset, query_rows, 1 - line_dim)
        scores = (
            jnp.einsum(
                f"{spec_q},{spec_k}->lhqk",
                query_block,
                key_rows,
                preferred_element_type=jnp.float32,
            )
            * scaling
        )
        if flipped:
            bias_block = lax.dynamic_slice_in_dim(bias_all, offset, query_rows, 2).transpose(
                0, 2, 1
            )
        else:
            bias_block = lax.dynamic_slice_in_dim(bias_all, offset, query_rows, 1)
        scores = scores + bias_block[None]
        chain_block = lax.dynamic_slice_in_dim(chain_ids, offset, query_rows, 0)
        same_chain = (chain_block[:, None] == chain_ids[None, :]).astype(jnp.float32)
        scores = scores + (chain_add[:, None, None] * same_chain[None])[None]
        scores = jnp.where(usable, scores, -1000000000.0)
        row_peak = jnp.max(scores, axis=-1, keepdims=True)
        weights = jnp.exp(scores - row_peak)
        attention = (weights / jnp.sum(weights, axis=-1, keepdims=True)).astype(jnp.bfloat16)
        mixed_rows = jnp.einsum(
            f"lhqk,{spec_k}->{spec_q}", attention, value_rows, preferred_element_type=jnp.float32
        )
        mixed_rows = mixed_rows.reshape(mixed_rows.shape[:2] + (width_all,))
        gate_block = lax.dynamic_slice_in_dim(gate_pre, offset, query_rows, 1 - line_dim)
        return (mixed_rows * jax.nn.sigmoid(gate_block)).astype(jnp.bfloat16)

    if blocks == 1:
        return one_block(0)
    outputs = lax.map(one_block, jnp.arange(blocks, dtype=jnp.int32) * query_rows)
    if line_dim == 0:
        outputs = outputs.transpose(1, 0, 2, 3)
    return outputs.reshape(gate_pre.shape[:2] + (width_all,))


def tri_acts(normed, weights, allowed):
    channels = normed.shape[-1]
    projected = jnp.dot(normed.reshape(-1, channels), weights, preferred_element_type=jnp.float32)
    projected = projected.reshape(normed.shape[0], normed.shape[1], 2 * channels)
    return (
        jax.nn.sigmoid(projected[..., channels:]) * projected[..., :channels] * allowed[..., None]
    ).astype(jnp.bfloat16)


def gather_lines(piece):
    device_count = lax.axis_size("row") * lax.axis_size("col")
    sent = jnp.broadcast_to(piece[None], (device_count,) + piece.shape)
    got = lax.all_to_all(sent, ("row", "col"), 0, 0, tiled=True)
    heads, rows_here, length = piece.shape
    return got.transpose(1, 0, 2, 3).reshape(heads, device_count * rows_here, length)


def shards(
    pair_rep,
    tile_mask,
    chain_ids,
    chain_bias,
    row_project,
    row_bias_proj,
    row_output,
    col_project,
    col_bias_proj,
    col_output,
    tri_left,
    tri_right,
    tri_gate,
    tri_output,
):
    n_row = lax.axis_size("row")
    n_col = lax.axis_size("col")
    device_count = n_row * n_col
    rows_here, length, channels = pair_rep.shape
    head_count = row_bias_proj.shape[1]
    head_size = channels // head_count
    row_index = lax.axis_index("row")
    col_index = lax.axis_index("col")
    device_index = row_index * n_col + col_index
    block_rows = length // n_row
    block_cols = length // n_col
    local_lines = device_index * rows_here + jnp.arange(rows_here, dtype=jnp.int32)
    local_cols = col_index * block_cols + row_index * rows_here + jnp.arange(rows_here, dtype=jnp.int32)
    normed = layer_norm(pair_rep).astype(jnp.bfloat16)
    flat_rows = normed.reshape(rows_here * length, channels)
    bias_rows = jnp.dot(flat_rows, row_bias_proj, preferred_element_type=jnp.float32)
    bias_rows = bias_rows.reshape(rows_here, length, head_count).transpose(2, 0, 1)
    bias_all = gather_lines(bias_rows)
    projected = jnp.dot(flat_rows, row_project, preferred_element_type=jnp.float32).reshape(
        rows_here, length, 4 * channels
    )
    qkv_rows = (
        projected[..., : 3 * channels]
        .astype(jnp.bfloat16)
        .reshape(rows_here, length, 3, head_count, head_size)
    )
    key_ok = tile_rows(local_lines, tile_mask, length)
    mixed_rows = attend_lines(
        qkv_rows[:, :, 0],
        qkv_rows[:, :, 1],
        qkv_rows[:, :, 2],
        projected[..., 3 * channels :],
        bias_all,
        key_ok,
        chain_ids,
        chain_bias[0],
        0,
        False,
    )
    update = jnp.dot(
        mixed_rows.reshape(-1, channels), row_output, preferred_element_type=jnp.float32
    ).reshape(rows_here, length, channels)
    first_pair = (pair_rep.astype(jnp.float32) + update).astype(jnp.bfloat16)
    normed_first = layer_norm(first_pair).astype(jnp.bfloat16)
    bias_next = jnp.dot(
        normed_first.reshape(-1, channels), col_bias_proj, preferred_element_type=jnp.float32
    )
    bias_next = bias_next.reshape(rows_here, length, head_count).transpose(2, 0, 1)
    pair_chunks = (
        first_pair.reshape(rows_here, n_col, n_row, rows_here, channels)
        .transpose(2, 1, 0, 3, 4)
        .reshape(device_count, rows_here * rows_here * channels)
        .astype(jnp.float32)
    )
    bias_chunks = jnp.broadcast_to(
        bias_next.reshape(1, -1), (device_count, head_count * rows_here * length)
    )
    merged = lax.all_to_all(
        jnp.concatenate([pair_chunks, bias_chunks], axis=1), ("row", "col"), 0, 0, tiled=True
    )
    pair_size = rows_here * rows_here * channels
    columns = (
        merged[:, :pair_size].astype(jnp.bfloat16).reshape(length, rows_here, channels)
    )
    bias_cols = (
        merged[:, pair_size:]
        .reshape(device_count, head_count, rows_here, length)
        .transpose(1, 0, 2, 3)
        .reshape(head_count, length, length)
    )
    normed_cols = layer_norm(columns).astype(jnp.bfloat16)
    projected_cols = jnp.dot(
        normed_cols.reshape(-1, channels), col_project, preferred_element_type=jnp.float32
    ).reshape(length, rows_here, 4 * channels)
    qkv_cols = (
        projected_cols[..., : 3 * channels]
        .astype(jnp.bfloat16)
        .reshape(length, rows_here, 3, head_count, head_size)
    )
    col_ok = tile_rows(local_cols, tile_mask.T, length)
    mixed_cols = attend_lines(
        qkv_cols[:, :, 0],
        qkv_cols[:, :, 1],
        qkv_cols[:, :, 2],
        projected_cols[..., 3 * channels :],
        bias_cols,
        col_ok,
        chain_ids,
        chain_bias[1],
        1,
        True,
    )
    update_cols = jnp.dot(
        mixed_cols.reshape(-1, channels), col_output, preferred_element_type=jnp.float32
    ).reshape(length, rows_here, channels)
    second_pair = (columns.astype(jnp.float32) + update_cols).astype(jnp.bfloat16)
    normed_second = layer_norm(second_pair).astype(jnp.bfloat16)
    edge_mask = tile_pairs(jnp.arange(length, dtype=jnp.int32), local_cols, tile_mask, length)
    left_all = tri_acts(normed_second, tri_left, edge_mask)
    right_all = tri_acts(normed_second, tri_right, edge_mask)
    raw_got = lax.all_to_all(
        second_pair.reshape(n_row, block_rows, rows_here, channels), "row", 0, 0, tiled=True
    )
    own_pair = raw_got.transpose(1, 0, 2, 3).reshape(block_rows, block_cols, channels)
    channels_here = channels // device_count
    edges = jnp.stack([left_all, right_all], axis=0).transpose(3, 0, 1, 2)
    edges_got = lax.all_to_all(edges, ("row", "col"), 0, 3, tiled=True)
    product_part = jnp.einsum(
        "cik,cjk->cij",
        edges_got[:, 0],
        edges_got[:, 1],
        preferred_element_type=jnp.float32,
    )
    product_sent = (
        product_part.reshape(channels_here, n_row, block_rows, n_col, block_cols)
        .transpose(1, 3, 0, 2, 4)
        .reshape(device_count, channels_here, block_rows, block_cols)
    )
    product_got = lax.all_to_all(product_sent, ("row", "col"), 0, 1, tiled=True)
    product_sum = product_got.reshape(channels, block_rows, block_cols).transpose(1, 2, 0)
    normed_own = layer_norm(own_pair).astype(jnp.bfloat16)
    gate_values = jax.nn.sigmoid(
        jnp.dot(normed_own.reshape(-1, channels), tri_gate, preferred_element_type=jnp.float32)
    ).reshape(block_rows, block_cols, channels)
    centered = layer_norm(product_sum).astype(jnp.bfloat16)
    update_tri = jnp.dot(
        centered.reshape(-1, channels), tri_output, preferred_element_type=jnp.float32
    ).reshape(block_rows, block_cols, channels)
    return (own_pair.astype(jnp.float32) + gate_values * update_tri).astype(jnp.bfloat16)


def solution(mesh):
    return jax.shard_map(
        shards,
        mesh=mesh,
        in_specs=(
            P(("row", "col"), None, None),
            P(),
            P(),
            P(),
            P(),
            P(),
            P(),
            P(),
            P(),
            P(),
            P(),
            P(),
            P(),
            P(),
        ),
        out_specs=P("row", "col", None),
        check_vma=False,
    )
```

```python
import jax
import jax.numpy as jnp
from jax import lax
from jax.sharding import PartitionSpec as P


def layer_norm(values):
    values = values.astype(jnp.float32)
    center = values - jnp.mean(values, axis=-1, keepdims=True)
    spread = jnp.mean(center * center, axis=-1, keepdims=True)
    return center * lax.rsqrt(spread + 1e-05)


def tile_rows(positions, tile_table, length):
    tile_count = tile_table.shape[0]
    tile_width = length // tile_count
    onehot = (positions[:, None] // tile_width == jnp.arange(tile_count)[None, :]).astype(
        jnp.float32
    )
    picked = jnp.dot(onehot, tile_table.astype(jnp.float32))
    spread_out = jnp.broadcast_to(picked[:, :, None], (positions.shape[0], tile_count, tile_width))
    return spread_out.reshape(positions.shape[0], length) > 0.5


def tile_pairs(row_pos, col_pos, tile_table, length):
    tile_count = tile_table.shape[0]
    tile_width = length // tile_count
    row_hot = (row_pos[:, None] // tile_width == jnp.arange(tile_count)[None, :]).astype(
        jnp.float32
    )
    col_hot = (col_pos[:, None] // tile_width == jnp.arange(tile_count)[None, :]).astype(
        jnp.float32
    )
    return jnp.dot(jnp.dot(row_hot, tile_table.astype(jnp.float32)), col_hot.T)


def attend_lines(
    queries,
    key_rows,
    value_rows,
    gate_pre,
    bias_all,
    key_ok,
    chain_ids,
    chain_add,
    line_dim,
    flipped,
):
    length = queries.shape[1 - line_dim]
    head_count = queries.shape[2]
    head_size = queries.shape[3]
    width_all = head_count * head_size
    query_rows = min(128, length)
    blocks = length // query_rows
    scaling = head_size ** (-0.5)
    spec_q = "lqhd" if line_dim == 0 else "qlhd"
    spec_k = "lkhd" if line_dim == 0 else "klhd"
    usable = key_ok[:, None, None, :]

    def one_block(offset):
        query_block = lax.dynamic_slice_in_dim(queries, offset, query_rows, 1 - line_dim)
        scores = (
            jnp.einsum(
                f"{spec_q},{spec_k}->lhqk",
                query_block,
                key_rows,
                preferred_element_type=jnp.float32,
            )
            * scaling
        )
        if flipped:
            bias_block = lax.dynamic_slice_in_dim(bias_all, offset, query_rows, 2).transpose(
                0, 2, 1
            )
        else:
            bias_block = lax.dynamic_slice_in_dim(bias_all, offset, query_rows, 1)
        scores = scores + bias_block[None]
        chain_block = lax.dynamic_slice_in_dim(chain_ids, offset, query_rows, 0)
        same_chain = (chain_block[:, None] == chain_ids[None, :]).astype(jnp.float32)
        scores = scores + (chain_add[:, None, None] * same_chain[None])[None]
        scores = jnp.where(usable, scores, -1000000000.0)
        row_peak = jnp.max(scores, axis=-1, keepdims=True)
        weights = jnp.exp(scores - row_peak)
        attention = (weights / jnp.sum(weights, axis=-1, keepdims=True)).astype(jnp.bfloat16)
        mixed_rows = jnp.einsum(
            f"lhqk,{spec_k}->{spec_q}", attention, value_rows, preferred_element_type=jnp.float32
        )
        mixed_rows = mixed_rows.reshape(mixed_rows.shape[:2] + (width_all,))
        gate_block = lax.dynamic_slice_in_dim(gate_pre, offset, query_rows, 1 - line_dim)
        return (mixed_rows * jax.nn.sigmoid(gate_block)).astype(jnp.bfloat16)

    if blocks == 1:
        return one_block(0)
    outputs = lax.map(one_block, jnp.arange(blocks, dtype=jnp.int32) * query_rows)
    if line_dim == 0:
        outputs = outputs.transpose(1, 0, 2, 3)
    return outputs.reshape(gate_pre.shape[:2] + (width_all,))


def tri_acts(normed, weights, allowed):
    channels = normed.shape[-1]
    projected = jnp.dot(normed.reshape(-1, channels), weights, preferred_element_type=jnp.float32)
    projected = projected.reshape(normed.shape[0], normed.shape[1], 2 * channels)
    return (
        jax.nn.sigmoid(projected[..., channels:]) * projected[..., :channels] * allowed[..., None]
    ).astype(jnp.bfloat16)


def gather_lines(piece):
    device_count = lax.axis_size("row") * lax.axis_size("col")
    sent = jnp.broadcast_to(piece[None], (device_count,) + piece.shape)
    got = lax.all_to_all(sent, ("row", "col"), 0, 0, tiled=True)
    heads, rows_here, length = piece.shape
    return got.transpose(1, 0, 2, 3).reshape(heads, device_count * rows_here, length)


def shards(
    pair_rep,
    tile_mask,
    chain_ids,
    chain_bias,
    row_project,
    row_bias_proj,
    row_output,
    col_project,
    col_bias_proj,
    col_output,
    tri_left,
    tri_right,
    tri_gate,
    tri_output,
):
    n_row = lax.axis_size("row")
    n_col = lax.axis_size("col")
    device_count = n_row * n_col
    rows_here, length, channels = pair_rep.shape
    head_count = row_bias_proj.shape[1]
    head_size = channels // head_count
    row_index = lax.axis_index("row")
    col_index = lax.axis_index("col")
    device_index = row_index * n_col + col_index
    block_rows = length // n_row
    block_cols = length // n_col
    local_lines = device_index * rows_here + jnp.arange(rows_here, dtype=jnp.int32)
    local_cols = col_index * block_cols + row_index * rows_here + jnp.arange(rows_here, dtype=jnp.int32)
    normed = layer_norm(pair_rep).astype(jnp.bfloat16)
    flat_rows = normed.reshape(rows_here * length, channels)
    bias_rows = jnp.dot(flat_rows, row_bias_proj, preferred_element_type=jnp.float32)
    bias_rows = bias_rows.reshape(rows_here, length, head_count).transpose(2, 0, 1)
    bias_all = gather_lines(bias_rows)
    projected = jnp.dot(flat_rows, row_project, preferred_element_type=jnp.float32).reshape(
        rows_here, length, 4 * channels
    )
    qkv_rows = (
        projected[..., : 3 * channels]
        .astype(jnp.bfloat16)
        .reshape(rows_here, length, 3, head_count, head_size)
    )
    key_ok = tile_rows(local_lines, tile_mask, length)
    mixed_rows = attend_lines(
        qkv_rows[:, :, 0],
        qkv_rows[:, :, 1],
        qkv_rows[:, :, 2],
        projected[..., 3 * channels :],
        bias_all,
        key_ok,
        chain_ids,
        chain_bias[0],
        0,
        False,
    )
    update = jnp.dot(
        mixed_rows.reshape(-1, channels), row_output, preferred_element_type=jnp.float32
    ).reshape(rows_here, length, channels)
    first_pair = (pair_rep.astype(jnp.float32) + update).astype(jnp.bfloat16)
    normed_first = layer_norm(first_pair).astype(jnp.bfloat16)
    bias_next = jnp.dot(
        normed_first.reshape(-1, channels), col_bias_proj, preferred_element_type=jnp.float32
    )
    bias_next = bias_next.reshape(rows_here, length, head_count).transpose(2, 0, 1)
    pair_chunks = (
        first_pair.reshape(rows_here, n_col, n_row, rows_here, channels)
        .transpose(2, 1, 0, 3, 4)
        .reshape(device_count, rows_here * rows_here * channels)
        .astype(jnp.float32)
    )
    bias_chunks = jnp.broadcast_to(
        bias_next.reshape(1, -1), (device_count, head_count * rows_here * length)
    )
    merged = lax.all_to_all(
        jnp.concatenate([pair_chunks, bias_chunks], axis=1), ("row", "col"), 0, 0, tiled=True
    )
    pair_size = rows_here * rows_here * channels
    columns = (
        merged[:, :pair_size].astype(jnp.bfloat16).reshape(length, rows_here, channels)
    )
    bias_cols = (
        merged[:, pair_size:]
        .reshape(device_count, head_count, rows_here, length)
        .transpose(1, 0, 2, 3)
        .reshape(head_count, length, length)
    )
    normed_cols = layer_norm(columns).astype(jnp.bfloat16)
    projected_cols = jnp.dot(
        normed_cols.reshape(-1, channels), col_project, preferred_element_type=jnp.float32
    ).reshape(length, rows_here, 4 * channels)
    qkv_cols = (
        projected_cols[..., : 3 * channels]
        .astype(jnp.bfloat16)
        .reshape(length, rows_here, 3, head_count, head_size)
    )
    col_ok = tile_rows(local_cols, tile_mask.T, length)
    mixed_cols = attend_lines(
        qkv_cols[:, :, 0],
        qkv_cols[:, :, 1],
        qkv_cols[:, :, 2],
        projected_cols[..., 3 * channels :],
        bias_cols,
        col_ok,
        chain_ids,
        chain_bias[1],
        1,
        True,
    )
    update_cols = jnp.dot(
        mixed_cols.reshape(-1, channels), col_output, preferred_element_type=jnp.float32
    ).reshape(length, rows_here, channels)
    second_pair = (columns.astype(jnp.float32) + update_cols).astype(jnp.bfloat16)
    normed_second = layer_norm(second_pair).astype(jnp.bfloat16)
    edge_mask = tile_pairs(jnp.arange(length, dtype=jnp.int32), local_cols, tile_mask, length)
    left_all = tri_acts(normed_second, tri_left, edge_mask)
    right_all = tri_acts(normed_second, tri_right, edge_mask)
    raw_chunks = second_pair.reshape(n_row, block_rows, rows_here, channels)
    raw_pieces = [lax.dynamic_index_in_dim(raw_chunks, row_index, 0, keepdims=False)]
    for shift in range(1, n_row):
        piece = lax.dynamic_index_in_dim(raw_chunks, (row_index + shift) % n_row, 0, keepdims=False)
        raw_pieces.append(
            lax.ppermute(piece, "row", perm=[(r, (r + shift) % n_row) for r in range(n_row)])
        )
    sources = (row_index - jnp.arange(n_row, dtype=jnp.int32)) % n_row
    raw_got = jnp.take(jnp.stack(raw_pieces, axis=0), sources, axis=0)
    own_pair = raw_got.transpose(1, 0, 2, 3).reshape(block_rows, block_cols, channels)
    channels_here = channels // device_count
    edges = jnp.stack([left_all, right_all], axis=0).transpose(3, 0, 1, 2)
    edges_got = lax.all_to_all(edges, ("row", "col"), 0, 3, tiled=True)
    product_part = jnp.einsum(
        "cik,cjk->cij",
        edges_got[:, 0],
        edges_got[:, 1],
        preferred_element_type=jnp.float32,
    )
    product_sent = (
        product_part.reshape(channels_here, n_row, block_rows, n_col, block_cols)
        .transpose(1, 3, 0, 2, 4)
        .reshape(device_count, channels_here, block_rows, block_cols)
    )
    product_got = lax.all_to_all(product_sent, ("row", "col"), 0, 1, tiled=True)
    product_sum = product_got.reshape(channels, block_rows, block_cols).transpose(1, 2, 0)
    normed_own = layer_norm(own_pair).astype(jnp.bfloat16)
    gate_values = jax.nn.sigmoid(
        jnp.dot(normed_own.reshape(-1, channels), tri_gate, preferred_element_type=jnp.float32)
    ).reshape(block_rows, block_cols, channels)
    centered = layer_norm(product_sum).astype(jnp.bfloat16)
    update_tri = jnp.dot(
        centered.reshape(-1, channels), tri_output, preferred_element_type=jnp.float32
    ).reshape(block_rows, block_cols, channels)
    return (own_pair.astype(jnp.float32) + gate_values * update_tri).astype(jnp.bfloat16)


def solution(mesh):
    return jax.shard_map(
        shards,
        mesh=mesh,
        in_specs=(
            P(("row", "col"), None, None),
            P(),
            P(),
            P(),
            P(),
            P(),
            P(),
            P(),
            P(),
            P(),
            P(),
            P(),
            P(),
            P(),
        ),
        out_specs=P("row", "col", None),
        check_vma=False,
    )
```

```python
import jax
import jax.numpy as jnp
from jax import lax
from jax.sharding import PartitionSpec as P


def layer_norm(values):
    values = values.astype(jnp.float32)
    center = values - jnp.mean(values, axis=-1, keepdims=True)
    spread = jnp.mean(center * center, axis=-1, keepdims=True)
    return center * lax.rsqrt(spread + 1e-05)


def layer_norm_lead(values):
    values = values.astype(jnp.float32)
    center = values - jnp.mean(values, axis=0, keepdims=True)
    spread = jnp.mean(center * center, axis=0, keepdims=True)
    return center * lax.rsqrt(spread + 1e-05)


def tile_rows(positions, tile_table, length):
    tile_count = tile_table.shape[0]
    tile_width = length // tile_count
    onehot = (positions[:, None] // tile_width == jnp.arange(tile_count)[None, :]).astype(
        jnp.float32
    )
    picked = jnp.dot(onehot, tile_table.astype(jnp.float32))
    spread_out = jnp.broadcast_to(picked[:, :, None], (positions.shape[0], tile_count, tile_width))
    return spread_out.reshape(positions.shape[0], length) > 0.5


def tile_pairs(row_pos, col_pos, tile_table, length):
    tile_count = tile_table.shape[0]
    tile_width = length // tile_count
    row_hot = (row_pos[:, None] // tile_width == jnp.arange(tile_count)[None, :]).astype(
        jnp.float32
    )
    col_hot = (col_pos[:, None] // tile_width == jnp.arange(tile_count)[None, :]).astype(
        jnp.float32
    )
    return jnp.dot(jnp.dot(row_hot, tile_table.astype(jnp.float32)), col_hot.T)


def attend_lines(
    queries,
    key_rows,
    value_rows,
    gate_pre,
    bias_all,
    key_ok,
    chain_ids,
    chain_add,
    line_dim,
    flipped,
):
    length = queries.shape[1 - line_dim]
    head_count = queries.shape[2]
    head_size = queries.shape[3]
    width_all = head_count * head_size
    query_rows = min(128, length)
    blocks = length // query_rows
    scaling = head_size ** (-0.5)
    spec_q = "lqhd" if line_dim == 0 else "qlhd"
    spec_k = "lkhd" if line_dim == 0 else "klhd"
    usable = key_ok[:, None, None, :]

    def one_block(offset):
        query_block = lax.dynamic_slice_in_dim(queries, offset, query_rows, 1 - line_dim)
        scores = (
            jnp.einsum(
                f"{spec_q},{spec_k}->lhqk",
                query_block,
                key_rows,
                preferred_element_type=jnp.float32,
            )
            * scaling
        )
        if flipped:
            bias_block = lax.dynamic_slice_in_dim(bias_all, offset, query_rows, 2).transpose(
                0, 2, 1
            )
        else:
            bias_block = lax.dynamic_slice_in_dim(bias_all, offset, query_rows, 1)
        scores = scores + bias_block[None]
        chain_block = lax.dynamic_slice_in_dim(chain_ids, offset, query_rows, 0)
        same_chain = (chain_block[:, None] == chain_ids[None, :]).astype(jnp.float32)
        scores = scores + (chain_add[:, None, None] * same_chain[None])[None]
        scores = jnp.where(usable, scores, -1000000000.0)
        row_peak = jnp.max(scores, axis=-1, keepdims=True)
        weights = jnp.exp(scores - row_peak)
        attention = (weights / jnp.sum(weights, axis=-1, keepdims=True)).astype(jnp.bfloat16)
        mixed_rows = jnp.einsum(
            f"lhqk,{spec_k}->{spec_q}", attention, value_rows, preferred_element_type=jnp.float32
        )
        mixed_rows = mixed_rows.reshape(mixed_rows.shape[:2] + (width_all,))
        gate_block = lax.dynamic_slice_in_dim(gate_pre, offset, query_rows, 1 - line_dim)
        return (mixed_rows * jax.nn.sigmoid(gate_block)).astype(jnp.bfloat16)

    if blocks == 1:
        return one_block(0)
    outputs = lax.map(one_block, jnp.arange(blocks, dtype=jnp.int32) * query_rows)
    if line_dim == 0:
        outputs = outputs.transpose(1, 0, 2, 3)
    return outputs.reshape(gate_pre.shape[:2] + (width_all,))


def tri_acts(normed, weights, allowed):
    channels = normed.shape[-1]
    projected = jnp.dot(normed.reshape(-1, channels), weights, preferred_element_type=jnp.float32)
    projected = projected.reshape(normed.shape[0], normed.shape[1], 2 * channels)
    return (
        jax.nn.sigmoid(projected[..., channels:]) * projected[..., :channels] * allowed[..., None]
    ).astype(jnp.bfloat16)


def gather_lines(piece):
    device_count = lax.axis_size("row") * lax.axis_size("col")
    sent = jnp.broadcast_to(piece[None], (device_count,) + piece.shape)
    got = lax.all_to_all(sent, ("row", "col"), 0, 0, tiled=True)
    heads, rows_here, length = piece.shape
    return got.transpose(1, 0, 2, 3).reshape(heads, device_count * rows_here, length)


def shards(
    pair_rep,
    tile_mask,
    chain_ids,
    chain_bias,
    row_project,
    row_bias_proj,
    row_output,
    col_project,
    col_bias_proj,
    col_output,
    tri_left,
    tri_right,
    tri_gate,
    tri_output,
):
    n_row = lax.axis_size("row")
    n_col = lax.axis_size("col")
    device_count = n_row * n_col
    rows_here, length, channels = pair_rep.shape
    head_count = row_bias_proj.shape[1]
    head_size = channels // head_count
    row_index = lax.axis_index("row")
    col_index = lax.axis_index("col")
    device_index = row_index * n_col + col_index
    block_rows = length // n_row
    block_cols = length // n_col
    local_lines = device_index * rows_here + jnp.arange(rows_here, dtype=jnp.int32)
    local_cols = col_index * block_cols + row_index * rows_here + jnp.arange(rows_here, dtype=jnp.int32)
    normed = layer_norm(pair_rep).astype(jnp.bfloat16)
    flat_rows = normed.reshape(rows_here * length, channels)
    bias_rows = jnp.dot(flat_rows, row_bias_proj, preferred_element_type=jnp.float32)
    bias_rows = bias_rows.reshape(rows_here, length, head_count).transpose(2, 0, 1)
    bias_all = gather_lines(bias_rows)
    projected = jnp.dot(flat_rows, row_project, preferred_element_type=jnp.float32).reshape(
        rows_here, length, 4 * channels
    )
    qkv_rows = (
        projected[..., : 3 * channels]
        .astype(jnp.bfloat16)
        .reshape(rows_here, length, 3, head_count, head_size)
    )
    key_ok = tile_rows(local_lines, tile_mask, length)
    mixed_rows = attend_lines(
        qkv_rows[:, :, 0],
        qkv_rows[:, :, 1],
        qkv_rows[:, :, 2],
        projected[..., 3 * channels :],
        bias_all,
        key_ok,
        chain_ids,
        chain_bias[0],
        0,
        False,
    )
    update = jnp.dot(
        mixed_rows.reshape(-1, channels), row_output, preferred_element_type=jnp.float32
    ).reshape(rows_here, length, channels)
    first_pair = (pair_rep.astype(jnp.float32) + update).astype(jnp.bfloat16)
    normed_first = layer_norm(first_pair).astype(jnp.bfloat16)
    bias_next = jnp.dot(
        normed_first.reshape(-1, channels), col_bias_proj, preferred_element_type=jnp.float32
    )
    bias_next = bias_next.reshape(rows_here, length, head_count).transpose(2, 0, 1)
    pair_chunks = (
        first_pair.reshape(rows_here, n_col, n_row, rows_here, channels)
        .transpose(2, 1, 0, 3, 4)
        .reshape(device_count, rows_here * rows_here * channels)
        .astype(jnp.float32)
    )
    bias_chunks = jnp.broadcast_to(
        bias_next.reshape(1, -1), (device_count, head_count * rows_here * length)
    )
    merged = lax.all_to_all(
        jnp.concatenate([pair_chunks, bias_chunks], axis=1), ("row", "col"), 0, 0, tiled=True
    )
    pair_size = rows_here * rows_here * channels
    columns = (
        merged[:, :pair_size].astype(jnp.bfloat16).reshape(length, rows_here, channels)
    )
    bias_cols = (
        merged[:, pair_size:]
        .reshape(device_count, head_count, rows_here, length)
        .transpose(1, 0, 2, 3)
        .reshape(head_count, length, length)
    )
    normed_cols = layer_norm(columns).astype(jnp.bfloat16)
    projected_cols = jnp.dot(
        normed_cols.reshape(-1, channels), col_project, preferred_element_type=jnp.float32
    ).reshape(length, rows_here, 4 * channels)
    qkv_cols = (
        projected_cols[..., : 3 * channels]
        .astype(jnp.bfloat16)
        .reshape(length, rows_here, 3, head_count, head_size)
    )
    col_ok = tile_rows(local_cols, tile_mask.T, length)
    mixed_cols = attend_lines(
        qkv_cols[:, :, 0],
        qkv_cols[:, :, 1],
        qkv_cols[:, :, 2],
        projected_cols[..., 3 * channels :],
        bias_cols,
        col_ok,
        chain_ids,
        chain_bias[1],
        1,
        True,
    )
    update_cols = jnp.dot(
        mixed_cols.reshape(-1, channels), col_output, preferred_element_type=jnp.float32
    ).reshape(length, rows_here, channels)
    second_pair = (columns.astype(jnp.float32) + update_cols).astype(jnp.bfloat16)
    normed_second = layer_norm(second_pair).astype(jnp.bfloat16)
    edge_mask = tile_pairs(jnp.arange(length, dtype=jnp.int32), local_cols, tile_mask, length)
    left_all = tri_acts(normed_second, tri_left, edge_mask)
    right_all = tri_acts(normed_second, tri_right, edge_mask)
    channels_here = channels // device_count
    edges = jnp.stack([left_all, right_all, second_pair], axis=0).transpose(3, 0, 1, 2)
    edges_got = lax.all_to_all(edges, ("row", "col"), 0, 3, tiled=True)
    product_part = jnp.einsum(
        "cik,cjk->cij",
        edges_got[:, 0],
        edges_got[:, 1],
        preferred_element_type=jnp.float32,
    )
    raw_part = (
        edges_got[:, 2]
        .reshape(channels_here, length, n_row, n_col, rows_here)
        .transpose(0, 1, 3, 2, 4)
        .reshape(channels_here, length, length)
        .astype(jnp.float32)
    )
    back = jnp.stack([product_part, raw_part], axis=0)
    back_sent = (
        back.reshape(2, channels_here, n_row, block_rows, n_col, block_cols)
        .transpose(2, 4, 0, 1, 3, 5)
        .reshape(device_count, 2 * channels_here, block_rows * block_cols)
    )
    back_got = lax.all_to_all(back_sent, ("row", "col"), 0, 1, tiled=True).reshape(
        device_count, 2, channels_here, block_rows * block_cols
    )
    product_sum = back_got[:, 0].reshape(channels, block_rows * block_cols)
    own_pair = back_got[:, 1].reshape(channels, block_rows * block_cols).astype(jnp.bfloat16)
    normed_own = layer_norm_lead(own_pair).astype(jnp.bfloat16)
    gate_values = jax.nn.sigmoid(
        jnp.einsum("cn,cd->nd", normed_own, tri_gate, preferred_element_type=jnp.float32)
    )
    centered = layer_norm_lead(product_sum).astype(jnp.bfloat16)
    update_tri = jnp.einsum("cn,cd->nd", centered, tri_output, preferred_element_type=jnp.float32)
    result = own_pair.T.astype(jnp.float32) + gate_values * update_tri
    return result.astype(jnp.bfloat16).reshape(block_rows, block_cols, channels)


def solution(mesh):
    return jax.shard_map(
        shards,
        mesh=mesh,
        in_specs=(
            P(("row", "col"), None, None),
            P(),
            P(),
            P(),
            P(),
            P(),
            P(),
            P(),
            P(),
            P(),
            P(),
            P(),
            P(),
            P(),
        ),
        out_specs=P("row", "col", None),
        check_vma=False,
    )
```

```python
import jax
import jax.numpy as jnp
from jax import lax
from jax.sharding import PartitionSpec as P


def layer_norm(values):
    values = values.astype(jnp.float32)
    center = values - jnp.mean(values, axis=-1, keepdims=True)
    spread = jnp.mean(center * center, axis=-1, keepdims=True)
    return center * lax.rsqrt(spread + 1e-05)


def layer_norm_lead(values):
    values = values.astype(jnp.float32)
    center = values - jnp.mean(values, axis=0, keepdims=True)
    spread = jnp.mean(center * center, axis=0, keepdims=True)
    return center * lax.rsqrt(spread + 1e-05)


def tile_rows(positions, tile_table, length):
    tile_count = tile_table.shape[0]
    tile_width = length // tile_count
    onehot = (positions[:, None] // tile_width == jnp.arange(tile_count)[None, :]).astype(
        jnp.float32
    )
    picked = jnp.dot(onehot, tile_table.astype(jnp.float32))
    spread_out = jnp.broadcast_to(picked[:, :, None], (positions.shape[0], tile_count, tile_width))
    return spread_out.reshape(positions.shape[0], length) > 0.5


def tile_pairs(row_pos, col_pos, tile_table, length):
    tile_count = tile_table.shape[0]
    tile_width = length // tile_count
    row_hot = (row_pos[:, None] // tile_width == jnp.arange(tile_count)[None, :]).astype(
        jnp.float32
    )
    col_hot = (col_pos[:, None] // tile_width == jnp.arange(tile_count)[None, :]).astype(
        jnp.float32
    )
    return jnp.dot(jnp.dot(row_hot, tile_table.astype(jnp.float32)), col_hot.T)


def attend_lines(
    queries,
    key_rows,
    value_rows,
    gate_pre,
    bias_all,
    key_ok,
    chain_ids,
    chain_add,
    line_dim,
    flipped,
):
    length = queries.shape[1 - line_dim]
    head_count = queries.shape[2]
    head_size = queries.shape[3]
    width_all = head_count * head_size
    query_rows = min(128, length)
    blocks = length // query_rows
    scaling = head_size ** (-0.5)
    spec_q = "lqhd" if line_dim == 0 else "qlhd"
    spec_k = "lkhd" if line_dim == 0 else "klhd"
    usable = key_ok[:, None, None, :]

    def one_block(offset):
        query_block = lax.dynamic_slice_in_dim(queries, offset, query_rows, 1 - line_dim)
        scores = (
            jnp.einsum(
                f"{spec_q},{spec_k}->lhqk",
                query_block,
                key_rows,
                preferred_element_type=jnp.float32,
            )
            * scaling
        )
        if flipped:
            bias_block = lax.dynamic_slice_in_dim(bias_all, offset, query_rows, 2).transpose(
                0, 2, 1
            )
        else:
            bias_block = lax.dynamic_slice_in_dim(bias_all, offset, query_rows, 1)
        scores = scores + bias_block[None]
        chain_block = lax.dynamic_slice_in_dim(chain_ids, offset, query_rows, 0)
        same_chain = (chain_block[:, None] == chain_ids[None, :]).astype(jnp.float32)
        scores = scores + (chain_add[:, None, None] * same_chain[None])[None]
        scores = jnp.where(usable, scores, -1000000000.0)
        row_peak = jnp.max(scores, axis=-1, keepdims=True)
        weights = jnp.exp(scores - row_peak)
        attention = (weights / jnp.sum(weights, axis=-1, keepdims=True)).astype(jnp.bfloat16)
        mixed_rows = jnp.einsum(
            f"lhqk,{spec_k}->{spec_q}", attention, value_rows, preferred_element_type=jnp.float32
        )
        mixed_rows = mixed_rows.reshape(mixed_rows.shape[:2] + (width_all,))
        gate_block = lax.dynamic_slice_in_dim(gate_pre, offset, query_rows, 1 - line_dim)
        return (mixed_rows * jax.nn.sigmoid(gate_block)).astype(jnp.bfloat16)

    if blocks == 1:
        return one_block(0)
    outputs = lax.map(one_block, jnp.arange(blocks, dtype=jnp.int32) * query_rows)
    if line_dim == 0:
        outputs = outputs.transpose(1, 0, 2, 3)
    return outputs.reshape(gate_pre.shape[:2] + (width_all,))


def tri_acts(normed, weights, allowed):
    channels = normed.shape[-1]
    projected = jnp.dot(normed.reshape(-1, channels), weights, preferred_element_type=jnp.float32)
    projected = projected.reshape(normed.shape[0], normed.shape[1], 2 * channels)
    return (
        jax.nn.sigmoid(projected[..., channels:]) * projected[..., :channels] * allowed[..., None]
    ).astype(jnp.bfloat16)


def gather_lines(piece):
    device_count = lax.axis_size("row") * lax.axis_size("col")
    heads, rows_here, length = piece.shape
    sent = jnp.broadcast_to(piece.reshape(1, 1, -1), (device_count, 1, piece.size))
    got = lax.all_to_all(sent, ("row", "col"), 0, 0, tiled=True)
    got = got.reshape(device_count, heads, rows_here, length)
    return got.transpose(1, 0, 2, 3).reshape(heads, device_count * rows_here, length)


def shards(
    pair_rep,
    tile_mask,
    chain_ids,
    chain_bias,
    row_project,
    row_bias_proj,
    row_output,
    col_project,
    col_bias_proj,
    col_output,
    tri_left,
    tri_right,
    tri_gate,
    tri_output,
):
    n_row = lax.axis_size("row")
    n_col = lax.axis_size("col")
    device_count = n_row * n_col
    rows_here, length, channels = pair_rep.shape
    head_count = row_bias_proj.shape[1]
    head_size = channels // head_count
    row_index = lax.axis_index("row")
    col_index = lax.axis_index("col")
    device_index = row_index * n_col + col_index
    block_rows = length // n_row
    block_cols = length // n_col
    local_lines = device_index * rows_here + jnp.arange(rows_here, dtype=jnp.int32)
    local_cols = col_index * block_cols + row_index * rows_here + jnp.arange(rows_here, dtype=jnp.int32)
    normed = layer_norm(pair_rep).astype(jnp.bfloat16)
    flat_rows = normed.reshape(rows_here * length, channels)
    bias_rows = jnp.dot(flat_rows, row_bias_proj, preferred_element_type=jnp.float32)
    bias_rows = bias_rows.reshape(rows_here, length, head_count).transpose(2, 0, 1)
    bias_all = gather_lines(bias_rows)
    projected = jnp.dot(flat_rows, row_project, preferred_element_type=jnp.float32).reshape(
        rows_here, length, 4 * channels
    )
    qkv_rows = (
        projected[..., : 3 * channels]
        .astype(jnp.bfloat16)
        .reshape(rows_here, length, 3, head_count, head_size)
    )
    key_ok = tile_rows(local_lines, tile_mask, length)
    mixed_rows = attend_lines(
        qkv_rows[:, :, 0],
        qkv_rows[:, :, 1],
        qkv_rows[:, :, 2],
        projected[..., 3 * channels :],
        bias_all,
        key_ok,
        chain_ids,
        chain_bias[0],
        0,
        False,
    )
    update = jnp.dot(
        mixed_rows.reshape(-1, channels), row_output, preferred_element_type=jnp.float32
    ).reshape(rows_here, length, channels)
    first_pair = (pair_rep.astype(jnp.float32) + update).astype(jnp.bfloat16)
    normed_first = layer_norm(first_pair).astype(jnp.bfloat16)
    bias_next = jnp.dot(
        normed_first.reshape(-1, channels), col_bias_proj, preferred_element_type=jnp.float32
    )
    bias_next = bias_next.reshape(rows_here, length, head_count).transpose(2, 0, 1)
    pair_chunks = (
        first_pair.reshape(rows_here, n_col, n_row, rows_here, channels)
        .transpose(2, 1, 0, 3, 4)
        .reshape(device_count, rows_here * rows_here * channels)
        .astype(jnp.float32)
    )
    bias_chunks = jnp.broadcast_to(
        bias_next.reshape(1, -1), (device_count, head_count * rows_here * length)
    )
    merged = lax.all_to_all(
        jnp.concatenate([pair_chunks, bias_chunks], axis=1), ("row", "col"), 0, 0, tiled=True
    )
    pair_size = rows_here * rows_here * channels
    columns = (
        merged[:, :pair_size].astype(jnp.bfloat16).reshape(length, rows_here, channels)
    )
    bias_cols = (
        merged[:, pair_size:]
        .reshape(device_count, head_count, rows_here, length)
        .transpose(1, 0, 2, 3)
        .reshape(head_count, length, length)
    )
    normed_cols = layer_norm(columns).astype(jnp.bfloat16)
    projected_cols = jnp.dot(
        normed_cols.reshape(-1, channels), col_project, preferred_element_type=jnp.float32
    ).reshape(length, rows_here, 4 * channels)
    qkv_cols = (
        projected_cols[..., : 3 * channels]
        .astype(jnp.bfloat16)
        .reshape(length, rows_here, 3, head_count, head_size)
    )
    col_ok = tile_rows(local_cols, tile_mask.T, length)
    mixed_cols = attend_lines(
        qkv_cols[:, :, 0],
        qkv_cols[:, :, 1],
        qkv_cols[:, :, 2],
        projected_cols[..., 3 * channels :],
        bias_cols,
        col_ok,
        chain_ids,
        chain_bias[1],
        1,
        True,
    )
    update_cols = jnp.dot(
        mixed_cols.reshape(-1, channels), col_output, preferred_element_type=jnp.float32
    ).reshape(length, rows_here, channels)
    second_pair = (columns.astype(jnp.float32) + update_cols).astype(jnp.bfloat16)
    normed_second = layer_norm(second_pair).astype(jnp.bfloat16)
    edge_mask = tile_pairs(jnp.arange(length, dtype=jnp.int32), local_cols, tile_mask, length)
    left_all = tri_acts(normed_second, tri_left, edge_mask)
    right_all = tri_acts(normed_second, tri_right, edge_mask)
    raw_chunks = second_pair.reshape(n_row, block_rows, rows_here, channels)
    raw_pieces = [lax.dynamic_index_in_dim(raw_chunks, row_index, 0, keepdims=False)]
    for shift in range(1, n_row):
        piece = lax.dynamic_index_in_dim(raw_chunks, (row_index + shift) % n_row, 0, keepdims=False)
        raw_pieces.append(
            lax.ppermute(piece, "row", perm=[(r, (r + shift) % n_row) for r in range(n_row)])
        )
    sources = (row_index - jnp.arange(n_row, dtype=jnp.int32)) % n_row
    raw_got = jnp.take(jnp.stack(raw_pieces, axis=0), sources, axis=0)
    own_pair = raw_got.transpose(1, 0, 2, 3).reshape(block_rows, block_cols, channels)
    channels_here = channels // device_count
    edges = jnp.stack([left_all, right_all], axis=0).transpose(3, 0, 1, 2)
    edges_got = lax.all_to_all(edges, ("row", "col"), 0, 3, tiled=True)
    product_part = jnp.einsum(
        "cik,cjk->cij",
        edges_got[:, 0],
        edges_got[:, 1],
        preferred_element_type=jnp.float32,
    )
    product_sent = (
        product_part.reshape(channels_here, n_row, block_rows, n_col, block_cols)
        .transpose(1, 3, 0, 2, 4)
        .reshape(device_count, channels_here, block_rows, block_cols)
    )
    product_got = lax.all_to_all(product_sent, ("row", "col"), 0, 1, tiled=True)
    product_sum = product_got.reshape(channels, block_rows * block_cols)
    normed_own = layer_norm(own_pair).astype(jnp.bfloat16)
    gate_values = jax.nn.sigmoid(
        jnp.dot(normed_own.reshape(-1, channels), tri_gate, preferred_element_type=jnp.float32)
    )
    centered = layer_norm_lead(product_sum).astype(jnp.bfloat16)
    update_tri = jnp.einsum("cn,cd->nd", centered, tri_output, preferred_element_type=jnp.float32)
    result = own_pair.reshape(-1, channels).astype(jnp.float32) + gate_values * update_tri
    return result.astype(jnp.bfloat16).reshape(block_rows, block_cols, channels)


def solution(mesh):
    return jax.shard_map(
        shards,
        mesh=mesh,
        in_specs=(
            P(("row", "col"), None, None),
            P(),
            P(),
            P(),
            P(),
            P(),
            P(),
            P(),
            P(),
            P(),
            P(),
            P(),
            P(),
            P(),
        ),
        out_specs=P("row", "col", None),
        check_vma=False,
    )
```

```python
import jax
import jax.numpy as jnp
from jax import lax
from jax.sharding import PartitionSpec as P


def layer_norm(values):
    values = values.astype(jnp.float32)
    center = values - jnp.mean(values, axis=-1, keepdims=True)
    spread = jnp.mean(center * center, axis=-1, keepdims=True)
    return center * lax.rsqrt(spread + 1e-05)


def layer_norm_lead(values):
    values = values.astype(jnp.float32)
    center = values - jnp.mean(values, axis=0, keepdims=True)
    spread = jnp.mean(center * center, axis=0, keepdims=True)
    return center * lax.rsqrt(spread + 1e-05)


def tile_rows(positions, tile_table, length):
    tile_count = tile_table.shape[0]
    tile_width = length // tile_count
    onehot = (positions[:, None] // tile_width == jnp.arange(tile_count)[None, :]).astype(
        jnp.float32
    )
    picked = jnp.dot(onehot, tile_table.astype(jnp.float32))
    spread_out = jnp.broadcast_to(picked[:, :, None], (positions.shape[0], tile_count, tile_width))
    return spread_out.reshape(positions.shape[0], length) > 0.5


def tile_pairs(row_pos, col_pos, tile_table, length):
    tile_count = tile_table.shape[0]
    tile_width = length // tile_count
    row_hot = (row_pos[:, None] // tile_width == jnp.arange(tile_count)[None, :]).astype(
        jnp.float32
    )
    col_hot = (col_pos[:, None] // tile_width == jnp.arange(tile_count)[None, :]).astype(
        jnp.float32
    )
    return jnp.dot(jnp.dot(row_hot, tile_table.astype(jnp.float32)), col_hot.T)


def attend_lines(
    queries,
    key_rows,
    value_rows,
    gate_pre,
    bias_all,
    key_ok,
    chain_ids,
    chain_add,
    line_dim,
    flipped,
):
    length = queries.shape[1 - line_dim]
    head_count = queries.shape[2]
    head_size = queries.shape[3]
    width_all = head_count * head_size
    query_rows = min(128, length)
    blocks = length // query_rows
    scaling = head_size ** (-0.5)
    spec_q = "lqhd" if line_dim == 0 else "qlhd"
    spec_k = "lkhd" if line_dim == 0 else "klhd"
    usable = key_ok[:, None, None, :]

    def one_block(offset):
        query_block = lax.dynamic_slice_in_dim(queries, offset, query_rows, 1 - line_dim)
        scores = (
            jnp.einsum(
                f"{spec_q},{spec_k}->lhqk",
                query_block,
                key_rows,
                preferred_element_type=jnp.float32,
            )
            * scaling
        )
        if flipped:
            bias_block = lax.dynamic_slice_in_dim(bias_all, offset, query_rows, 2).transpose(
                0, 2, 1
            )
        else:
            bias_block = lax.dynamic_slice_in_dim(bias_all, offset, query_rows, 1)
        scores = scores + bias_block[None]
        chain_block = lax.dynamic_slice_in_dim(chain_ids, offset, query_rows, 0)
        same_chain = (chain_block[:, None] == chain_ids[None, :]).astype(jnp.float32)
        scores = scores + (chain_add[:, None, None] * same_chain[None])[None]
        scores = jnp.where(usable, scores, -1000000000.0)
        row_peak = jnp.max(scores, axis=-1, keepdims=True)
        weights = jnp.exp(scores - row_peak)
        attention = (weights / jnp.sum(weights, axis=-1, keepdims=True)).astype(jnp.bfloat16)
        mixed_rows = jnp.einsum(
            f"lhqk,{spec_k}->{spec_q}", attention, value_rows, preferred_element_type=jnp.float32
        )
        mixed_rows = mixed_rows.reshape(mixed_rows.shape[:2] + (width_all,))
        gate_block = lax.dynamic_slice_in_dim(gate_pre, offset, query_rows, 1 - line_dim)
        return (mixed_rows * jax.nn.sigmoid(gate_block)).astype(jnp.bfloat16)

    if blocks == 1:
        return one_block(0)
    outputs = lax.map(one_block, jnp.arange(blocks, dtype=jnp.int32) * query_rows)
    if line_dim == 0:
        outputs = outputs.transpose(1, 0, 2, 3)
    return outputs.reshape(gate_pre.shape[:2] + (width_all,))


def tri_acts(normed, weights, allowed):
    channels = normed.shape[-1]
    projected = jnp.dot(normed.reshape(-1, channels), weights, preferred_element_type=jnp.float32)
    projected = projected.reshape(normed.shape[0], normed.shape[1], 2 * channels)
    return (
        jax.nn.sigmoid(projected[..., channels:]) * projected[..., :channels] * allowed[..., None]
    ).astype(jnp.bfloat16)


def gather_lines(piece):
    device_count = lax.axis_size("row") * lax.axis_size("col")
    heads, rows_here, length = piece.shape
    sent = jnp.broadcast_to(piece.reshape(1, 1, -1), (device_count, 1, piece.size))
    got = lax.all_to_all(sent, ("row", "col"), 0, 0, tiled=True)
    got = got.reshape(device_count, heads, rows_here, length)
    return got.transpose(1, 0, 2, 3).reshape(heads, device_count * rows_here, length)


def shards(
    pair_rep,
    tile_mask,
    chain_ids,
    chain_bias,
    row_project,
    row_bias_proj,
    row_output,
    col_project,
    col_bias_proj,
    col_output,
    tri_left,
    tri_right,
    tri_gate,
    tri_output,
):
    slab_parts = [row_project, col_project, tri_left, tri_right, tri_gate, row_output, col_output, tri_output]
    slab = lax.optimization_barrier(jnp.concatenate(slab_parts, axis=1))
    cuts = [0]
    for part in slab_parts:
        cuts.append(cuts[-1] + part.shape[1])
    (row_project, col_project, tri_left, tri_right, tri_gate, row_output, col_output, tri_output) = [
        slab[:, cuts[n] : cuts[n + 1]] for n in range(len(slab_parts))
    ]
    n_row = lax.axis_size("row")
    n_col = lax.axis_size("col")
    device_count = n_row * n_col
    rows_here, length, channels = pair_rep.shape
    head_count = row_bias_proj.shape[1]
    head_size = channels // head_count
    row_index = lax.axis_index("row")
    col_index = lax.axis_index("col")
    device_index = row_index * n_col + col_index
    block_rows = length // n_row
    block_cols = length // n_col
    local_lines = device_index * rows_here + jnp.arange(rows_here, dtype=jnp.int32)
    local_cols = col_index * block_cols + row_index * rows_here + jnp.arange(rows_here, dtype=jnp.int32)
    normed = layer_norm(pair_rep).astype(jnp.bfloat16)
    flat_rows = normed.reshape(rows_here * length, channels)
    bias_rows = jnp.dot(flat_rows, row_bias_proj, preferred_element_type=jnp.float32)
    bias_rows = bias_rows.reshape(rows_here, length, head_count).transpose(2, 0, 1)
    bias_all = gather_lines(bias_rows)
    projected = jnp.dot(flat_rows, row_project, preferred_element_type=jnp.float32).reshape(
        rows_here, length, 4 * channels
    )
    qkv_rows = (
        projected[..., : 3 * channels]
        .astype(jnp.bfloat16)
        .reshape(rows_here, length, 3, head_count, head_size)
    )
    key_ok = tile_rows(local_lines, tile_mask, length)
    mixed_rows = attend_lines(
        qkv_rows[:, :, 0],
        qkv_rows[:, :, 1],
        qkv_rows[:, :, 2],
        projected[..., 3 * channels :],
        bias_all,
        key_ok,
        chain_ids,
        chain_bias[0],
        0,
        False,
    )
    update = jnp.dot(
        mixed_rows.reshape(-1, channels), row_output, preferred_element_type=jnp.float32
    ).reshape(rows_here, length, channels)
    first_pair = (pair_rep.astype(jnp.float32) + update).astype(jnp.bfloat16)
    normed_first = layer_norm(first_pair).astype(jnp.bfloat16)
    bias_next = jnp.dot(
        normed_first.reshape(-1, channels), col_bias_proj, preferred_element_type=jnp.float32
    )
    bias_next = bias_next.reshape(rows_here, length, head_count).transpose(2, 0, 1)
    pair_chunks = (
        first_pair.reshape(rows_here, n_col, n_row, rows_here, channels)
        .transpose(2, 1, 0, 3, 4)
        .reshape(device_count, rows_here * rows_here * channels)
        .astype(jnp.float32)
    )
    bias_chunks = jnp.broadcast_to(
        bias_next.reshape(1, -1), (device_count, head_count * rows_here * length)
    )
    merged = lax.all_to_all(
        jnp.concatenate([pair_chunks, bias_chunks], axis=1), ("row", "col"), 0, 0, tiled=True
    )
    pair_size = rows_here * rows_here * channels
    columns = (
        merged[:, :pair_size].astype(jnp.bfloat16).reshape(length, rows_here, channels)
    )
    bias_cols = (
        merged[:, pair_size:]
        .reshape(device_count, head_count, rows_here, length)
        .transpose(1, 0, 2, 3)
        .reshape(head_count, length, length)
    )
    normed_cols = layer_norm(columns).astype(jnp.bfloat16)
    projected_cols = jnp.dot(
        normed_cols.reshape(-1, channels), col_project, preferred_element_type=jnp.float32
    ).reshape(length, rows_here, 4 * channels)
    qkv_cols = (
        projected_cols[..., : 3 * channels]
        .astype(jnp.bfloat16)
        .reshape(length, rows_here, 3, head_count, head_size)
    )
    col_ok = tile_rows(local_cols, tile_mask.T, length)
    mixed_cols = attend_lines(
        qkv_cols[:, :, 0],
        qkv_cols[:, :, 1],
        qkv_cols[:, :, 2],
        projected_cols[..., 3 * channels :],
        bias_cols,
        col_ok,
        chain_ids,
        chain_bias[1],
        1,
        True,
    )
    update_cols = jnp.dot(
        mixed_cols.reshape(-1, channels), col_output, preferred_element_type=jnp.float32
    ).reshape(length, rows_here, channels)
    second_pair = (columns.astype(jnp.float32) + update_cols).astype(jnp.bfloat16)
    normed_second = layer_norm(second_pair).astype(jnp.bfloat16)
    edge_mask = tile_pairs(jnp.arange(length, dtype=jnp.int32), local_cols, tile_mask, length)
    left_all = tri_acts(normed_second, tri_left, edge_mask)
    right_all = tri_acts(normed_second, tri_right, edge_mask)
    raw_chunks = second_pair.reshape(n_row, block_rows, rows_here, channels)
    raw_pieces = [lax.dynamic_index_in_dim(raw_chunks, row_index, 0, keepdims=False)]
    for shift in range(1, n_row):
        piece = lax.dynamic_index_in_dim(raw_chunks, (row_index + shift) % n_row, 0, keepdims=False)
        raw_pieces.append(
            lax.ppermute(piece, "row", perm=[(r, (r + shift) % n_row) for r in range(n_row)])
        )
    sources = (row_index - jnp.arange(n_row, dtype=jnp.int32)) % n_row
    raw_got = jnp.take(jnp.stack(raw_pieces, axis=0), sources, axis=0)
    own_pair = raw_got.transpose(1, 0, 2, 3).reshape(block_rows, block_cols, channels)
    channels_here = channels // device_count
    edges = jnp.stack([left_all, right_all], axis=0).transpose(3, 0, 1, 2)
    edges_got = lax.all_to_all(edges, ("row", "col"), 0, 3, tiled=True)
    product_part = jnp.einsum(
        "cik,cjk->cij",
        edges_got[:, 0],
        edges_got[:, 1],
        preferred_element_type=jnp.float32,
    )
    product_sent = (
        product_part.reshape(channels_here, n_row, block_rows, n_col, block_cols)
        .transpose(1, 3, 0, 2, 4)
        .reshape(device_count, channels_here, block_rows, block_cols)
    )
    product_got = lax.all_to_all(product_sent, ("row", "col"), 0, 1, tiled=True)
    product_sum = product_got.reshape(channels, block_rows * block_cols)
    normed_own = layer_norm(own_pair).astype(jnp.bfloat16)
    gate_values = jax.nn.sigmoid(
        jnp.dot(normed_own.reshape(-1, channels), tri_gate, preferred_element_type=jnp.float32)
    )
    centered = layer_norm_lead(product_sum).astype(jnp.bfloat16)
    update_tri = jnp.einsum("cn,cd->nd", centered, tri_output, preferred_element_type=jnp.float32)
    result = own_pair.reshape(-1, channels).astype(jnp.float32) + gate_values * update_tri
    return result.astype(jnp.bfloat16).reshape(block_rows, block_cols, channels)


def solution(mesh):
    return jax.shard_map(
        shards,
        mesh=mesh,
        in_specs=(
            P(("row", "col"), None, None),
            P(),
            P(),
            P(),
            P(),
            P(),
            P(),
            P(),
            P(),
            P(),
            P(),
            P(),
            P(),
            P(),
        ),
        out_specs=P("row", "col", None),
        check_vma=False,
    )
```

```python
import jax
import jax.numpy as jnp
from jax import lax
from jax.sharding import PartitionSpec as P


def layer_norm(values):
    values = values.astype(jnp.float32)
    center = values - jnp.mean(values, axis=-1, keepdims=True)
    spread = jnp.mean(center * center, axis=-1, keepdims=True)
    return center * lax.rsqrt(spread + 1e-05)


def tile_rows(positions, tile_table, length):
    tile_count = tile_table.shape[0]
    tile_width = length // tile_count
    onehot = (positions[:, None] // tile_width == jnp.arange(tile_count)[None, :]).astype(
        jnp.float32
    )
    picked = jnp.dot(onehot, tile_table.astype(jnp.float32))
    spread_out = jnp.broadcast_to(picked[:, :, None], (positions.shape[0], tile_count, tile_width))
    return spread_out.reshape(positions.shape[0], length) > 0.5


def tile_pairs(row_pos, col_pos, tile_table, length):
    tile_count = tile_table.shape[0]
    tile_width = length // tile_count
    row_hot = (row_pos[:, None] // tile_width == jnp.arange(tile_count)[None, :]).astype(
        jnp.float32
    )
    col_hot = (col_pos[:, None] // tile_width == jnp.arange(tile_count)[None, :]).astype(
        jnp.float32
    )
    return jnp.dot(jnp.dot(row_hot, tile_table.astype(jnp.float32)), col_hot.T)


def attend_lines(
    queries,
    key_rows,
    value_rows,
    gate_pre,
    bias_all,
    key_ok,
    chain_ids,
    chain_add,
    line_dim,
    flipped,
):
    length = queries.shape[1 - line_dim]
    head_count = queries.shape[2]
    head_size = queries.shape[3]
    width_all = head_count * head_size
    query_rows = min(128, length)
    blocks = length // query_rows
    scaling = head_size ** (-0.5)
    spec_q = "lqhd" if line_dim == 0 else "qlhd"
    spec_k = "lkhd" if line_dim == 0 else "klhd"
    usable = key_ok[:, None, None, :]

    def one_block(offset):
        query_block = lax.dynamic_slice_in_dim(queries, offset, query_rows, 1 - line_dim)
        scores = (
            jnp.einsum(
                f"{spec_q},{spec_k}->lhqk",
                query_block,
                key_rows,
                preferred_element_type=jnp.float32,
            )
            * scaling
        )
        if flipped:
            bias_block = lax.dynamic_slice_in_dim(bias_all, offset, query_rows, 2).transpose(
                0, 2, 1
            )
        else:
            bias_block = lax.dynamic_slice_in_dim(bias_all, offset, query_rows, 1)
        scores = scores + bias_block[None]
        chain_block = lax.dynamic_slice_in_dim(chain_ids, offset, query_rows, 0)
        same_chain = (chain_block[:, None] == chain_ids[None, :]).astype(jnp.float32)
        scores = scores + (chain_add[:, None, None] * same_chain[None])[None]
        scores = jnp.where(usable, scores, -1000000000.0)
        row_peak = jnp.max(scores, axis=-1, keepdims=True)
        weights = jnp.exp(scores - row_peak)
        attention = (weights / jnp.sum(weights, axis=-1, keepdims=True)).astype(jnp.bfloat16)
        mixed_rows = jnp.einsum(
            f"lhqk,{spec_k}->{spec_q}", attention, value_rows, preferred_element_type=jnp.float32
        )
        mixed_rows = mixed_rows.reshape(mixed_rows.shape[:2] + (width_all,))
        gate_block = lax.dynamic_slice_in_dim(gate_pre, offset, query_rows, 1 - line_dim)
        return (mixed_rows * jax.nn.sigmoid(gate_block)).astype(jnp.bfloat16)

    if blocks == 1:
        return one_block(0)
    outputs = lax.map(one_block, jnp.arange(blocks, dtype=jnp.int32) * query_rows)
    if line_dim == 0:
        outputs = outputs.transpose(1, 0, 2, 3)
    return outputs.reshape(gate_pre.shape[:2] + (width_all,))


def tri_acts(normed, weights, allowed):
    channels = normed.shape[-1]
    projected = jnp.dot(normed.reshape(-1, channels), weights, preferred_element_type=jnp.float32)
    projected = projected.reshape(normed.shape[0], normed.shape[1], 2 * channels)
    return (
        jax.nn.sigmoid(projected[..., channels:]) * projected[..., :channels] * allowed[..., None]
    ).astype(jnp.bfloat16)


def gather_lines(piece):
    device_count = lax.axis_size("row") * lax.axis_size("col")
    sent = jnp.broadcast_to(piece[None], (device_count,) + piece.shape)
    got = lax.all_to_all(sent, ("row", "col"), 0, 0, tiled=True)
    heads, rows_here, length = piece.shape
    return got.transpose(1, 0, 2, 3).reshape(heads, device_count * rows_here, length)


def shards(
    pair_rep,
    tile_mask,
    chain_ids,
    chain_bias,
    row_project,
    row_bias_proj,
    row_output,
    col_project,
    col_bias_proj,
    col_output,
    tri_left,
    tri_right,
    tri_gate,
    tri_output,
):
    n_row = lax.axis_size("row")
    n_col = lax.axis_size("col")
    device_count = n_row * n_col
    rows_here, length, channels = pair_rep.shape
    head_count = row_bias_proj.shape[1]
    head_size = channels // head_count
    row_index = lax.axis_index("row")
    col_index = lax.axis_index("col")
    device_index = row_index * n_col + col_index
    block_rows = length // n_row
    block_cols = length // n_col
    local_lines = device_index * rows_here + jnp.arange(rows_here, dtype=jnp.int32)
    local_cols = col_index * block_cols + row_index * rows_here + jnp.arange(rows_here, dtype=jnp.int32)
    normed = layer_norm(pair_rep).astype(jnp.bfloat16)
    flat_rows = normed.reshape(rows_here * length, channels)
    bias_rows = jnp.dot(flat_rows, row_bias_proj, preferred_element_type=jnp.float32)
    bias_rows = bias_rows.reshape(rows_here, length, head_count).transpose(2, 0, 1)
    bias_all = gather_lines(bias_rows)
    projected = jnp.dot(flat_rows, row_project, preferred_element_type=jnp.float32).reshape(
        rows_here, length, 4 * channels
    )
    qkv_rows = (
        projected[..., : 3 * channels]
        .astype(jnp.bfloat16)
        .reshape(rows_here, length, 3, head_count, head_size)
    )
    key_ok = tile_rows(local_lines, tile_mask, length)
    mixed_rows = attend_lines(
        qkv_rows[:, :, 0],
        qkv_rows[:, :, 1],
        qkv_rows[:, :, 2],
        projected[..., 3 * channels :],
        bias_all,
        key_ok,
        chain_ids,
        chain_bias[0],
        0,
        False,
    )
    update = jnp.dot(
        mixed_rows.reshape(-1, channels), row_output, preferred_element_type=jnp.float32
    ).reshape(rows_here, length, channels)
    first_pair = (pair_rep.astype(jnp.float32) + update).astype(jnp.bfloat16)
    normed_first = layer_norm(first_pair).astype(jnp.bfloat16)
    bias_next = jnp.dot(
        normed_first.reshape(-1, channels), col_bias_proj, preferred_element_type=jnp.float32
    )
    bias_next = bias_next.reshape(rows_here, length, head_count).transpose(2, 0, 1)
    pair_chunks = (
        first_pair.reshape(rows_here, n_col, n_row, rows_here, channels)
        .transpose(2, 1, 0, 3, 4)
        .reshape(device_count, rows_here * rows_here * channels)
    )
    bias_high = bias_next.astype(jnp.bfloat16)
    bias_low = (bias_next - bias_high.astype(jnp.float32)).astype(jnp.bfloat16)
    bias_words = jnp.stack([bias_high, bias_low], axis=0).reshape(1, -1)
    bias_chunks = jnp.broadcast_to(bias_words, (device_count, bias_words.shape[1]))
    merged = lax.all_to_all(
        jnp.concatenate([pair_chunks, bias_chunks], axis=1), ("row", "col"), 0, 0, tiled=True
    )
    pair_size = rows_here * rows_here * channels
    columns = merged[:, :pair_size].reshape(length, rows_here, channels)
    bias_got = (
        merged[:, pair_size:]
        .reshape(device_count, 2, head_count, rows_here, length)
        .astype(jnp.float32)
    )
    bias_cols = (
        (bias_got[:, 0] + bias_got[:, 1])
        .transpose(1, 0, 2, 3)
        .reshape(head_count, length, length)
    )
    normed_cols = layer_norm(columns).astype(jnp.bfloat16)
    projected_cols = jnp.dot(
        normed_cols.reshape(-1, channels), col_project, preferred_element_type=jnp.float32
    ).reshape(length, rows_here, 4 * channels)
    qkv_cols = (
        projected_cols[..., : 3 * channels]
        .astype(jnp.bfloat16)
        .reshape(length, rows_here, 3, head_count, head_size)
    )
    col_ok = tile_rows(local_cols, tile_mask.T, length)
    mixed_cols = attend_lines(
        qkv_cols[:, :, 0],
        qkv_cols[:, :, 1],
        qkv_cols[:, :, 2],
        projected_cols[..., 3 * channels :],
        bias_cols,
        col_ok,
        chain_ids,
        chain_bias[1],
        1,
        True,
    )
    update_cols = jnp.dot(
        mixed_cols.reshape(-1, channels), col_output, preferred_element_type=jnp.float32
    ).reshape(length, rows_here, channels)
    second_pair = (columns.astype(jnp.float32) + update_cols).astype(jnp.bfloat16)
    normed_second = layer_norm(second_pair).astype(jnp.bfloat16)
    edge_mask = tile_pairs(jnp.arange(length, dtype=jnp.int32), local_cols, tile_mask, length)
    left_all = tri_acts(normed_second, tri_left, edge_mask)
    right_all = tri_acts(normed_second, tri_right, edge_mask)
    raw_chunks = second_pair.reshape(n_row, block_rows, rows_here, channels)
    raw_pieces = [lax.dynamic_index_in_dim(raw_chunks, row_index, 0, keepdims=False)]
    for shift in range(1, n_row):
        piece = lax.dynamic_index_in_dim(raw_chunks, (row_index + shift) % n_row, 0, keepdims=False)
        raw_pieces.append(
            lax.ppermute(piece, "row", perm=[(r, (r + shift) % n_row) for r in range(n_row)])
        )
    sources = (row_index - jnp.arange(n_row, dtype=jnp.int32)) % n_row
    raw_got = jnp.take(jnp.stack(raw_pieces, axis=0), sources, axis=0)
    own_pair = raw_got.transpose(1, 0, 2, 3).reshape(block_rows, block_cols, channels)
    channels_here = channels // device_count
    edges = jnp.stack([left_all, right_all], axis=0).transpose(3, 0, 1, 2)
    edges_got = lax.all_to_all(edges, ("row", "col"), 0, 3, tiled=True)
    product_part = jnp.einsum(
        "cik,cjk->cij",
        edges_got[:, 0],
        edges_got[:, 1],
        preferred_element_type=jnp.float32,
    )
    product_sent = (
        product_part.reshape(channels_here, n_row, block_rows, n_col, block_cols)
        .transpose(1, 3, 0, 2, 4)
        .reshape(device_count, channels_here, block_rows, block_cols)
    )
    product_got = lax.all_to_all(product_sent, ("row", "col"), 0, 1, tiled=True)
    product_sum = product_got.reshape(channels, block_rows, block_cols).transpose(1, 2, 0)
    normed_own = layer_norm(own_pair).astype(jnp.bfloat16)
    gate_values = jax.nn.sigmoid(
        jnp.dot(normed_own.reshape(-1, channels), tri_gate, preferred_element_type=jnp.float32)
    ).reshape(block_rows, block_cols, channels)
    centered = layer_norm(product_sum).astype(jnp.bfloat16)
    update_tri = jnp.dot(
        centered.reshape(-1, channels), tri_output, preferred_element_type=jnp.float32
    ).reshape(block_rows, block_cols, channels)
    return (own_pair.astype(jnp.float32) + gate_values * update_tri).astype(jnp.bfloat16)


def solution(mesh):
    return jax.shard_map(
        shards,
        mesh=mesh,
        in_specs=(
            P(("row", "col"), None, None),
            P(),
            P(),
            P(),
            P(),
            P(),
            P(),
            P(),
            P(),
            P(),
            P(),
            P(),
            P(),
            P(),
        ),
        out_specs=P("row", "col", None),
        check_vma=False,
    )
```

```python
import jax
import jax.numpy as jnp
from jax import lax
from jax.sharding import PartitionSpec as P


def layer_norm(values):
    values = values.astype(jnp.float32)
    center = values - jnp.mean(values, axis=-1, keepdims=True)
    spread = jnp.mean(center * center, axis=-1, keepdims=True)
    return center * lax.rsqrt(spread + 1e-05)


def tile_rows(positions, tile_table, length):
    tile_count = tile_table.shape[0]
    tile_width = length // tile_count
    onehot = (positions[:, None] // tile_width == jnp.arange(tile_count)[None, :]).astype(
        jnp.float32
    )
    picked = jnp.dot(onehot, tile_table.astype(jnp.float32))
    spread_out = jnp.broadcast_to(picked[:, :, None], (positions.shape[0], tile_count, tile_width))
    return spread_out.reshape(positions.shape[0], length) > 0.5


def tile_pairs(row_pos, col_pos, tile_table, length):
    tile_count = tile_table.shape[0]
    tile_width = length // tile_count
    row_hot = (row_pos[:, None] // tile_width == jnp.arange(tile_count)[None, :]).astype(
        jnp.float32
    )
    col_hot = (col_pos[:, None] // tile_width == jnp.arange(tile_count)[None, :]).astype(
        jnp.float32
    )
    return jnp.dot(jnp.dot(row_hot, tile_table.astype(jnp.float32)), col_hot.T)


def attend_lines(
    queries,
    key_rows,
    value_rows,
    gate_pre,
    bias_all,
    key_ok,
    chain_ids,
    chain_add,
    line_dim,
    flipped,
):
    length = queries.shape[1 - line_dim]
    head_count = queries.shape[2]
    head_size = queries.shape[3]
    width_all = head_count * head_size
    query_rows = min(128, length)
    blocks = length // query_rows
    scaling = head_size ** (-0.5)
    spec_q = "lqhd" if line_dim == 0 else "qlhd"
    spec_k = "lkhd" if line_dim == 0 else "klhd"
    usable = key_ok[:, None, None, :]

    def one_block(offset):
        query_block = lax.dynamic_slice_in_dim(queries, offset, query_rows, 1 - line_dim)
        scores = (
            jnp.einsum(
                f"{spec_q},{spec_k}->lhqk",
                query_block,
                key_rows,
                preferred_element_type=jnp.float32,
            )
            * scaling
        )
        if flipped:
            bias_block = lax.dynamic_slice_in_dim(bias_all, offset, query_rows, 2).transpose(
                0, 2, 1
            )
        else:
            bias_block = lax.dynamic_slice_in_dim(bias_all, offset, query_rows, 1)
        scores = scores + bias_block[None]
        chain_block = lax.dynamic_slice_in_dim(chain_ids, offset, query_rows, 0)
        same_chain = (chain_block[:, None] == chain_ids[None, :]).astype(jnp.float32)
        scores = scores + (chain_add[:, None, None] * same_chain[None])[None]
        scores = jnp.where(usable, scores, -1000000000.0)
        row_peak = jnp.max(scores, axis=-1, keepdims=True)
        weights = jnp.exp(scores - row_peak)
        attention = (weights / jnp.sum(weights, axis=-1, keepdims=True)).astype(jnp.bfloat16)
        mixed_rows = jnp.einsum(
            f"lhqk,{spec_k}->{spec_q}", attention, value_rows, preferred_element_type=jnp.float32
        )
        mixed_rows = mixed_rows.reshape(mixed_rows.shape[:2] + (width_all,))
        gate_block = lax.dynamic_slice_in_dim(gate_pre, offset, query_rows, 1 - line_dim)
        return (mixed_rows * jax.nn.sigmoid(gate_block)).astype(jnp.bfloat16)

    if blocks == 1:
        return one_block(0)
    outputs = lax.map(one_block, jnp.arange(blocks, dtype=jnp.int32) * query_rows)
    if line_dim == 0:
        outputs = outputs.transpose(1, 0, 2, 3)
    return outputs.reshape(gate_pre.shape[:2] + (width_all,))


def tri_acts(normed, weights, allowed):
    channels = normed.shape[-1]
    projected = jnp.dot(normed.reshape(-1, channels), weights, preferred_element_type=jnp.float32)
    projected = projected.reshape(normed.shape[0], normed.shape[1], 2 * channels)
    return (
        jax.nn.sigmoid(projected[..., channels:]) * projected[..., :channels] * allowed[..., None]
    ).astype(jnp.bfloat16)


def gather_lines(piece):
    device_count = lax.axis_size("row") * lax.axis_size("col")
    sent = jnp.broadcast_to(piece[None], (device_count,) + piece.shape)
    got = lax.all_to_all(sent, ("row", "col"), 0, 0, tiled=True)
    heads, rows_here, length = piece.shape
    return got.transpose(1, 0, 2, 3).reshape(heads, device_count * rows_here, length)


def shards(
    pair_rep,
    tile_mask,
    chain_ids,
    chain_bias,
    row_project,
    row_bias_proj,
    row_output,
    col_project,
    col_bias_proj,
    col_output,
    tri_left,
    tri_right,
    tri_gate,
    tri_output,
):
    n_row = lax.axis_size("row")
    n_col = lax.axis_size("col")
    device_count = n_row * n_col
    rows_here, length, channels = pair_rep.shape
    head_count = row_bias_proj.shape[1]
    head_size = channels // head_count
    row_index = lax.axis_index("row")
    col_index = lax.axis_index("col")
    device_index = row_index * n_col + col_index
    block_rows = length // n_row
    block_cols = length // n_col
    local_lines = device_index * rows_here + jnp.arange(rows_here, dtype=jnp.int32)
    local_cols = col_index * block_cols + row_index * rows_here + jnp.arange(rows_here, dtype=jnp.int32)
    normed = layer_norm(pair_rep).astype(jnp.bfloat16)
    flat_rows = normed.reshape(rows_here * length, channels)
    bias_rows = jnp.dot(flat_rows, row_bias_proj, preferred_element_type=jnp.float32)
    bias_rows = bias_rows.reshape(rows_here, length, head_count).transpose(2, 0, 1)
    bias_all = gather_lines(bias_rows)
    projected = jnp.dot(flat_rows, row_project, preferred_element_type=jnp.float32).reshape(
        rows_here, length, 4 * channels
    )
    qkv_rows = (
        projected[..., : 3 * channels]
        .astype(jnp.bfloat16)
        .reshape(rows_here, length, 3, head_count, head_size)
    )
    key_ok = tile_rows(local_lines, tile_mask, length)
    mixed_rows = attend_lines(
        qkv_rows[:, :, 0],
        qkv_rows[:, :, 1],
        qkv_rows[:, :, 2],
        projected[..., 3 * channels :],
        bias_all,
        key_ok,
        chain_ids,
        chain_bias[0],
        0,
        False,
    )
    update = jnp.dot(
        mixed_rows.reshape(-1, channels), row_output, preferred_element_type=jnp.float32
    ).reshape(rows_here, length, channels)
    first_pair = (pair_rep.astype(jnp.float32) + update).astype(jnp.bfloat16)
    normed_first = layer_norm(first_pair).astype(jnp.bfloat16)
    bias_next = jnp.dot(
        normed_first.reshape(-1, channels), col_bias_proj, preferred_element_type=jnp.float32
    )
    bias_next = bias_next.reshape(rows_here, length, head_count).transpose(2, 0, 1)
    pair_chunks = (
        first_pair.reshape(rows_here, n_col, n_row, rows_here, channels)
        .transpose(2, 1, 0, 3, 4)
        .reshape(device_count, rows_here * rows_here * channels)
    )
    bias_high = bias_next.astype(jnp.bfloat16)
    bias_low = (bias_next - bias_high.astype(jnp.float32)).astype(jnp.bfloat16)
    bias_words = jnp.stack([bias_high, bias_low], axis=0).reshape(1, -1)
    bias_chunks = jnp.broadcast_to(bias_words, (device_count, bias_words.shape[1]))
    merged = lax.all_to_all(
        jnp.concatenate([pair_chunks, bias_chunks], axis=1), ("row", "col"), 0, 0, tiled=True
    )
    pair_size = rows_here * rows_here * channels
    columns = merged[:, :pair_size].reshape(length, rows_here, channels)
    bias_got = (
        merged[:, pair_size:]
        .reshape(device_count, 2, head_count, rows_here, length)
        .astype(jnp.float32)
    )
    bias_cols = (
        (bias_got[:, 0] + bias_got[:, 1])
        .transpose(1, 0, 2, 3)
        .reshape(head_count, length, length)
    )
    normed_cols = layer_norm(columns).astype(jnp.bfloat16)
    projected_cols = jnp.dot(
        normed_cols.reshape(-1, channels), col_project, preferred_element_type=jnp.float32
    ).reshape(length, rows_here, 4 * channels)
    qkv_cols = (
        projected_cols[..., : 3 * channels]
        .astype(jnp.bfloat16)
        .reshape(length, rows_here, 3, head_count, head_size)
    )
    col_ok = tile_rows(local_cols, tile_mask.T, length)
    mixed_cols = attend_lines(
        qkv_cols[:, :, 0],
        qkv_cols[:, :, 1],
        qkv_cols[:, :, 2],
        projected_cols[..., 3 * channels :],
        bias_cols,
        col_ok,
        chain_ids,
        chain_bias[1],
        1,
        True,
    )
    update_cols = jnp.dot(
        mixed_cols.reshape(-1, channels), col_output, preferred_element_type=jnp.float32
    ).reshape(length, rows_here, channels)
    second_pair = (columns.astype(jnp.float32) + update_cols).astype(jnp.bfloat16)
    normed_second = layer_norm(second_pair).astype(jnp.bfloat16)
    edge_mask = tile_pairs(jnp.arange(length, dtype=jnp.int32), local_cols, tile_mask, length)
    left_all = tri_acts(normed_second, tri_left, edge_mask)
    right_all = tri_acts(normed_second, tri_right, edge_mask)
    raw_chunks = second_pair.reshape(n_row, block_rows, rows_here, channels)
    positions = jnp.arange(n_row, dtype=jnp.int32)
    if n_row & (n_row - 1) == 0:
        held = jnp.take(raw_chunks, (row_index + positions) % n_row, axis=0)
        step = 1
        while step < n_row:
            moving = [p for p in range(n_row) if p & step]
            came = lax.ppermute(
                held[jnp.array(moving)], "row", perm=[(r, (r + step) % n_row) for r in range(n_row)]
            )
            held = held.at[jnp.array(moving)].set(came)
            step *= 2
        stacked = held
    else:
        raw_pieces = [lax.dynamic_index_in_dim(raw_chunks, row_index, 0, keepdims=False)]
        for shift in range(1, n_row):
            piece = lax.dynamic_index_in_dim(raw_chunks, (row_index + shift) % n_row, 0, keepdims=False)
            raw_pieces.append(
                lax.ppermute(piece, "row", perm=[(r, (r + shift) % n_row) for r in range(n_row)])
            )
        stacked = jnp.stack(raw_pieces, axis=0)
    raw_got = jnp.take(stacked, (row_index - positions) % n_row, axis=0)
    own_pair = raw_got.transpose(1, 0, 2, 3).reshape(block_rows, block_cols, channels)
    channels_here = channels // device_count
    edges = jnp.stack([left_all, right_all], axis=0).transpose(3, 0, 1, 2)
    edges_got = lax.all_to_all(edges, ("row", "col"), 0, 3, tiled=True)
    product_part = jnp.einsum(
        "cik,cjk->cij",
        edges_got[:, 0],
        edges_got[:, 1],
        preferred_element_type=jnp.float32,
    )
    product_sent = (
        product_part.reshape(channels_here, n_row, block_rows, n_col, block_cols)
        .transpose(1, 3, 0, 2, 4)
        .reshape(device_count, channels_here, block_rows, block_cols)
    )
    product_got = lax.all_to_all(product_sent, ("row", "col"), 0, 1, tiled=True)
    product_sum = product_got.reshape(channels, block_rows, block_cols).transpose(1, 2, 0)
    normed_own = layer_norm(own_pair).astype(jnp.bfloat16)
    gate_values = jax.nn.sigmoid(
        jnp.dot(normed_own.reshape(-1, channels), tri_gate, preferred_element_type=jnp.float32)
    ).reshape(block_rows, block_cols, channels)
    centered = layer_norm(product_sum).astype(jnp.bfloat16)
    update_tri = jnp.dot(
        centered.reshape(-1, channels), tri_output, preferred_element_type=jnp.float32
    ).reshape(block_rows, block_cols, channels)
    return (own_pair.astype(jnp.float32) + gate_values * update_tri).astype(jnp.bfloat16)


def solution(mesh):
    return jax.shard_map(
        shards,
        mesh=mesh,
        in_specs=(
            P(("row", "col"), None, None),
            P(),
            P(),
            P(),
            P(),
            P(),
            P(),
            P(),
            P(),
            P(),
            P(),
            P(),
            P(),
            P(),
        ),
        out_specs=P("row", "col", None),
        check_vma=False,
    )
```

```python
import jax
import jax.numpy as jnp
from jax import lax
from jax.sharding import PartitionSpec as P


def layer_norm(values):
    values = values.astype(jnp.float32)
    center = values - jnp.mean(values, axis=-1, keepdims=True)
    spread = jnp.mean(center * center, axis=-1, keepdims=True)
    return center * lax.rsqrt(spread + 1e-05)


def tile_rows(positions, tile_table, length):
    tile_count = tile_table.shape[0]
    tile_width = length // tile_count
    onehot = (positions[:, None] // tile_width == jnp.arange(tile_count)[None, :]).astype(
        jnp.float32
    )
    picked = jnp.dot(onehot, tile_table.astype(jnp.float32))
    spread_out = jnp.broadcast_to(picked[:, :, None], (positions.shape[0], tile_count, tile_width))
    return spread_out.reshape(positions.shape[0], length) > 0.5


def tile_pairs(row_pos, col_pos, tile_table, length):
    tile_count = tile_table.shape[0]
    tile_width = length // tile_count
    row_hot = (row_pos[:, None] // tile_width == jnp.arange(tile_count)[None, :]).astype(
        jnp.float32
    )
    col_hot = (col_pos[:, None] // tile_width == jnp.arange(tile_count)[None, :]).astype(
        jnp.float32
    )
    return jnp.dot(jnp.dot(row_hot, tile_table.astype(jnp.float32)), col_hot.T)


def attend_lines(
    queries,
    key_rows,
    value_rows,
    gate_pre,
    bias_all,
    key_ok,
    chain_ids,
    chain_add,
    line_dim,
    flipped,
):
    length = queries.shape[1 - line_dim]
    head_count = queries.shape[2]
    head_size = queries.shape[3]
    width_all = head_count * head_size
    query_rows = min(128, length)
    blocks = length // query_rows
    scaling = head_size ** (-0.5)
    spec_q = "lqhd" if line_dim == 0 else "qlhd"
    spec_k = "lkhd" if line_dim == 0 else "klhd"
    usable = key_ok[:, None, None, :]

    def one_block(offset):
        query_block = lax.dynamic_slice_in_dim(queries, offset, query_rows, 1 - line_dim)
        scores = (
            jnp.einsum(
                f"{spec_q},{spec_k}->lhqk",
                query_block,
                key_rows,
                preferred_element_type=jnp.float32,
            )
            * scaling
        )
        if flipped:
            bias_block = lax.dynamic_slice_in_dim(bias_all, offset, query_rows, 2).transpose(
                0, 2, 1
            )
        else:
            bias_block = lax.dynamic_slice_in_dim(bias_all, offset, query_rows, 1)
        scores = scores + bias_block[None]
        chain_block = lax.dynamic_slice_in_dim(chain_ids, offset, query_rows, 0)
        same_chain = (chain_block[:, None] == chain_ids[None, :]).astype(jnp.float32)
        scores = scores + (chain_add[:, None, None] * same_chain[None])[None]
        scores = jnp.where(usable, scores, -1000000000.0)
        row_peak = jnp.max(scores, axis=-1, keepdims=True)
        weights = jnp.exp(scores - row_peak)
        attention = (weights / jnp.sum(weights, axis=-1, keepdims=True)).astype(jnp.bfloat16)
        mixed_rows = jnp.einsum(
            f"lhqk,{spec_k}->{spec_q}", attention, value_rows, preferred_element_type=jnp.float32
        )
        mixed_rows = mixed_rows.reshape(mixed_rows.shape[:2] + (width_all,))
        gate_block = lax.dynamic_slice_in_dim(gate_pre, offset, query_rows, 1 - line_dim)
        return (mixed_rows * jax.nn.sigmoid(gate_block)).astype(jnp.bfloat16)

    if blocks == 1:
        return one_block(0)
    outputs = lax.map(one_block, jnp.arange(blocks, dtype=jnp.int32) * query_rows)
    if line_dim == 0:
        outputs = outputs.transpose(1, 0, 2, 3)
    return outputs.reshape(gate_pre.shape[:2] + (width_all,))


def tri_acts(normed, weights, allowed):
    channels = normed.shape[-1]
    projected = jnp.dot(normed.reshape(-1, channels), weights, preferred_element_type=jnp.float32)
    projected = projected.reshape(normed.shape[0], normed.shape[1], 2 * channels)
    return (
        jax.nn.sigmoid(projected[..., channels:]) * projected[..., :channels] * allowed[..., None]
    ).astype(jnp.bfloat16)


def gather_lines(piece):
    device_count = lax.axis_size("row") * lax.axis_size("col")
    sent = jnp.broadcast_to(piece[None], (device_count,) + piece.shape)
    got = lax.all_to_all(sent, ("row", "col"), 0, 0, tiled=True)
    heads, rows_here, length = piece.shape
    return got.transpose(1, 0, 2, 3).reshape(heads, device_count * rows_here, length)


def shards(
    pair_rep,
    tile_mask,
    chain_ids,
    chain_bias,
    row_project,
    row_bias_proj,
    row_output,
    col_project,
    col_bias_proj,
    col_output,
    tri_left,
    tri_right,
    tri_gate,
    tri_output,
):
    n_row = lax.axis_size("row")
    n_col = lax.axis_size("col")
    device_count = n_row * n_col
    rows_here, length, channels = pair_rep.shape
    head_count = row_bias_proj.shape[1]
    head_size = channels // head_count
    row_index = lax.axis_index("row")
    col_index = lax.axis_index("col")
    device_index = row_index * n_col + col_index
    block_rows = length // n_row
    block_cols = length // n_col
    local_lines = device_index * rows_here + jnp.arange(rows_here, dtype=jnp.int32)
    local_cols = col_index * block_cols + row_index * rows_here + jnp.arange(rows_here, dtype=jnp.int32)
    normed = layer_norm(pair_rep).astype(jnp.bfloat16)
    flat_rows = normed.reshape(rows_here * length, channels)
    bias_rows = jnp.dot(flat_rows, row_bias_proj, preferred_element_type=jnp.float32)
    bias_rows = bias_rows.reshape(rows_here, length, head_count).transpose(2, 0, 1)
    bias_all = gather_lines(bias_rows)
    projected = jnp.dot(flat_rows, row_project, preferred_element_type=jnp.float32).reshape(
        rows_here, length, 4 * channels
    )
    qkv_rows = (
        projected[..., : 3 * channels]
        .astype(jnp.bfloat16)
        .reshape(rows_here, length, 3, head_count, head_size)
    )
    key_ok = tile_rows(local_lines, tile_mask, length)
    mixed_rows = attend_lines(
        qkv_rows[:, :, 0],
        qkv_rows[:, :, 1],
        qkv_rows[:, :, 2],
        projected[..., 3 * channels :],
        bias_all,
        key_ok,
        chain_ids,
        chain_bias[0],
        0,
        False,
    )
    update = jnp.dot(
        mixed_rows.reshape(-1, channels), row_output, preferred_element_type=jnp.float32
    ).reshape(rows_here, length, channels)
    first_pair = (pair_rep.astype(jnp.float32) + update).astype(jnp.bfloat16)
    normed_first = layer_norm(first_pair).astype(jnp.bfloat16)
    bias_next = jnp.dot(
        normed_first.reshape(-1, channels), col_bias_proj, preferred_element_type=jnp.float32
    )
    bias_next = bias_next.reshape(rows_here, length, head_count).transpose(2, 0, 1)
    lanes = 128
    pair_chunks = (
        first_pair.reshape(rows_here, n_col, n_row, rows_here, channels)
        .transpose(2, 1, 0, 3, 4)
        .reshape(device_count, rows_here * rows_here * channels // lanes, lanes)
    )
    bias_high = bias_next.astype(jnp.bfloat16)
    bias_low = (bias_next - bias_high.astype(jnp.float32)).astype(jnp.bfloat16)
    bias_words = jnp.stack([bias_high, bias_low], axis=0).reshape(1, -1, lanes)
    bias_chunks = jnp.broadcast_to(bias_words, (device_count,) + bias_words.shape[1:])
    merged = lax.all_to_all(
        jnp.concatenate([pair_chunks, bias_chunks], axis=1), ("row", "col"), 0, 0, tiled=True
    )
    pair_rows = pair_chunks.shape[1]
    columns = merged[:, :pair_rows].reshape(length, rows_here, channels)
    bias_got = (
        merged[:, pair_rows:]
        .reshape(device_count, 2, head_count, rows_here, length)
        .astype(jnp.float32)
    )
    bias_cols = (
        (bias_got[:, 0] + bias_got[:, 1])
        .transpose(1, 0, 2, 3)
        .reshape(head_count, length, length)
    )
    normed_cols = layer_norm(columns).astype(jnp.bfloat16)
    projected_cols = jnp.dot(
        normed_cols.reshape(-1, channels), col_project, preferred_element_type=jnp.float32
    ).reshape(length, rows_here, 4 * channels)
    qkv_cols = (
        projected_cols[..., : 3 * channels]
        .astype(jnp.bfloat16)
        .reshape(length, rows_here, 3, head_count, head_size)
    )
    col_ok = tile_rows(local_cols, tile_mask.T, length)
    mixed_cols = attend_lines(
        qkv_cols[:, :, 0],
        qkv_cols[:, :, 1],
        qkv_cols[:, :, 2],
        projected_cols[..., 3 * channels :],
        bias_cols,
        col_ok,
        chain_ids,
        chain_bias[1],
        1,
        True,
    )
    update_cols = jnp.dot(
        mixed_cols.reshape(-1, channels), col_output, preferred_element_type=jnp.float32
    ).reshape(length, rows_here, channels)
    second_pair = (columns.astype(jnp.float32) + update_cols).astype(jnp.bfloat16)
    normed_second = layer_norm(second_pair).astype(jnp.bfloat16)
    edge_mask = tile_pairs(jnp.arange(length, dtype=jnp.int32), local_cols, tile_mask, length)
    left_all = tri_acts(normed_second, tri_left, edge_mask)
    right_all = tri_acts(normed_second, tri_right, edge_mask)
    raw_chunks = second_pair.reshape(n_row, block_rows, rows_here, channels)
    raw_pieces = [lax.dynamic_index_in_dim(raw_chunks, row_index, 0, keepdims=False)]
    for shift in range(1, n_row):
        piece = lax.dynamic_index_in_dim(raw_chunks, (row_index + shift) % n_row, 0, keepdims=False)
        raw_pieces.append(
            lax.ppermute(piece, "row", perm=[(r, (r + shift) % n_row) for r in range(n_row)])
        )
    sources = (row_index - jnp.arange(n_row, dtype=jnp.int32)) % n_row
    raw_got = jnp.take(jnp.stack(raw_pieces, axis=0), sources, axis=0)
    own_pair = raw_got.transpose(1, 0, 2, 3).reshape(block_rows, block_cols, channels)
    channels_here = channels // device_count
    edges = jnp.stack([left_all, right_all], axis=0).transpose(3, 0, 1, 2)
    edges_got = lax.all_to_all(edges, ("row", "col"), 0, 3, tiled=True)
    product_part = jnp.einsum(
        "cik,cjk->cij",
        edges_got[:, 0],
        edges_got[:, 1],
        preferred_element_type=jnp.float32,
    )
    product_sent = (
        product_part.reshape(channels_here, n_row, block_rows, n_col, block_cols)
        .transpose(1, 3, 0, 2, 4)
        .reshape(device_count, channels_here, block_rows, block_cols)
    )
    product_got = lax.all_to_all(
        product_sent.reshape(device_count, -1, lanes), ("row", "col"), 0, 0, tiled=True
    )
    product_sum = product_got.reshape(channels, block_rows, block_cols).transpose(1, 2, 0)
    normed_own = layer_norm(own_pair).astype(jnp.bfloat16)
    gate_values = jax.nn.sigmoid(
        jnp.dot(normed_own.reshape(-1, channels), tri_gate, preferred_element_type=jnp.float32)
    ).reshape(block_rows, block_cols, channels)
    centered = layer_norm(product_sum).astype(jnp.bfloat16)
    update_tri = jnp.dot(
        centered.reshape(-1, channels), tri_output, preferred_element_type=jnp.float32
    ).reshape(block_rows, block_cols, channels)
    return (own_pair.astype(jnp.float32) + gate_values * update_tri).astype(jnp.bfloat16)


def solution(mesh):
    return jax.shard_map(
        shards,
        mesh=mesh,
        in_specs=(
            P(("row", "col"), None, None),
            P(),
            P(),
            P(),
            P(),
            P(),
            P(),
            P(),
            P(),
            P(),
            P(),
            P(),
            P(),
            P(),
        ),
        out_specs=P("row", "col", None),
        check_vma=False,
    )
```

```python
import jax
import jax.numpy as jnp
from jax import lax
from jax.sharding import PartitionSpec as P


def layer_norm(values):
    values = values.astype(jnp.float32)
    center = values - jnp.mean(values, axis=-1, keepdims=True)
    spread = jnp.mean(center * center, axis=-1, keepdims=True)
    return center * lax.rsqrt(spread + 1e-05)


def tile_rows(positions, tile_table, length):
    tile_count = tile_table.shape[0]
    tile_width = length // tile_count
    onehot = (positions[:, None] // tile_width == jnp.arange(tile_count)[None, :]).astype(
        jnp.float32
    )
    picked = jnp.dot(onehot, tile_table.astype(jnp.float32))
    spread_out = jnp.broadcast_to(picked[:, :, None], (positions.shape[0], tile_count, tile_width))
    return spread_out.reshape(positions.shape[0], length) > 0.5


def tile_pairs(row_pos, col_pos, tile_table, length):
    tile_count = tile_table.shape[0]
    tile_width = length // tile_count
    row_hot = (row_pos[:, None] // tile_width == jnp.arange(tile_count)[None, :]).astype(
        jnp.float32
    )
    col_hot = (col_pos[:, None] // tile_width == jnp.arange(tile_count)[None, :]).astype(
        jnp.float32
    )
    return jnp.dot(jnp.dot(row_hot, tile_table.astype(jnp.float32)), col_hot.T)


def attend_lines(
    queries,
    key_rows,
    value_rows,
    gate_pre,
    bias_all,
    key_ok,
    chain_ids,
    chain_add,
    line_dim,
    flipped,
):
    length = queries.shape[1 - line_dim]
    head_count = queries.shape[2]
    head_size = queries.shape[3]
    width_all = head_count * head_size
    query_rows = min(128, length)
    blocks = length // query_rows
    scaling = head_size ** (-0.5)
    spec_q = "lqhd" if line_dim == 0 else "qlhd"
    spec_k = "lkhd" if line_dim == 0 else "klhd"
    usable = key_ok[:, None, None, :]
    if flipped:
        bias_all = bias_all.transpose(0, 2, 1)
    same_all = (chain_ids[:, None] == chain_ids[None, :]).astype(jnp.float32)
    bias_all = bias_all + chain_add[:, None, None] * same_all[None]

    def one_block(offset):
        query_block = lax.dynamic_slice_in_dim(queries, offset, query_rows, 1 - line_dim)
        scores = (
            jnp.einsum(
                f"{spec_q},{spec_k}->lhqk",
                query_block,
                key_rows,
                preferred_element_type=jnp.float32,
            )
            * scaling
        )
        bias_block = lax.dynamic_slice_in_dim(bias_all, offset, query_rows, 1)
        scores = scores + bias_block[None]
        scores = jnp.where(usable, scores, -1000000000.0)
        row_peak = jnp.max(scores, axis=-1, keepdims=True)
        weights = jnp.exp(scores - row_peak)
        attention = (weights / jnp.sum(weights, axis=-1, keepdims=True)).astype(jnp.bfloat16)
        mixed_rows = jnp.einsum(
            f"lhqk,{spec_k}->{spec_q}", attention, value_rows, preferred_element_type=jnp.float32
        )
        mixed_rows = mixed_rows.reshape(mixed_rows.shape[:2] + (width_all,))
        gate_block = lax.dynamic_slice_in_dim(gate_pre, offset, query_rows, 1 - line_dim)
        return (mixed_rows * jax.nn.sigmoid(gate_block)).astype(jnp.bfloat16)

    if blocks == 1:
        return one_block(0)
    outputs = lax.map(one_block, jnp.arange(blocks, dtype=jnp.int32) * query_rows)
    if line_dim == 0:
        outputs = outputs.transpose(1, 0, 2, 3)
    return outputs.reshape(gate_pre.shape[:2] + (width_all,))


def tri_acts(normed, weights, allowed):
    channels = normed.shape[-1]
    projected = jnp.dot(normed.reshape(-1, channels), weights, preferred_element_type=jnp.float32)
    projected = projected.reshape(normed.shape[0], normed.shape[1], 2 * channels)
    return (
        jax.nn.sigmoid(projected[..., channels:]) * projected[..., :channels] * allowed[..., None]
    ).astype(jnp.bfloat16)


def gather_lines(piece):
    device_count = lax.axis_size("row") * lax.axis_size("col")
    sent = jnp.broadcast_to(piece[None], (device_count,) + piece.shape)
    got = lax.all_to_all(sent, ("row", "col"), 0, 0, tiled=True)
    heads, rows_here, length = piece.shape
    return got.transpose(1, 0, 2, 3).reshape(heads, device_count * rows_here, length)


def shards(
    pair_rep,
    tile_mask,
    chain_ids,
    chain_bias,
    row_project,
    row_bias_proj,
    row_output,
    col_project,
    col_bias_proj,
    col_output,
    tri_left,
    tri_right,
    tri_gate,
    tri_output,
):
    n_row = lax.axis_size("row")
    n_col = lax.axis_size("col")
    device_count = n_row * n_col
    rows_here, length, channels = pair_rep.shape
    head_count = row_bias_proj.shape[1]
    head_size = channels // head_count
    row_index = lax.axis_index("row")
    col_index = lax.axis_index("col")
    device_index = row_index * n_col + col_index
    block_rows = length // n_row
    block_cols = length // n_col
    local_lines = device_index * rows_here + jnp.arange(rows_here, dtype=jnp.int32)
    local_cols = col_index * block_cols + row_index * rows_here + jnp.arange(rows_here, dtype=jnp.int32)
    normed = layer_norm(pair_rep).astype(jnp.bfloat16)
    flat_rows = normed.reshape(rows_here * length, channels)
    bias_rows = jnp.dot(flat_rows, row_bias_proj, preferred_element_type=jnp.float32)
    bias_rows = bias_rows.reshape(rows_here, length, head_count).transpose(2, 0, 1)
    bias_all = gather_lines(bias_rows)
    projected = jnp.dot(flat_rows, row_project, preferred_element_type=jnp.float32).reshape(
        rows_here, length, 4 * channels
    )
    qkv_rows = (
        projected[..., : 3 * channels]
        .astype(jnp.bfloat16)
        .reshape(rows_here, length, 3, head_count, head_size)
    )
    key_ok = tile_rows(local_lines, tile_mask, length)
    mixed_rows = attend_lines(
        qkv_rows[:, :, 0],
        qkv_rows[:, :, 1],
        qkv_rows[:, :, 2],
        projected[..., 3 * channels :],
        bias_all,
        key_ok,
        chain_ids,
        chain_bias[0],
        0,
        False,
    )
    update = jnp.dot(
        mixed_rows.reshape(-1, channels), row_output, preferred_element_type=jnp.float32
    ).reshape(rows_here, length, channels)
    first_pair = (pair_rep.astype(jnp.float32) + update).astype(jnp.bfloat16)
    normed_first = layer_norm(first_pair).astype(jnp.bfloat16)
    bias_next = jnp.dot(
        normed_first.reshape(-1, channels), col_bias_proj, preferred_element_type=jnp.float32
    )
    bias_next = bias_next.reshape(rows_here, length, head_count).transpose(2, 0, 1)
    lanes = 128
    pair_chunks = (
        first_pair.reshape(rows_here, n_col, n_row, rows_here, channels)
        .transpose(2, 1, 0, 3, 4)
        .reshape(device_count, rows_here * rows_here * channels // lanes, lanes)
    )
    bias_high = bias_next.astype(jnp.bfloat16)
    bias_low = (bias_next - bias_high.astype(jnp.float32)).astype(jnp.bfloat16)
    bias_words = jnp.stack([bias_high, bias_low], axis=0).reshape(1, -1, lanes)
    bias_chunks = jnp.broadcast_to(bias_words, (device_count,) + bias_words.shape[1:])
    merged = lax.all_to_all(
        jnp.concatenate([pair_chunks, bias_chunks], axis=1), ("row", "col"), 0, 0, tiled=True
    )
    pair_rows = pair_chunks.shape[1]
    columns = merged[:, :pair_rows].reshape(length, rows_here, channels)
    bias_got = (
        merged[:, pair_rows:]
        .reshape(device_count, 2, head_count, rows_here, length)
        .astype(jnp.float32)
    )
    bias_cols = (
        (bias_got[:, 0] + bias_got[:, 1])
        .transpose(1, 0, 2, 3)
        .reshape(head_count, length, length)
    )
    normed_cols = layer_norm(columns).astype(jnp.bfloat16)
    projected_cols = jnp.dot(
        normed_cols.reshape(-1, channels), col_project, preferred_element_type=jnp.float32
    ).reshape(length, rows_here, 4 * channels)
    qkv_cols = (
        projected_cols[..., : 3 * channels]
        .astype(jnp.bfloat16)
        .reshape(length, rows_here, 3, head_count, head_size)
    )
    col_ok = tile_rows(local_cols, tile_mask.T, length)
    mixed_cols = attend_lines(
        qkv_cols[:, :, 0],
        qkv_cols[:, :, 1],
        qkv_cols[:, :, 2],
        projected_cols[..., 3 * channels :],
        bias_cols,
        col_ok,
        chain_ids,
        chain_bias[1],
        1,
        True,
    )
    update_cols = jnp.dot(
        mixed_cols.reshape(-1, channels), col_output, preferred_element_type=jnp.float32
    ).reshape(length, rows_here, channels)
    second_pair = (columns.astype(jnp.float32) + update_cols).astype(jnp.bfloat16)
    normed_second = layer_norm(second_pair).astype(jnp.bfloat16)
    edge_mask = tile_pairs(jnp.arange(length, dtype=jnp.int32), local_cols, tile_mask, length)
    left_all = tri_acts(normed_second, tri_left, edge_mask)
    right_all = tri_acts(normed_second, tri_right, edge_mask)
    raw_chunks = second_pair.reshape(n_row, block_rows, rows_here, channels)
    raw_pieces = [lax.dynamic_index_in_dim(raw_chunks, row_index, 0, keepdims=False)]
    for shift in range(1, n_row):
        piece = lax.dynamic_index_in_dim(raw_chunks, (row_index + shift) % n_row, 0, keepdims=False)
        raw_pieces.append(
            lax.ppermute(piece, "row", perm=[(r, (r + shift) % n_row) for r in range(n_row)])
        )
    sources = (row_index - jnp.arange(n_row, dtype=jnp.int32)) % n_row
    raw_got = jnp.take(jnp.stack(raw_pieces, axis=0), sources, axis=0)
    own_pair = raw_got.transpose(1, 0, 2, 3).reshape(block_rows, block_cols, channels)
    channels_here = channels // device_count
    edges = jnp.stack([left_all, right_all], axis=0).transpose(3, 0, 1, 2)
    edges_got = lax.all_to_all(edges, ("row", "col"), 0, 3, tiled=True)
    product_part = jnp.einsum(
        "cik,cjk->cij",
        edges_got[:, 0],
        edges_got[:, 1],
        preferred_element_type=jnp.float32,
    )
    product_sent = (
        product_part.reshape(channels_here, n_row, block_rows, n_col, block_cols)
        .transpose(1, 3, 0, 2, 4)
        .reshape(device_count, channels_here, block_rows, block_cols)
    )
    product_got = lax.all_to_all(
        product_sent.reshape(device_count, -1, lanes), ("row", "col"), 0, 0, tiled=True
    )
    product_sum = product_got.reshape(channels, block_rows, block_cols).transpose(1, 2, 0)
    normed_own = layer_norm(own_pair).astype(jnp.bfloat16)
    gate_values = jax.nn.sigmoid(
        jnp.dot(normed_own.reshape(-1, channels), tri_gate, preferred_element_type=jnp.float32)
    ).reshape(block_rows, block_cols, channels)
    centered = layer_norm(product_sum).astype(jnp.bfloat16)
    update_tri = jnp.dot(
        centered.reshape(-1, channels), tri_output, preferred_element_type=jnp.float32
    ).reshape(block_rows, block_cols, channels)
    return (own_pair.astype(jnp.float32) + gate_values * update_tri).astype(jnp.bfloat16)


def solution(mesh):
    return jax.shard_map(
        shards,
        mesh=mesh,
        in_specs=(
            P(("row", "col"), None, None),
            P(),
            P(),
            P(),
            P(),
            P(),
            P(),
            P(),
            P(),
            P(),
            P(),
            P(),
            P(),
            P(),
        ),
        out_specs=P("row", "col", None),
        check_vma=False,
    )
```

```python
import jax
import jax.numpy as jnp
from jax import lax
from jax.sharding import PartitionSpec as P


def layer_norm(values):
    values = values.astype(jnp.float32)
    center = values - jnp.mean(values, axis=-1, keepdims=True)
    spread = jnp.mean(center * center, axis=-1, keepdims=True)
    return center * lax.rsqrt(spread + 1e-05)


def tile_rows(positions, tile_table, length):
    tile_count = tile_table.shape[0]
    tile_width = length // tile_count
    onehot = (positions[:, None] // tile_width == jnp.arange(tile_count)[None, :]).astype(
        jnp.float32
    )
    picked = jnp.dot(onehot, tile_table.astype(jnp.float32))
    spread_out = jnp.broadcast_to(picked[:, :, None], (positions.shape[0], tile_count, tile_width))
    return spread_out.reshape(positions.shape[0], length) > 0.5


def tile_pairs(row_pos, col_pos, tile_table, length):
    tile_count = tile_table.shape[0]
    tile_width = length // tile_count
    row_hot = (row_pos[:, None] // tile_width == jnp.arange(tile_count)[None, :]).astype(
        jnp.float32
    )
    col_hot = (col_pos[:, None] // tile_width == jnp.arange(tile_count)[None, :]).astype(
        jnp.float32
    )
    return jnp.dot(jnp.dot(row_hot, tile_table.astype(jnp.float32)), col_hot.T)


def attend_lines(
    queries,
    key_rows,
    value_rows,
    gate_pre,
    bias_all,
    key_ok,
    chain_ids,
    chain_add,
    line_dim,
    flipped,
):
    length = queries.shape[1 - line_dim]
    head_count = queries.shape[2]
    head_size = queries.shape[3]
    width_all = head_count * head_size
    query_rows = min(128, length)
    blocks = length // query_rows
    scaling = head_size ** (-0.5)
    spec_q = "lqhd" if line_dim == 0 else "qlhd"
    spec_k = "lkhd" if line_dim == 0 else "klhd"
    usable = key_ok[:, None, None, :]
    if flipped:
        bias_all = bias_all.transpose(0, 2, 1)
    same_all = (chain_ids[:, None] == chain_ids[None, :]).astype(jnp.float32)
    bias_all = bias_all + chain_add[:, None, None] * same_all[None]

    def one_block(offset):
        query_block = lax.dynamic_slice_in_dim(queries, offset, query_rows, 1 - line_dim)
        scores = (
            jnp.einsum(
                f"{spec_q},{spec_k}->lhqk",
                query_block,
                key_rows,
                preferred_element_type=jnp.float32,
            )
            * scaling
        )
        bias_block = lax.dynamic_slice_in_dim(bias_all, offset, query_rows, 1)
        scores = scores + bias_block[None]
        scores = jnp.where(usable, scores, -1000000000.0)
        row_peak = jnp.max(scores, axis=-1, keepdims=True)
        weights = jnp.exp(scores - row_peak)
        attention = (weights / jnp.sum(weights, axis=-1, keepdims=True)).astype(jnp.bfloat16)
        mixed_rows = jnp.einsum(
            f"lhqk,{spec_k}->{spec_q}", attention, value_rows, preferred_element_type=jnp.float32
        )
        mixed_rows = mixed_rows.reshape(mixed_rows.shape[:2] + (width_all,))
        gate_block = lax.dynamic_slice_in_dim(gate_pre, offset, query_rows, 1 - line_dim)
        return (mixed_rows * jax.nn.sigmoid(gate_block)).astype(jnp.bfloat16)

    if blocks == 1:
        return one_block(0)
    outputs = lax.map(one_block, jnp.arange(blocks, dtype=jnp.int32) * query_rows)
    if line_dim == 0:
        outputs = outputs.transpose(1, 0, 2, 3)
    return outputs.reshape(gate_pre.shape[:2] + (width_all,))


def tri_acts(normed, weights, allowed):
    channels = normed.shape[-1]
    projected = jnp.dot(normed.reshape(-1, channels), weights, preferred_element_type=jnp.float32)
    projected = projected.reshape(normed.shape[0], normed.shape[1], 2 * channels)
    return (
        jax.nn.sigmoid(projected[..., channels:]) * projected[..., :channels] * allowed[..., None]
    ).astype(jnp.bfloat16)


def gather_lines(piece):
    device_count = lax.axis_size("row") * lax.axis_size("col")
    sent = jnp.broadcast_to(piece[None], (device_count,) + piece.shape)
    got = lax.all_to_all(sent, ("row", "col"), 0, 0, tiled=True)
    heads, rows_here, length = piece.shape
    return got.transpose(1, 0, 2, 3).reshape(heads, device_count * rows_here, length)


def shards(
    pair_rep,
    tile_mask,
    chain_ids,
    chain_bias,
    row_project,
    row_bias_proj,
    row_output,
    col_project,
    col_bias_proj,
    col_output,
    tri_left,
    tri_right,
    tri_gate,
    tri_output,
):
    n_row = lax.axis_size("row")
    n_col = lax.axis_size("col")
    device_count = n_row * n_col
    rows_here, length, channels = pair_rep.shape
    head_count = row_bias_proj.shape[1]
    head_size = channels // head_count
    row_index = lax.axis_index("row")
    col_index = lax.axis_index("col")
    device_index = row_index * n_col + col_index
    block_rows = length // n_row
    block_cols = length // n_col
    local_lines = device_index * rows_here + jnp.arange(rows_here, dtype=jnp.int32)
    local_cols = col_index * block_cols + row_index * rows_here + jnp.arange(rows_here, dtype=jnp.int32)
    normed = layer_norm(pair_rep).astype(jnp.bfloat16)
    flat_rows = normed.reshape(rows_here * length, channels)
    bias_rows = jnp.dot(flat_rows, row_bias_proj, preferred_element_type=jnp.float32)
    bias_rows = bias_rows.reshape(rows_here, length, head_count).transpose(2, 0, 1)
    bias_all = gather_lines(bias_rows)
    projected = jnp.dot(flat_rows, row_project, preferred_element_type=jnp.float32).reshape(
        rows_here, length, 4 * channels
    )
    qkv_rows = (
        projected[..., : 3 * channels]
        .astype(jnp.bfloat16)
        .reshape(rows_here, length, 3, head_count, head_size)
    )
    key_ok = tile_rows(local_lines, tile_mask, length)
    mixed_rows = attend_lines(
        qkv_rows[:, :, 0],
        qkv_rows[:, :, 1],
        qkv_rows[:, :, 2],
        projected[..., 3 * channels :],
        bias_all,
        key_ok,
        chain_ids,
        chain_bias[0],
        0,
        False,
    )
    update = jnp.dot(
        mixed_rows.reshape(-1, channels), row_output, preferred_element_type=jnp.float32
    ).reshape(rows_here, length, channels)
    first_pair = (pair_rep.astype(jnp.float32) + update).astype(jnp.bfloat16)
    normed_first = layer_norm(first_pair).astype(jnp.bfloat16)
    bias_next = jnp.dot(
        normed_first.reshape(-1, channels), col_bias_proj, preferred_element_type=jnp.float32
    )
    bias_next = bias_next.reshape(rows_here, length, head_count).transpose(2, 0, 1)
    lanes = 128
    pair_chunks = (
        first_pair.reshape(rows_here, n_col, n_row, rows_here, channels)
        .transpose(2, 1, 0, 3, 4)
        .reshape(device_count, rows_here * rows_here * channels // lanes, lanes)
    )
    bias_high = bias_next.astype(jnp.bfloat16)
    bias_low = (bias_next - bias_high.astype(jnp.float32)).astype(jnp.bfloat16)
    bias_words = jnp.stack([bias_high, bias_low], axis=0).reshape(1, -1, lanes)
    bias_chunks = jnp.broadcast_to(bias_words, (device_count,) + bias_words.shape[1:])
    merged = lax.all_to_all(
        jnp.concatenate([pair_chunks, bias_chunks], axis=1), ("row", "col"), 0, 0, tiled=True
    )
    pair_rows = pair_chunks.shape[1]
    columns = merged[:, :pair_rows].reshape(length, rows_here, channels)
    bias_got = (
        merged[:, pair_rows:]
        .reshape(device_count, 2, head_count, rows_here, length)
        .astype(jnp.float32)
    )
    bias_cols = (
        (bias_got[:, 0] + bias_got[:, 1])
        .transpose(1, 0, 2, 3)
        .reshape(head_count, length, length)
    )
    normed_cols = layer_norm(columns).astype(jnp.bfloat16)
    projected_cols = jnp.dot(
        normed_cols.reshape(-1, channels), col_project, preferred_element_type=jnp.float32
    ).reshape(length, rows_here, 4 * channels)
    qkv_cols = (
        projected_cols[..., : 3 * channels]
        .astype(jnp.bfloat16)
        .reshape(length, rows_here, 3, head_count, head_size)
    )
    col_ok = tile_rows(local_cols, tile_mask.T, length)
    mixed_cols = attend_lines(
        qkv_cols[:, :, 0],
        qkv_cols[:, :, 1],
        qkv_cols[:, :, 2],
        projected_cols[..., 3 * channels :],
        bias_cols,
        col_ok,
        chain_ids,
        chain_bias[1],
        1,
        True,
    )
    update_cols = jnp.dot(
        mixed_cols.reshape(-1, channels), col_output, preferred_element_type=jnp.float32
    ).reshape(length, rows_here, channels)
    second_pair = (columns.astype(jnp.float32) + update_cols).astype(jnp.bfloat16)
    normed_second = layer_norm(second_pair).astype(jnp.bfloat16)
    edge_mask = tile_pairs(jnp.arange(length, dtype=jnp.int32), local_cols, tile_mask, length)
    left_all = tri_acts(normed_second, tri_left, edge_mask)
    right_all = tri_acts(normed_second, tri_right, edge_mask)
    raw_got = lax.all_to_all(
        second_pair.reshape(n_row, block_rows, rows_here, channels), "row", 0, 0, tiled=True
    )
    own_pair = raw_got.transpose(1, 0, 2, 3).reshape(block_rows, block_cols, channels)
    channels_here = channels // device_count
    edges = jnp.stack([left_all, right_all], axis=0).transpose(3, 0, 1, 2)
    edges_got = lax.all_to_all(edges, ("row", "col"), 0, 3, tiled=True)
    product_part = jnp.einsum(
        "cik,cjk->cij",
        edges_got[:, 0],
        edges_got[:, 1],
        preferred_element_type=jnp.float32,
    )
    product_sent = (
        product_part.reshape(channels_here, n_row, block_rows, n_col, block_cols)
        .transpose(1, 3, 0, 2, 4)
        .reshape(device_count, channels_here, block_rows, block_cols)
    )
    product_got = lax.all_to_all(
        product_sent.reshape(device_count, -1, lanes), ("row", "col"), 0, 0, tiled=True
    )
    product_sum = product_got.reshape(channels, block_rows, block_cols).transpose(1, 2, 0)
    normed_own = layer_norm(own_pair).astype(jnp.bfloat16)
    gate_values = jax.nn.sigmoid(
        jnp.dot(normed_own.reshape(-1, channels), tri_gate, preferred_element_type=jnp.float32)
    ).reshape(block_rows, block_cols, channels)
    centered = layer_norm(product_sum).astype(jnp.bfloat16)
    update_tri = jnp.dot(
        centered.reshape(-1, channels), tri_output, preferred_element_type=jnp.float32
    ).reshape(block_rows, block_cols, channels)
    return (own_pair.astype(jnp.float32) + gate_values * update_tri).astype(jnp.bfloat16)


def solution(mesh):
    return jax.shard_map(
        shards,
        mesh=mesh,
        in_specs=(
            P(("row", "col"), None, None),
            P(),
            P(),
            P(),
            P(),
            P(),
            P(),
            P(),
            P(),
            P(),
            P(),
            P(),
            P(),
            P(),
        ),
        out_specs=P("row", "col", None),
        check_vma=False,
    )
```

```python
import jax
import jax.numpy as jnp
from jax import lax
from jax.sharding import PartitionSpec as P


def layer_norm(values):
    values = values.astype(jnp.float32)
    center = values - jnp.mean(values, axis=-1, keepdims=True)
    spread = jnp.mean(center * center, axis=-1, keepdims=True)
    return center * lax.rsqrt(spread + 1e-05)


def tile_rows(positions, tile_table, length):
    tile_count = tile_table.shape[0]
    tile_width = length // tile_count
    onehot = (positions[:, None] // tile_width == jnp.arange(tile_count)[None, :]).astype(
        jnp.float32
    )
    picked = jnp.dot(onehot, tile_table.astype(jnp.float32))
    spread_out = jnp.broadcast_to(picked[:, :, None], (positions.shape[0], tile_count, tile_width))
    return spread_out.reshape(positions.shape[0], length) > 0.5


def tile_pairs(row_pos, col_pos, tile_table, length):
    tile_count = tile_table.shape[0]
    tile_width = length // tile_count
    row_hot = (row_pos[:, None] // tile_width == jnp.arange(tile_count)[None, :]).astype(
        jnp.float32
    )
    col_hot = (col_pos[:, None] // tile_width == jnp.arange(tile_count)[None, :]).astype(
        jnp.float32
    )
    return jnp.dot(jnp.dot(row_hot, tile_table.astype(jnp.float32)), col_hot.T)


def attend_lines(
    queries,
    key_rows,
    value_rows,
    gate_pre,
    bias_all,
    key_ok,
    chain_ids,
    chain_add,
    line_dim,
    flipped,
):
    length = queries.shape[1 - line_dim]
    head_count = queries.shape[2]
    head_size = queries.shape[3]
    width_all = head_count * head_size
    query_rows = min(128, length)
    blocks = length // query_rows
    scaling = head_size ** (-0.5)
    spec_q = "lqhd" if line_dim == 0 else "qlhd"
    spec_k = "lkhd" if line_dim == 0 else "klhd"
    usable = key_ok[:, None, None, :]
    if flipped:
        bias_all = bias_all.transpose(0, 2, 1)
    same_all = (chain_ids[:, None] == chain_ids[None, :]).astype(jnp.float32)
    bias_all = bias_all + chain_add[:, None, None] * same_all[None]

    def one_block(offset):
        query_block = lax.dynamic_slice_in_dim(queries, offset, query_rows, 1 - line_dim)
        scores = (
            jnp.einsum(
                f"{spec_q},{spec_k}->lhqk",
                query_block,
                key_rows,
                preferred_element_type=jnp.float32,
            )
            * scaling
        )
        bias_block = lax.dynamic_slice_in_dim(bias_all, offset, query_rows, 1)
        scores = scores + bias_block[None]
        scores = jnp.where(usable, scores, -1000000000.0)
        row_peak = jnp.max(scores, axis=-1, keepdims=True)
        weights = jnp.exp(scores - row_peak)
        attention = (weights / jnp.sum(weights, axis=-1, keepdims=True)).astype(jnp.bfloat16)
        mixed_rows = jnp.einsum(
            f"lhqk,{spec_k}->{spec_q}", attention, value_rows, preferred_element_type=jnp.float32
        )
        mixed_rows = mixed_rows.reshape(mixed_rows.shape[:2] + (width_all,))
        gate_block = lax.dynamic_slice_in_dim(gate_pre, offset, query_rows, 1 - line_dim)
        return (mixed_rows * jax.nn.sigmoid(gate_block)).astype(jnp.bfloat16)

    if blocks == 1:
        return one_block(0)
    outputs = lax.map(one_block, jnp.arange(blocks, dtype=jnp.int32) * query_rows)
    if line_dim == 0:
        outputs = outputs.transpose(1, 0, 2, 3)
    return outputs.reshape(gate_pre.shape[:2] + (width_all,))


def tri_acts(normed, weights, allowed):
    channels = normed.shape[-1]
    projected = jnp.dot(normed.reshape(-1, channels), weights, preferred_element_type=jnp.float32)
    projected = projected.reshape(normed.shape[0], normed.shape[1], 2 * channels)
    return (
        jax.nn.sigmoid(projected[..., channels:]) * projected[..., :channels] * allowed[..., None]
    ).astype(jnp.bfloat16)


def gather_lines(piece):
    device_count = lax.axis_size("row") * lax.axis_size("col")
    sent = jnp.broadcast_to(piece[None], (device_count,) + piece.shape)
    got = lax.all_to_all(sent, ("row", "col"), 0, 0, tiled=True)
    heads, rows_here, length = piece.shape
    return got.transpose(1, 0, 2, 3).reshape(heads, device_count * rows_here, length)


def shards(
    pair_rep,
    tile_mask,
    chain_ids,
    chain_bias,
    row_project,
    row_bias_proj,
    row_output,
    col_project,
    col_bias_proj,
    col_output,
    tri_left,
    tri_right,
    tri_gate,
    tri_output,
):
    n_row = lax.axis_size("row")
    n_col = lax.axis_size("col")
    device_count = n_row * n_col
    rows_here, length, channels = pair_rep.shape
    head_count = row_bias_proj.shape[1]
    head_size = channels // head_count
    row_index = lax.axis_index("row")
    col_index = lax.axis_index("col")
    device_index = row_index * n_col + col_index
    block_rows = length // n_row
    block_cols = length // n_col
    local_lines = device_index * rows_here + jnp.arange(rows_here, dtype=jnp.int32)
    local_cols = col_index * block_cols + row_index * rows_here + jnp.arange(rows_here, dtype=jnp.int32)
    normed = layer_norm(pair_rep).astype(jnp.bfloat16)
    flat_rows = normed.reshape(rows_here * length, channels)
    bias_rows = jnp.dot(flat_rows, row_bias_proj, preferred_element_type=jnp.float32)
    bias_rows = bias_rows.reshape(rows_here, length, head_count).transpose(2, 0, 1)
    bias_all = gather_lines(bias_rows)
    projected = jnp.dot(flat_rows, row_project, preferred_element_type=jnp.float32).reshape(
        rows_here, length, 4 * channels
    )
    qkv_rows = (
        projected[..., : 3 * channels]
        .astype(jnp.bfloat16)
        .reshape(rows_here, length, 3, head_count, head_size)
    )
    key_ok = tile_rows(local_lines, tile_mask, length)
    mixed_rows = attend_lines(
        qkv_rows[:, :, 0],
        qkv_rows[:, :, 1],
        qkv_rows[:, :, 2],
        projected[..., 3 * channels :],
        bias_all,
        key_ok,
        chain_ids,
        chain_bias[0],
        0,
        False,
    )
    update = jnp.dot(
        mixed_rows.reshape(-1, channels), row_output, preferred_element_type=jnp.float32
    ).reshape(rows_here, length, channels)
    first_pair = (pair_rep.astype(jnp.float32) + update).astype(jnp.bfloat16)
    normed_first = layer_norm(first_pair).astype(jnp.bfloat16)
    bias_next = jnp.dot(
        normed_first.reshape(-1, channels), col_bias_proj, preferred_element_type=jnp.float32
    )
    bias_next = bias_next.reshape(rows_here, length, head_count).transpose(2, 0, 1)
    lanes = 128
    pair_chunks = (
        first_pair.reshape(rows_here, n_col, n_row, rows_here, channels)
        .transpose(2, 1, 0, 3, 4)
        .reshape(device_count, rows_here * rows_here * channels // lanes, lanes)
    )
    bias_high = bias_next.astype(jnp.bfloat16)
    bias_low = (bias_next - bias_high.astype(jnp.float32)).astype(jnp.bfloat16)
    bias_words = jnp.stack([bias_high, bias_low], axis=0).reshape(1, -1, lanes)
    bias_chunks = jnp.broadcast_to(bias_words, (device_count,) + bias_words.shape[1:])
    merged = lax.all_to_all(
        jnp.concatenate([pair_chunks, bias_chunks], axis=1), ("row", "col"), 0, 0, tiled=True
    )
    pair_rows = pair_chunks.shape[1]
    columns = (
        merged[:, :pair_rows]
        .reshape(device_count, rows_here, rows_here, channels)
        .transpose(2, 0, 1, 3)
        .reshape(rows_here, length, channels)
    )
    bias_got = (
        merged[:, pair_rows:]
        .reshape(device_count, 2, head_count, rows_here, length)
        .astype(jnp.float32)
    )
    bias_cols = (
        (bias_got[:, 0] + bias_got[:, 1])
        .transpose(1, 0, 2, 3)
        .reshape(head_count, length, length)
    )
    normed_cols = layer_norm(columns).astype(jnp.bfloat16)
    projected_cols = jnp.dot(
        normed_cols.reshape(-1, channels), col_project, preferred_element_type=jnp.float32
    ).reshape(rows_here, length, 4 * channels)
    qkv_cols = (
        projected_cols[..., : 3 * channels]
        .astype(jnp.bfloat16)
        .reshape(rows_here, length, 3, head_count, head_size)
    )
    col_ok = tile_rows(local_cols, tile_mask.T, length)
    mixed_cols = attend_lines(
        qkv_cols[:, :, 0],
        qkv_cols[:, :, 1],
        qkv_cols[:, :, 2],
        projected_cols[..., 3 * channels :],
        bias_cols,
        col_ok,
        chain_ids,
        chain_bias[1],
        0,
        True,
    )
    update_cols = jnp.dot(
        mixed_cols.reshape(-1, channels), col_output, preferred_element_type=jnp.float32
    ).reshape(rows_here, length, channels)
    second_pair = (columns.astype(jnp.float32) + update_cols).astype(jnp.bfloat16)
    normed_second = layer_norm(second_pair).astype(jnp.bfloat16)
    edge_mask = tile_pairs(local_cols, jnp.arange(length, dtype=jnp.int32), tile_mask.T, length)
    left_all = tri_acts(normed_second, tri_left, edge_mask)
    right_all = tri_acts(normed_second, tri_right, edge_mask)
    raw_chunks = second_pair.reshape(rows_here, n_row, block_rows, channels).transpose(1, 2, 0, 3)
    raw_pieces = [lax.dynamic_index_in_dim(raw_chunks, row_index, 0, keepdims=False)]
    for shift in range(1, n_row):
        piece = lax.dynamic_index_in_dim(raw_chunks, (row_index + shift) % n_row, 0, keepdims=False)
        raw_pieces.append(
            lax.ppermute(piece, "row", perm=[(r, (r + shift) % n_row) for r in range(n_row)])
        )
    sources = (row_index - jnp.arange(n_row, dtype=jnp.int32)) % n_row
    raw_got = jnp.take(jnp.stack(raw_pieces, axis=0), sources, axis=0)
    own_pair = raw_got.transpose(1, 0, 2, 3).reshape(block_rows, block_cols, channels)
    channels_here = channels // device_count
    edges = jnp.stack([left_all, right_all], axis=0).transpose(3, 0, 1, 2)
    edges_got = lax.all_to_all(edges, ("row", "col"), 0, 2, tiled=True)
    product_part = jnp.einsum(
        "cki,ckj->cij",
        edges_got[:, 0],
        edges_got[:, 1],
        preferred_element_type=jnp.float32,
    )
    product_sent = (
        product_part.reshape(channels_here, n_row, block_rows, n_col, block_cols)
        .transpose(1, 3, 0, 2, 4)
        .reshape(device_count, channels_here, block_rows, block_cols)
    )
    product_got = lax.all_to_all(
        product_sent.reshape(device_count, -1, lanes), ("row", "col"), 0, 0, tiled=True
    )
    product_sum = product_got.reshape(channels, block_rows, block_cols).transpose(1, 2, 0)
    normed_own = layer_norm(own_pair).astype(jnp.bfloat16)
    gate_values = jax.nn.sigmoid(
        jnp.dot(normed_own.reshape(-1, channels), tri_gate, preferred_element_type=jnp.float32)
    ).reshape(block_rows, block_cols, channels)
    centered = layer_norm(product_sum).astype(jnp.bfloat16)
    update_tri = jnp.dot(
        centered.reshape(-1, channels), tri_output, preferred_element_type=jnp.float32
    ).reshape(block_rows, block_cols, channels)
    return (own_pair.astype(jnp.float32) + gate_values * update_tri).astype(jnp.bfloat16)


def solution(mesh):
    return jax.shard_map(
        shards,
        mesh=mesh,
        in_specs=(
            P(("row", "col"), None, None),
            P(),
            P(),
            P(),
            P(),
            P(),
            P(),
            P(),
            P(),
            P(),
            P(),
            P(),
            P(),
            P(),
        ),
        out_specs=P("row", "col", None),
        check_vma=False,
    )
```

```python
import jax
import jax.numpy as jnp
from jax import lax
from jax.sharding import PartitionSpec as P


def layer_norm(values):
    values = values.astype(jnp.float32)
    center = values - jnp.mean(values, axis=-1, keepdims=True)
    spread = jnp.mean(center * center, axis=-1, keepdims=True)
    return center * lax.rsqrt(spread + 1e-05)


def tile_rows(positions, tile_table, length):
    tile_count = tile_table.shape[0]
    tile_width = length // tile_count
    onehot = (positions[:, None] // tile_width == jnp.arange(tile_count)[None, :]).astype(
        jnp.float32
    )
    picked = jnp.dot(onehot, tile_table.astype(jnp.float32))
    spread_out = jnp.broadcast_to(picked[:, :, None], (positions.shape[0], tile_count, tile_width))
    return spread_out.reshape(positions.shape[0], length) > 0.5


def tile_pairs(row_pos, col_pos, tile_table, length):
    tile_count = tile_table.shape[0]
    tile_width = length // tile_count
    row_hot = (row_pos[:, None] // tile_width == jnp.arange(tile_count)[None, :]).astype(
        jnp.float32
    )
    col_hot = (col_pos[:, None] // tile_width == jnp.arange(tile_count)[None, :]).astype(
        jnp.float32
    )
    return jnp.dot(jnp.dot(row_hot, tile_table.astype(jnp.float32)), col_hot.T)


def attend_lines(
    queries,
    key_rows,
    value_rows,
    gate_pre,
    bias_all,
    key_ok,
    chain_ids,
    chain_add,
    line_dim,
    flipped,
):
    length = queries.shape[1 - line_dim]
    head_count = queries.shape[2]
    head_size = queries.shape[3]
    width_all = head_count * head_size
    query_rows = min(128, length)
    blocks = length // query_rows
    scaling = head_size ** (-0.5)
    spec_q = "lqhd" if line_dim == 0 else "qlhd"
    spec_k = "lkhd" if line_dim == 0 else "klhd"
    usable = key_ok[:, None, None, :]
    if flipped:
        bias_all = bias_all.transpose(0, 2, 1)
    same_all = (chain_ids[:, None] == chain_ids[None, :]).astype(jnp.float32)
    bias_all = bias_all + chain_add[:, None, None] * same_all[None]

    def one_block(offset):
        query_block = lax.dynamic_slice_in_dim(queries, offset, query_rows, 1 - line_dim)
        scores = (
            jnp.einsum(
                f"{spec_q},{spec_k}->lhqk",
                query_block,
                key_rows,
                preferred_element_type=jnp.float32,
            )
            * scaling
        )
        bias_block = lax.dynamic_slice_in_dim(bias_all, offset, query_rows, 1)
        scores = scores + bias_block[None]
        scores = jnp.where(usable, scores, -1000000000.0)
        row_peak = jnp.max(scores, axis=-1, keepdims=True)
        weights = jnp.exp(scores - row_peak)
        attention = (weights / jnp.sum(weights, axis=-1, keepdims=True)).astype(jnp.bfloat16)
        mixed_rows = jnp.einsum(
            f"lhqk,{spec_k}->{spec_q}", attention, value_rows, preferred_element_type=jnp.float32
        )
        mixed_rows = mixed_rows.reshape(mixed_rows.shape[:2] + (width_all,))
        gate_block = lax.dynamic_slice_in_dim(gate_pre, offset, query_rows, 1 - line_dim)
        return (mixed_rows * jax.nn.sigmoid(gate_block)).astype(jnp.bfloat16)

    if blocks == 1:
        return one_block(0)
    outputs = lax.map(one_block, jnp.arange(blocks, dtype=jnp.int32) * query_rows)
    if line_dim == 0:
        outputs = outputs.transpose(1, 0, 2, 3)
    return outputs.reshape(gate_pre.shape[:2] + (width_all,))


def tri_acts(normed, weights, allowed):
    channels = normed.shape[-1]
    projected = jnp.dot(normed.reshape(-1, channels), weights, preferred_element_type=jnp.float32)
    projected = projected.reshape(normed.shape[0], normed.shape[1], 2 * channels)
    return (
        jax.nn.sigmoid(projected[..., channels:]) * projected[..., :channels] * allowed[..., None]
    ).astype(jnp.bfloat16)


def gather_lines(piece):
    device_count = lax.axis_size("row") * lax.axis_size("col")
    sent = jnp.broadcast_to(piece[None], (device_count,) + piece.shape)
    got = lax.all_to_all(sent, ("row", "col"), 0, 0, tiled=True)
    heads, rows_here, length = piece.shape
    return got.transpose(1, 0, 2, 3).reshape(heads, device_count * rows_here, length)


def shards(
    pair_rep,
    tile_mask,
    chain_ids,
    chain_bias,
    row_project,
    row_bias_proj,
    row_output,
    col_project,
    col_bias_proj,
    col_output,
    tri_left,
    tri_right,
    tri_gate,
    tri_output,
):
    n_row = lax.axis_size("row")
    n_col = lax.axis_size("col")
    device_count = n_row * n_col
    rows_here, length, channels = pair_rep.shape
    head_count = row_bias_proj.shape[1]
    head_size = channels // head_count
    row_index = lax.axis_index("row")
    col_index = lax.axis_index("col")
    device_index = row_index * n_col + col_index
    block_rows = length // n_row
    block_cols = length // n_col
    local_lines = device_index * rows_here + jnp.arange(rows_here, dtype=jnp.int32)
    local_cols = col_index * block_cols + row_index * rows_here + jnp.arange(rows_here, dtype=jnp.int32)
    normed = layer_norm(pair_rep).astype(jnp.bfloat16)
    flat_rows = normed.reshape(rows_here * length, channels)
    bias_rows = jnp.dot(flat_rows, row_bias_proj, preferred_element_type=jnp.float32)
    bias_rows = bias_rows.reshape(rows_here, length, head_count).transpose(2, 0, 1)
    bias_all = gather_lines(bias_rows)
    projected = jnp.dot(flat_rows, row_project, preferred_element_type=jnp.float32).reshape(
        rows_here, length, 4 * channels
    )
    qkv_rows = (
        projected[..., : 3 * channels]
        .astype(jnp.bfloat16)
        .reshape(rows_here, length, 3, head_count, head_size)
    )
    key_ok = tile_rows(local_lines, tile_mask, length)
    mixed_rows = attend_lines(
        qkv_rows[:, :, 0],
        qkv_rows[:, :, 1],
        qkv_rows[:, :, 2],
        projected[..., 3 * channels :],
        bias_all,
        key_ok,
        chain_ids,
        chain_bias[0],
        0,
        False,
    )
    update = jnp.dot(
        mixed_rows.reshape(-1, channels), row_output, preferred_element_type=jnp.float32
    ).reshape(rows_here, length, channels)
    first_pair = (pair_rep.astype(jnp.float32) + update).astype(jnp.bfloat16)
    normed_first = layer_norm(first_pair).astype(jnp.bfloat16)
    bias_next = jnp.dot(
        normed_first.reshape(-1, channels), col_bias_proj, preferred_element_type=jnp.float32
    )
    bias_next = bias_next.reshape(rows_here, length, head_count).transpose(2, 0, 1)
    lanes = 128
    pair_chunks = (
        first_pair.reshape(rows_here, n_col, n_row, rows_here, channels)
        .transpose(2, 1, 0, 3, 4)
        .reshape(device_count, rows_here * rows_here * channels // lanes, lanes)
    )
    bias_high = bias_next.astype(jnp.bfloat16)
    bias_low = (bias_next - bias_high.astype(jnp.float32)).astype(jnp.bfloat16)
    bias_words = jnp.stack([bias_high, bias_low], axis=0).reshape(1, -1, lanes)
    bias_chunks = jnp.broadcast_to(bias_words, (device_count,) + bias_words.shape[1:])
    merged = lax.all_to_all(
        jnp.concatenate([pair_chunks, bias_chunks], axis=1), ("row", "col"), 0, 0, tiled=True
    )
    pair_rows = pair_chunks.shape[1]
    columns = (
        merged[:, :pair_rows]
        .reshape(device_count, rows_here, rows_here, channels)
        .transpose(2, 0, 1, 3)
        .reshape(rows_here, length, channels)
    )
    bias_got = (
        merged[:, pair_rows:]
        .reshape(device_count, 2, head_count, rows_here, length)
        .astype(jnp.float32)
    )
    bias_cols = (
        (bias_got[:, 0] + bias_got[:, 1])
        .transpose(1, 0, 2, 3)
        .reshape(head_count, length, length)
    )
    normed_cols = layer_norm(columns).astype(jnp.bfloat16)
    projected_cols = jnp.dot(
        normed_cols.reshape(-1, channels), col_project, preferred_element_type=jnp.float32
    ).reshape(rows_here, length, 4 * channels)
    qkv_cols = (
        projected_cols[..., : 3 * channels]
        .astype(jnp.bfloat16)
        .reshape(rows_here, length, 3, head_count, head_size)
    )
    col_ok = tile_rows(local_cols, tile_mask.T, length)
    mixed_cols = attend_lines(
        qkv_cols[:, :, 0],
        qkv_cols[:, :, 1],
        qkv_cols[:, :, 2],
        projected_cols[..., 3 * channels :],
        bias_cols,
        col_ok,
        chain_ids,
        chain_bias[1],
        0,
        True,
    )
    update_cols = jnp.dot(
        mixed_cols.reshape(-1, channels), col_output, preferred_element_type=jnp.float32
    ).reshape(rows_here, length, channels)
    second_pair = (columns.astype(jnp.float32) + update_cols).astype(jnp.bfloat16)
    normed_second = layer_norm(second_pair).astype(jnp.bfloat16)
    edge_mask = tile_pairs(local_cols, jnp.arange(length, dtype=jnp.int32), tile_mask.T, length)
    both = jnp.dot(
        normed_second.reshape(-1, channels),
        jnp.concatenate([tri_left, tri_right], axis=1),
        preferred_element_type=jnp.float32,
    ).reshape(normed_second.shape[:2] + (4 * channels,))
    left_all, right_all = (
        (
            jax.nn.sigmoid(half[..., channels:]) * half[..., :channels] * edge_mask[..., None]
        ).astype(jnp.bfloat16)
        for half in (both[..., : 2 * channels], both[..., 2 * channels :])
    )
    raw_chunks = second_pair.reshape(rows_here, n_row, block_rows, channels).transpose(1, 2, 0, 3)
    raw_pieces = [lax.dynamic_index_in_dim(raw_chunks, row_index, 0, keepdims=False)]
    for shift in range(1, n_row):
        piece = lax.dynamic_index_in_dim(raw_chunks, (row_index + shift) % n_row, 0, keepdims=False)
        raw_pieces.append(
            lax.ppermute(piece, "row", perm=[(r, (r + shift) % n_row) for r in range(n_row)])
        )
    sources = (row_index - jnp.arange(n_row, dtype=jnp.int32)) % n_row
    raw_got = jnp.take(jnp.stack(raw_pieces, axis=0), sources, axis=0)
    own_pair = raw_got.transpose(1, 0, 2, 3).reshape(block_rows, block_cols, channels)
    channels_here = channels // device_count
    edges = jnp.stack([left_all, right_all], axis=0).transpose(3, 0, 1, 2)
    edges_got = lax.all_to_all(edges, ("row", "col"), 0, 2, tiled=True)
    product_part = jnp.einsum(
        "cki,ckj->cij",
        edges_got[:, 0],
        edges_got[:, 1],
        preferred_element_type=jnp.float32,
    )
    product_sent = (
        product_part.reshape(channels_here, n_row, block_rows, n_col, block_cols)
        .transpose(1, 3, 0, 2, 4)
        .reshape(device_count, channels_here, block_rows, block_cols)
    )
    product_got = lax.all_to_all(
        product_sent.reshape(device_count, -1, lanes), ("row", "col"), 0, 0, tiled=True
    )
    product_sum = product_got.reshape(channels, block_rows, block_cols).transpose(1, 2, 0)
    normed_own = layer_norm(own_pair).astype(jnp.bfloat16)
    gate_values = jax.nn.sigmoid(
        jnp.dot(normed_own.reshape(-1, channels), tri_gate, preferred_element_type=jnp.float32)
    ).reshape(block_rows, block_cols, channels)
    centered = layer_norm(product_sum).astype(jnp.bfloat16)
    update_tri = jnp.dot(
        centered.reshape(-1, channels), tri_output, preferred_element_type=jnp.float32
    ).reshape(block_rows, block_cols, channels)
    return (own_pair.astype(jnp.float32) + gate_values * update_tri).astype(jnp.bfloat16)


def solution(mesh):
    return jax.shard_map(
        shards,
        mesh=mesh,
        in_specs=(
            P(("row", "col"), None, None),
            P(),
            P(),
            P(),
            P(),
            P(),
            P(),
            P(),
            P(),
            P(),
            P(),
            P(),
            P(),
            P(),
        ),
        out_specs=P("row", "col", None),
        check_vma=False,
    )
```

```python
import jax
import jax.numpy as jnp
from jax import lax
from jax.sharding import PartitionSpec as P


def layer_norm(values):
    values = values.astype(jnp.float32)
    center = values - jnp.mean(values, axis=-1, keepdims=True)
    spread = jnp.mean(center * center, axis=-1, keepdims=True)
    return center * lax.rsqrt(spread + 1e-05)


def tile_rows(positions, tile_table, length):
    tile_count = tile_table.shape[0]
    tile_width = length // tile_count
    onehot = (positions[:, None] // tile_width == jnp.arange(tile_count)[None, :]).astype(
        jnp.float32
    )
    picked = jnp.dot(onehot, tile_table.astype(jnp.float32))
    spread_out = jnp.broadcast_to(picked[:, :, None], (positions.shape[0], tile_count, tile_width))
    return spread_out.reshape(positions.shape[0], length) > 0.5


def tile_pairs(row_pos, col_pos, tile_table, length):
    tile_count = tile_table.shape[0]
    tile_width = length // tile_count
    row_hot = (row_pos[:, None] // tile_width == jnp.arange(tile_count)[None, :]).astype(
        jnp.float32
    )
    col_hot = (col_pos[:, None] // tile_width == jnp.arange(tile_count)[None, :]).astype(
        jnp.float32
    )
    return jnp.dot(jnp.dot(row_hot, tile_table.astype(jnp.float32)), col_hot.T)


def attend_lines(
    queries,
    key_rows,
    value_rows,
    gate_pre,
    bias_all,
    key_ok,
    chain_ids,
    chain_add,
    line_dim,
    flipped,
):
    length = queries.shape[1 - line_dim]
    head_count = queries.shape[2]
    head_size = queries.shape[3]
    width_all = head_count * head_size
    query_rows = min(128, length)
    blocks = length // query_rows
    scaling = head_size ** (-0.5)
    spec_q = "lqhd" if line_dim == 0 else "qlhd"
    spec_k = "lkhd" if line_dim == 0 else "klhd"
    usable = key_ok[:, None, None, :]
    if flipped:
        bias_all = bias_all.transpose(0, 2, 1)
    same_all = (chain_ids[:, None] == chain_ids[None, :]).astype(jnp.float32)
    bias_all = bias_all + chain_add[:, None, None] * same_all[None]

    def one_block(offset):
        query_block = lax.dynamic_slice_in_dim(queries, offset, query_rows, 1 - line_dim)
        scores = (
            jnp.einsum(
                f"{spec_q},{spec_k}->lhqk",
                query_block,
                key_rows,
                preferred_element_type=jnp.float32,
            )
            * scaling
        )
        bias_block = lax.dynamic_slice_in_dim(bias_all, offset, query_rows, 1)
        scores = scores + bias_block[None]
        scores = jnp.where(usable, scores, -1000000000.0)
        row_peak = jnp.max(scores, axis=-1, keepdims=True)
        weights = jnp.exp(scores - row_peak)
        attention = (weights / jnp.sum(weights, axis=-1, keepdims=True)).astype(jnp.bfloat16)
        mixed_rows = jnp.einsum(
            f"lhqk,{spec_k}->{spec_q}", attention, value_rows, preferred_element_type=jnp.float32
        )
        mixed_rows = mixed_rows.reshape(mixed_rows.shape[:2] + (width_all,))
        gate_block = lax.dynamic_slice_in_dim(gate_pre, offset, query_rows, 1 - line_dim)
        return (mixed_rows * jax.nn.sigmoid(gate_block)).astype(jnp.bfloat16)

    if blocks == 1:
        return one_block(0)
    outputs = lax.map(one_block, jnp.arange(blocks, dtype=jnp.int32) * query_rows)
    if line_dim == 0:
        outputs = outputs.transpose(1, 0, 2, 3)
    return outputs.reshape(gate_pre.shape[:2] + (width_all,))


def tri_acts(normed, weights, allowed):
    channels = normed.shape[-1]
    projected = jnp.dot(normed.reshape(-1, channels), weights, preferred_element_type=jnp.float32)
    projected = projected.reshape(normed.shape[0], normed.shape[1], 2 * channels)
    return (
        jax.nn.sigmoid(projected[..., channels:]) * projected[..., :channels] * allowed[..., None]
    ).astype(jnp.bfloat16)


def gather_lines(piece):
    device_count = lax.axis_size("row") * lax.axis_size("col")
    sent = jnp.broadcast_to(piece[None], (device_count,) + piece.shape)
    got = lax.all_to_all(sent, ("row", "col"), 0, 0, tiled=True)
    heads, rows_here, length = piece.shape
    return got.transpose(1, 0, 2, 3).reshape(heads, device_count * rows_here, length)


def shards(
    pair_rep,
    tile_mask,
    chain_ids,
    chain_bias,
    row_project,
    row_bias_proj,
    row_output,
    col_project,
    col_bias_proj,
    col_output,
    tri_left,
    tri_right,
    tri_gate,
    tri_output,
):
    n_row = lax.axis_size("row")
    n_col = lax.axis_size("col")
    device_count = n_row * n_col
    rows_here, length, channels = pair_rep.shape
    head_count = row_bias_proj.shape[1]
    head_size = channels // head_count
    row_index = lax.axis_index("row")
    col_index = lax.axis_index("col")
    device_index = row_index * n_col + col_index
    block_rows = length // n_row
    block_cols = length // n_col
    local_lines = device_index * rows_here + jnp.arange(rows_here, dtype=jnp.int32)
    local_cols = col_index * block_cols + row_index * rows_here + jnp.arange(rows_here, dtype=jnp.int32)
    normed = layer_norm(pair_rep).astype(jnp.bfloat16)
    flat_rows = normed.reshape(rows_here * length, channels)
    bias_rows = jnp.dot(flat_rows, row_bias_proj, preferred_element_type=jnp.float32)
    bias_rows = bias_rows.reshape(rows_here, length, head_count).transpose(2, 0, 1)
    bias_all = gather_lines(bias_rows)
    projected = jnp.dot(flat_rows, row_project, preferred_element_type=jnp.float32).reshape(
        rows_here, length, 4 * channels
    )
    qkv_rows = (
        projected[..., : 3 * channels]
        .astype(jnp.bfloat16)
        .reshape(rows_here, length, 3, head_count, head_size)
    )
    key_ok = tile_rows(local_lines, tile_mask, length)
    mixed_rows = attend_lines(
        qkv_rows[:, :, 0],
        qkv_rows[:, :, 1],
        qkv_rows[:, :, 2],
        projected[..., 3 * channels :],
        bias_all,
        key_ok,
        chain_ids,
        chain_bias[0],
        0,
        False,
    )
    update = jnp.dot(
        mixed_rows.reshape(-1, channels), row_output, preferred_element_type=jnp.float32
    ).reshape(rows_here, length, channels)
    first_pair = (pair_rep.astype(jnp.float32) + update).astype(jnp.bfloat16)
    normed_first = layer_norm(first_pair).astype(jnp.bfloat16)
    bias_next = jnp.dot(
        normed_first.reshape(-1, channels), col_bias_proj, preferred_element_type=jnp.float32
    )
    bias_next = bias_next.reshape(rows_here, length, head_count).transpose(2, 0, 1)
    lanes = 128
    pair_chunks = (
        first_pair.reshape(rows_here, n_col, n_row, rows_here, channels)
        .transpose(2, 1, 0, 3, 4)
        .reshape(device_count, rows_here * rows_here * channels // lanes, lanes)
    )
    bias_high = bias_next.astype(jnp.bfloat16)
    bias_low = (bias_next - bias_high.astype(jnp.float32)).astype(jnp.bfloat16)
    bias_words = jnp.stack([bias_high, bias_low], axis=0).reshape(1, -1, lanes)
    bias_chunks = jnp.broadcast_to(bias_words, (device_count,) + bias_words.shape[1:])
    merged = lax.all_to_all(
        jnp.concatenate([pair_chunks, bias_chunks], axis=1), ("row", "col"), 0, 0, tiled=True
    )
    pair_rows = pair_chunks.shape[1]
    columns = (
        merged[:, :pair_rows]
        .reshape(device_count, rows_here, rows_here, channels)
        .transpose(2, 0, 1, 3)
        .reshape(rows_here, length, channels)
    )
    bias_got = (
        merged[:, pair_rows:]
        .reshape(device_count, 2, head_count, rows_here, length)
        .astype(jnp.float32)
    )
    bias_cols = (
        (bias_got[:, 0] + bias_got[:, 1])
        .transpose(1, 0, 2, 3)
        .reshape(head_count, length, length)
    )
    normed_cols = layer_norm(columns).astype(jnp.bfloat16)
    projected_cols = jnp.dot(
        normed_cols.reshape(-1, channels), col_project, preferred_element_type=jnp.float32
    ).reshape(rows_here, length, 4 * channels)
    qkv_cols = (
        projected_cols[..., : 3 * channels]
        .astype(jnp.bfloat16)
        .reshape(rows_here, length, 3, head_count, head_size)
    )
    col_ok = tile_rows(local_cols, tile_mask.T, length)
    mixed_cols = attend_lines(
        qkv_cols[:, :, 0],
        qkv_cols[:, :, 1],
        qkv_cols[:, :, 2],
        projected_cols[..., 3 * channels :],
        bias_cols,
        col_ok,
        chain_ids,
        chain_bias[1],
        0,
        True,
    )
    update_cols = jnp.dot(
        mixed_cols.reshape(-1, channels), col_output, preferred_element_type=jnp.float32
    ).reshape(rows_here, length, channels)
    second_pair = (columns.astype(jnp.float32) + update_cols).astype(jnp.bfloat16)
    normed_second = layer_norm(second_pair).astype(jnp.bfloat16)
    edge_mask = tile_pairs(local_cols, jnp.arange(length, dtype=jnp.int32), tile_mask.T, length)
    both = jnp.dot(
        normed_second.reshape(-1, channels),
        jnp.concatenate([tri_left, tri_right], axis=1),
        preferred_element_type=jnp.float32,
    ).reshape(normed_second.shape[:2] + (4 * channels,))
    left_all, right_all = (
        (
            jax.nn.sigmoid(half[..., channels:]) * half[..., :channels] * edge_mask[..., None]
        ).astype(jnp.bfloat16)
        for half in (both[..., : 2 * channels], both[..., 2 * channels :])
    )
    channels_here = channels // device_count
    edges = jnp.stack([left_all, right_all], axis=0).transpose(3, 0, 1, 2)
    edges_got = lax.all_to_all(edges, ("row", "col"), 0, 2, tiled=True)
    product_part = jnp.einsum(
        "cki,ckj->cij",
        edges_got[:, 0],
        edges_got[:, 1],
        preferred_element_type=jnp.float32,
    )
    product_sent = (
        product_part.reshape(channels_here, n_row, block_rows, n_col, block_cols)
        .transpose(1, 3, 0, 2, 4)
        .reshape(device_count, channels_here, block_rows, block_cols)
    )
    product_sent, second_pair = lax.optimization_barrier((product_sent, second_pair))
    raw_chunks = second_pair.reshape(rows_here, n_row, block_rows, channels).transpose(1, 2, 0, 3)
    raw_pieces = [lax.dynamic_index_in_dim(raw_chunks, row_index, 0, keepdims=False)]
    for shift in range(1, n_row):
        piece = lax.dynamic_index_in_dim(raw_chunks, (row_index + shift) % n_row, 0, keepdims=False)
        raw_pieces.append(
            lax.ppermute(piece, "row", perm=[(r, (r + shift) % n_row) for r in range(n_row)])
        )
    sources = (row_index - jnp.arange(n_row, dtype=jnp.int32)) % n_row
    raw_got = jnp.take(jnp.stack(raw_pieces, axis=0), sources, axis=0)
    own_pair = raw_got.transpose(1, 0, 2, 3).reshape(block_rows, block_cols, channels)
    product_got = lax.all_to_all(
        product_sent.reshape(device_count, -1, lanes), ("row", "col"), 0, 0, tiled=True
    )
    product_sum = product_got.reshape(channels, block_rows, block_cols).transpose(1, 2, 0)
    normed_own = layer_norm(own_pair).astype(jnp.bfloat16)
    gate_values = jax.nn.sigmoid(
        jnp.dot(normed_own.reshape(-1, channels), tri_gate, preferred_element_type=jnp.float32)
    ).reshape(block_rows, block_cols, channels)
    centered = layer_norm(product_sum).astype(jnp.bfloat16)
    update_tri = jnp.dot(
        centered.reshape(-1, channels), tri_output, preferred_element_type=jnp.float32
    ).reshape(block_rows, block_cols, channels)
    return (own_pair.astype(jnp.float32) + gate_values * update_tri).astype(jnp.bfloat16)


def solution(mesh):
    return jax.shard_map(
        shards,
        mesh=mesh,
        in_specs=(
            P(("row", "col"), None, None),
            P(),
            P(),
            P(),
            P(),
            P(),
            P(),
            P(),
            P(),
            P(),
            P(),
            P(),
            P(),
            P(),
        ),
        out_specs=P("row", "col", None),
        check_vma=False,
    )
```

```python
import jax
import jax.numpy as jnp
from jax import lax
from jax.sharding import PartitionSpec as P


def layer_norm(values):
    values = values.astype(jnp.float32)
    center = values - jnp.mean(values, axis=-1, keepdims=True)
    spread = jnp.mean(center * center, axis=-1, keepdims=True)
    return center * lax.rsqrt(spread + 1e-05)


def tile_rows(positions, tile_table, length):
    tile_count = tile_table.shape[0]
    tile_width = length // tile_count
    onehot = (positions[:, None] // tile_width == jnp.arange(tile_count)[None, :]).astype(
        jnp.float32
    )
    picked = jnp.dot(onehot, tile_table.astype(jnp.float32))
    spread_out = jnp.broadcast_to(picked[:, :, None], (positions.shape[0], tile_count, tile_width))
    return spread_out.reshape(positions.shape[0], length) > 0.5


def tile_pairs(row_pos, col_pos, tile_table, length):
    tile_count = tile_table.shape[0]
    tile_width = length // tile_count
    row_hot = (row_pos[:, None] // tile_width == jnp.arange(tile_count)[None, :]).astype(
        jnp.float32
    )
    col_hot = (col_pos[:, None] // tile_width == jnp.arange(tile_count)[None, :]).astype(
        jnp.float32
    )
    return jnp.dot(jnp.dot(row_hot, tile_table.astype(jnp.float32)), col_hot.T)


def attend_lines(
    queries,
    key_rows,
    value_rows,
    gate_pre,
    bias_all,
    key_ok,
    chain_ids,
    chain_add,
    line_dim,
    flipped,
):
    length = queries.shape[1 - line_dim]
    head_count = queries.shape[2]
    head_size = queries.shape[3]
    width_all = head_count * head_size
    query_rows = min(128, length)
    blocks = length // query_rows
    scaling = head_size ** (-0.5)
    spec_q = "lqhd" if line_dim == 0 else "qlhd"
    spec_k = "lkhd" if line_dim == 0 else "klhd"
    usable = key_ok[:, None, None, :]
    if flipped:
        bias_all = bias_all.transpose(0, 2, 1)
    same_all = (chain_ids[:, None] == chain_ids[None, :]).astype(jnp.float32)
    bias_all = bias_all + chain_add[:, None, None] * same_all[None]

    def one_block(offset):
        query_block = lax.dynamic_slice_in_dim(queries, offset, query_rows, 1 - line_dim)
        scores = (
            jnp.einsum(
                f"{spec_q},{spec_k}->lhqk",
                query_block,
                key_rows,
                preferred_element_type=jnp.float32,
            )
            * scaling
        )
        bias_block = lax.dynamic_slice_in_dim(bias_all, offset, query_rows, 1)
        scores = scores + bias_block[None]
        scores = jnp.where(usable, scores, -1000000000.0)
        row_peak = jnp.max(scores, axis=-1, keepdims=True)
        weights = jnp.exp(scores - row_peak)
        attention = (weights / jnp.sum(weights, axis=-1, keepdims=True)).astype(jnp.bfloat16)
        mixed_rows = jnp.einsum(
            f"lhqk,{spec_k}->{spec_q}", attention, value_rows, preferred_element_type=jnp.float32
        )
        mixed_rows = mixed_rows.reshape(mixed_rows.shape[:2] + (width_all,))
        gate_block = lax.dynamic_slice_in_dim(gate_pre, offset, query_rows, 1 - line_dim)
        return (mixed_rows * jax.nn.sigmoid(gate_block)).astype(jnp.bfloat16)

    if blocks == 1:
        return one_block(0)
    outputs = lax.map(one_block, jnp.arange(blocks, dtype=jnp.int32) * query_rows)
    if line_dim == 0:
        outputs = outputs.transpose(1, 0, 2, 3)
    return outputs.reshape(gate_pre.shape[:2] + (width_all,))


def tri_acts(normed, weights, allowed):
    channels = normed.shape[-1]
    projected = jnp.dot(normed.reshape(-1, channels), weights, preferred_element_type=jnp.float32)
    projected = projected.reshape(normed.shape[0], normed.shape[1], 2 * channels)
    return (
        jax.nn.sigmoid(projected[..., channels:]) * projected[..., :channels] * allowed[..., None]
    ).astype(jnp.bfloat16)


def gather_lines(piece):
    device_count = lax.axis_size("row") * lax.axis_size("col")
    sent = jnp.broadcast_to(piece[None], (device_count,) + piece.shape)
    got = lax.all_to_all(sent, ("row", "col"), 0, 0, tiled=True)
    heads, rows_here, length = piece.shape
    return got.transpose(1, 0, 2, 3).reshape(heads, device_count * rows_here, length)


def shards(
    pair_rep,
    tile_mask,
    chain_ids,
    chain_bias,
    row_project,
    row_bias_proj,
    row_output,
    col_project,
    col_bias_proj,
    col_output,
    tri_left,
    tri_right,
    tri_gate,
    tri_output,
):
    n_row = lax.axis_size("row")
    n_col = lax.axis_size("col")
    device_count = n_row * n_col
    rows_here, length, channels = pair_rep.shape
    head_count = row_bias_proj.shape[1]
    head_size = channels // head_count
    row_index = lax.axis_index("row")
    col_index = lax.axis_index("col")
    device_index = row_index * n_col + col_index
    block_rows = length // n_row
    block_cols = length // n_col
    local_lines = device_index * rows_here + jnp.arange(rows_here, dtype=jnp.int32)
    local_cols = col_index * block_cols + row_index * rows_here + jnp.arange(rows_here, dtype=jnp.int32)
    normed = layer_norm(pair_rep).astype(jnp.bfloat16)
    flat_rows = normed.reshape(rows_here * length, channels)
    bias_rows = jnp.dot(flat_rows, row_bias_proj, preferred_element_type=jnp.float32)
    bias_rows = bias_rows.reshape(rows_here, length, head_count).transpose(2, 0, 1)
    bias_all = gather_lines(bias_rows)
    projected = jnp.dot(flat_rows, row_project, preferred_element_type=jnp.float32).reshape(
        rows_here, length, 4 * channels
    )
    qkv_rows = (
        projected[..., : 3 * channels]
        .astype(jnp.bfloat16)
        .reshape(rows_here, length, 3, head_count, head_size)
    )
    key_ok = tile_rows(local_lines, tile_mask, length)
    mixed_rows = attend_lines(
        qkv_rows[:, :, 0],
        qkv_rows[:, :, 1],
        qkv_rows[:, :, 2],
        projected[..., 3 * channels :],
        bias_all,
        key_ok,
        chain_ids,
        chain_bias[0],
        0,
        False,
    )
    update = jnp.dot(
        mixed_rows.reshape(-1, channels), row_output, preferred_element_type=jnp.float32
    ).reshape(rows_here, length, channels)
    first_pair = (pair_rep.astype(jnp.float32) + update).astype(jnp.bfloat16)
    normed_first = layer_norm(first_pair).astype(jnp.bfloat16)
    bias_next = jnp.dot(
        normed_first.reshape(-1, channels), col_bias_proj, preferred_element_type=jnp.float32
    )
    bias_next = bias_next.reshape(rows_here, length, head_count).transpose(2, 0, 1)
    lanes = 128
    pair_chunks = (
        first_pair.reshape(rows_here, n_col, n_row, rows_here, channels)
        .transpose(2, 1, 0, 3, 4)
        .reshape(device_count, rows_here * rows_here * channels // lanes, lanes)
    )
    bias_high = bias_next.astype(jnp.bfloat16)
    bias_low = (bias_next - bias_high.astype(jnp.float32)).astype(jnp.bfloat16)
    bias_words = jnp.stack([bias_high, bias_low], axis=0).reshape(1, -1, lanes)
    bias_chunks = jnp.broadcast_to(bias_words, (device_count,) + bias_words.shape[1:])
    merged = lax.all_to_all(
        jnp.concatenate([pair_chunks, bias_chunks], axis=1), ("row", "col"), 0, 0, tiled=True
    )
    pair_rows = pair_chunks.shape[1]
    columns = (
        merged[:, :pair_rows]
        .reshape(device_count, rows_here, rows_here, channels)
        .transpose(2, 0, 1, 3)
        .reshape(rows_here, length, channels)
    )
    bias_got = (
        merged[:, pair_rows:]
        .reshape(device_count, 2, head_count, rows_here, length)
        .astype(jnp.float32)
    )
    bias_cols = (
        (bias_got[:, 0] + bias_got[:, 1])
        .transpose(1, 0, 2, 3)
        .reshape(head_count, length, length)
    )
    normed_cols = layer_norm(columns).astype(jnp.bfloat16)
    projected_cols = jnp.dot(
        normed_cols.reshape(-1, channels), col_project, preferred_element_type=jnp.float32
    ).reshape(rows_here, length, 4 * channels)
    qkv_cols = (
        projected_cols[..., : 3 * channels]
        .astype(jnp.bfloat16)
        .reshape(rows_here, length, 3, head_count, head_size)
    )
    col_ok = tile_rows(local_cols, tile_mask.T, length)
    mixed_cols = attend_lines(
        qkv_cols[:, :, 0],
        qkv_cols[:, :, 1],
        qkv_cols[:, :, 2],
        projected_cols[..., 3 * channels :],
        bias_cols,
        col_ok,
        chain_ids,
        chain_bias[1],
        0,
        True,
    )
    update_cols = jnp.dot(
        mixed_cols.reshape(-1, channels), col_output, preferred_element_type=jnp.float32
    ).reshape(rows_here, length, channels)
    second_pair = (columns.astype(jnp.float32) + update_cols).astype(jnp.bfloat16)
    normed_second = layer_norm(second_pair).astype(jnp.bfloat16)
    edge_mask = tile_pairs(local_cols, jnp.arange(length, dtype=jnp.int32), tile_mask.T, length)
    both = jnp.dot(
        normed_second.reshape(-1, channels),
        jnp.concatenate([tri_left, tri_right], axis=1),
        preferred_element_type=jnp.float32,
    ).reshape(normed_second.shape[:2] + (4 * channels,))
    left_all, right_all = (
        (
            jax.nn.sigmoid(half[..., channels:]) * half[..., :channels] * edge_mask[..., None]
        ).astype(jnp.bfloat16)
        for half in (both[..., : 2 * channels], both[..., 2 * channels :])
    )
    channels_here = channels // device_count
    edges = jnp.stack([left_all, right_all], axis=0).transpose(3, 0, 1, 2)
    edges_got = lax.all_to_all(edges, ("row", "col"), 0, 2, tiled=True)
    product_part = jnp.einsum(
        "cki,ckj->cij",
        edges_got[:, 0],
        edges_got[:, 1],
        preferred_element_type=jnp.float32,
    )
    product_sent = (
        product_part.reshape(channels_here, n_row, block_rows, n_col, block_cols)
        .transpose(1, 3, 0, 2, 4)
        .reshape(device_count, channels_here, block_rows, block_cols)
    )
    raw_chunks = second_pair.reshape(rows_here, n_row, block_rows, channels).transpose(1, 2, 0, 3)
    early = n_row // 2 - 1
    raw_pieces = [lax.dynamic_index_in_dim(raw_chunks, row_index, 0, keepdims=False)]
    for shift in range(1, n_row):
        if shift == early + 1:
            product_sent, raw_chunks = lax.optimization_barrier((product_sent, raw_chunks))
        piece = lax.dynamic_index_in_dim(raw_chunks, (row_index + shift) % n_row, 0, keepdims=False)
        raw_pieces.append(
            lax.ppermute(piece, "row", perm=[(r, (r + shift) % n_row) for r in range(n_row)])
        )
    sources = (row_index - jnp.arange(n_row, dtype=jnp.int32)) % n_row
    raw_got = jnp.take(jnp.stack(raw_pieces, axis=0), sources, axis=0)
    own_pair = raw_got.transpose(1, 0, 2, 3).reshape(block_rows, block_cols, channels)
    product_got = lax.all_to_all(
        product_sent.reshape(device_count, -1, lanes), ("row", "col"), 0, 0, tiled=True
    )
    product_sum = product_got.reshape(channels, block_rows, block_cols).transpose(1, 2, 0)
    normed_own = layer_norm(own_pair).astype(jnp.bfloat16)
    gate_values = jax.nn.sigmoid(
        jnp.dot(normed_own.reshape(-1, channels), tri_gate, preferred_element_type=jnp.float32)
    ).reshape(block_rows, block_cols, channels)
    centered = layer_norm(product_sum).astype(jnp.bfloat16)
    update_tri = jnp.dot(
        centered.reshape(-1, channels), tri_output, preferred_element_type=jnp.float32
    ).reshape(block_rows, block_cols, channels)
    return (own_pair.astype(jnp.float32) + gate_values * update_tri).astype(jnp.bfloat16)


def solution(mesh):
    return jax.shard_map(
        shards,
        mesh=mesh,
        in_specs=(
            P(("row", "col"), None, None),
            P(),
            P(),
            P(),
            P(),
            P(),
            P(),
            P(),
            P(),
            P(),
            P(),
            P(),
            P(),
            P(),
        ),
        out_specs=P("row", "col", None),
        check_vma=False,
    )
```

```python
import jax
import jax.numpy as jnp
from jax import lax
from jax.sharding import PartitionSpec as P


def layer_norm(values):
    values = values.astype(jnp.float32)
    center = values - jnp.mean(values, axis=-1, keepdims=True)
    spread = jnp.mean(center * center, axis=-1, keepdims=True)
    return center * lax.rsqrt(spread + 1e-05)


def tile_rows(positions, tile_table, length):
    tile_count = tile_table.shape[0]
    tile_width = length // tile_count
    onehot = (positions[:, None] // tile_width == jnp.arange(tile_count)[None, :]).astype(
        jnp.float32
    )
    picked = jnp.dot(onehot, tile_table.astype(jnp.float32))
    spread_out = jnp.broadcast_to(picked[:, :, None], (positions.shape[0], tile_count, tile_width))
    return spread_out.reshape(positions.shape[0], length) > 0.5


def tile_pairs(row_pos, col_pos, tile_table, length):
    tile_count = tile_table.shape[0]
    tile_width = length // tile_count
    row_hot = (row_pos[:, None] // tile_width == jnp.arange(tile_count)[None, :]).astype(
        jnp.float32
    )
    col_hot = (col_pos[:, None] // tile_width == jnp.arange(tile_count)[None, :]).astype(
        jnp.float32
    )
    return jnp.dot(jnp.dot(row_hot, tile_table.astype(jnp.float32)), col_hot.T)


def attend_lines(
    queries,
    key_rows,
    value_rows,
    gate_pre,
    bias_all,
    key_ok,
    chain_ids,
    chain_add,
    line_dim,
    flipped,
):
    length = queries.shape[1 - line_dim]
    head_count = queries.shape[2]
    head_size = queries.shape[3]
    width_all = head_count * head_size
    query_rows = min(128, length)
    blocks = length // query_rows
    scaling = head_size ** (-0.5)
    spec_q = "lqhd" if line_dim == 0 else "qlhd"
    spec_k = "lkhd" if line_dim == 0 else "klhd"
    usable = key_ok[:, None, None, :]
    if flipped:
        bias_all = bias_all.transpose(0, 2, 1)
    same_all = (chain_ids[:, None] == chain_ids[None, :]).astype(jnp.float32)
    bias_all = bias_all + chain_add[:, None, None] * same_all[None]

    def one_block(offset):
        query_block = lax.dynamic_slice_in_dim(queries, offset, query_rows, 1 - line_dim)
        scores = (
            jnp.einsum(
                f"{spec_q},{spec_k}->lhqk",
                query_block,
                key_rows,
                preferred_element_type=jnp.float32,
            )
            * scaling
        )
        bias_block = lax.dynamic_slice_in_dim(bias_all, offset, query_rows, 1)
        scores = scores + bias_block[None]
        scores = jnp.where(usable, scores, -1000000000.0)
        row_peak = jnp.max(scores, axis=-1, keepdims=True)
        weights = jnp.exp(scores - row_peak)
        attention = (weights / jnp.sum(weights, axis=-1, keepdims=True)).astype(jnp.bfloat16)
        mixed_rows = jnp.einsum(
            f"lhqk,{spec_k}->{spec_q}", attention, value_rows, preferred_element_type=jnp.float32
        )
        mixed_rows = mixed_rows.reshape(mixed_rows.shape[:2] + (width_all,))
        gate_block = lax.dynamic_slice_in_dim(gate_pre, offset, query_rows, 1 - line_dim)
        return (mixed_rows * jax.nn.sigmoid(gate_block)).astype(jnp.bfloat16)

    if blocks == 1:
        return one_block(0)
    outputs = lax.map(one_block, jnp.arange(blocks, dtype=jnp.int32) * query_rows)
    if line_dim == 0:
        outputs = outputs.transpose(1, 0, 2, 3)
    return outputs.reshape(gate_pre.shape[:2] + (width_all,))


def tri_acts(normed, weights, allowed):
    channels = normed.shape[-1]
    projected = jnp.dot(normed.reshape(-1, channels), weights, preferred_element_type=jnp.float32)
    projected = projected.reshape(normed.shape[0], normed.shape[1], 2 * channels)
    return (
        jax.nn.sigmoid(projected[..., channels:]) * projected[..., :channels] * allowed[..., None]
    ).astype(jnp.bfloat16)


def gather_lines(piece):
    device_count = lax.axis_size("row") * lax.axis_size("col")
    sent = jnp.broadcast_to(piece[None], (device_count,) + piece.shape)
    got = lax.all_to_all(sent, ("row", "col"), 0, 0, tiled=True)
    heads, rows_here, length = piece.shape
    return got.transpose(1, 0, 2, 3).reshape(heads, device_count * rows_here, length)


def shards(
    pair_rep,
    tile_mask,
    chain_ids,
    chain_bias,
    row_project,
    row_bias_proj,
    row_output,
    col_project,
    col_bias_proj,
    col_output,
    tri_left,
    tri_right,
    tri_gate,
    tri_output,
):
    n_row = lax.axis_size("row")
    n_col = lax.axis_size("col")
    device_count = n_row * n_col
    rows_here, length, channels = pair_rep.shape
    head_count = row_bias_proj.shape[1]
    head_size = channels // head_count
    row_index = lax.axis_index("row")
    col_index = lax.axis_index("col")
    device_index = row_index * n_col + col_index
    block_rows = length // n_row
    block_cols = length // n_col
    local_lines = device_index * rows_here + jnp.arange(rows_here, dtype=jnp.int32)
    local_cols = col_index * block_cols + row_index * rows_here + jnp.arange(rows_here, dtype=jnp.int32)
    normed = layer_norm(pair_rep).astype(jnp.bfloat16)
    flat_rows = normed.reshape(rows_here * length, channels)
    bias_rows = jnp.dot(flat_rows, row_bias_proj, preferred_element_type=jnp.float32)
    bias_rows = bias_rows.reshape(rows_here, length, head_count).transpose(2, 0, 1)
    bias_all = gather_lines(bias_rows)
    projected = jnp.dot(flat_rows, row_project, preferred_element_type=jnp.float32).reshape(
        rows_here, length, 4 * channels
    )
    qkv_rows = (
        projected[..., : 3 * channels]
        .astype(jnp.bfloat16)
        .reshape(rows_here, length, 3, head_count, head_size)
    )
    key_ok = tile_rows(local_lines, tile_mask, length)
    mixed_rows = attend_lines(
        qkv_rows[:, :, 0],
        qkv_rows[:, :, 1],
        qkv_rows[:, :, 2],
        projected[..., 3 * channels :],
        bias_all,
        key_ok,
        chain_ids,
        chain_bias[0],
        0,
        False,
    )
    update = jnp.dot(
        mixed_rows.reshape(-1, channels), row_output, preferred_element_type=jnp.float32
    ).reshape(rows_here, length, channels)
    first_pair = (pair_rep.astype(jnp.float32) + update).astype(jnp.bfloat16)
    normed_first = layer_norm(first_pair).astype(jnp.bfloat16)
    bias_next = jnp.dot(
        normed_first.reshape(-1, channels), col_bias_proj, preferred_element_type=jnp.float32
    )
    bias_next = bias_next.reshape(rows_here, length, head_count).transpose(2, 0, 1)
    lanes = 128
    pair_chunks = (
        first_pair.reshape(rows_here, n_col, n_row, rows_here, channels)
        .transpose(2, 1, 0, 3, 4)
        .reshape(device_count, rows_here * rows_here * channels // lanes, lanes)
    )
    bias_high = bias_next.astype(jnp.bfloat16)
    bias_low = (bias_next - bias_high.astype(jnp.float32)).astype(jnp.bfloat16)
    bias_words = jnp.stack([bias_high, bias_low], axis=0).reshape(1, -1, lanes)
    bias_chunks = jnp.broadcast_to(bias_words, (device_count,) + bias_words.shape[1:])
    merged = lax.all_to_all(
        jnp.concatenate([pair_chunks, bias_chunks], axis=1), ("row", "col"), 0, 0, tiled=True
    )
    pair_rows = pair_chunks.shape[1]
    columns = (
        merged[:, :pair_rows]
        .reshape(device_count, rows_here, rows_here, channels)
        .transpose(2, 0, 1, 3)
        .reshape(rows_here, length, channels)
    )
    bias_got = (
        merged[:, pair_rows:]
        .reshape(device_count, 2, head_count, rows_here, length)
        .astype(jnp.float32)
    )
    bias_cols = (
        (bias_got[:, 0] + bias_got[:, 1])
        .transpose(1, 0, 2, 3)
        .reshape(head_count, length, length)
    )
    normed_cols = layer_norm(columns).astype(jnp.bfloat16)
    projected_cols = jnp.dot(
        normed_cols.reshape(-1, channels), col_project, preferred_element_type=jnp.float32
    ).reshape(rows_here, length, 4 * channels)
    qkv_cols = (
        projected_cols[..., : 3 * channels]
        .astype(jnp.bfloat16)
        .reshape(rows_here, length, 3, head_count, head_size)
    )
    col_ok = tile_rows(local_cols, tile_mask.T, length)
    mixed_cols = attend_lines(
        qkv_cols[:, :, 0],
        qkv_cols[:, :, 1],
        qkv_cols[:, :, 2],
        projected_cols[..., 3 * channels :],
        bias_cols,
        col_ok,
        chain_ids,
        chain_bias[1],
        0,
        True,
    )
    update_cols = jnp.dot(
        mixed_cols.reshape(-1, channels), col_output, preferred_element_type=jnp.float32
    ).reshape(rows_here, length, channels)
    second_pair = (columns.astype(jnp.float32) + update_cols).astype(jnp.bfloat16)
    normed_second = layer_norm(second_pair).astype(jnp.bfloat16)
    edge_mask = tile_pairs(local_cols, jnp.arange(length, dtype=jnp.int32), tile_mask.T, length)
    both = jnp.dot(
        normed_second.reshape(-1, channels),
        jnp.concatenate([tri_left, tri_right], axis=1),
        preferred_element_type=jnp.float32,
    ).reshape(normed_second.shape[:2] + (4 * channels,))
    left_all, right_all = (
        (
            jax.nn.sigmoid(half[..., channels:]) * half[..., :channels] * edge_mask[..., None]
        ).astype(jnp.bfloat16)
        for half in (both[..., : 2 * channels], both[..., 2 * channels :])
    )
    channels_here = channels // device_count
    edges = jnp.stack([left_all, right_all], axis=0).transpose(3, 0, 1, 2)
    edges_got = lax.all_to_all(edges, ("row", "col"), 0, 2, tiled=True)
    product_part = jnp.einsum(
        "cki,ckj->cij",
        edges_got[:, 0],
        edges_got[:, 1],
        preferred_element_type=jnp.float32,
    )
    product_sent = (
        product_part.reshape(channels_here, n_row, block_rows, n_col, block_cols)
        .transpose(1, 3, 0, 2, 4)
        .reshape(device_count, channels_here, block_rows, block_cols)
    )
    raw_chunks = second_pair.reshape(rows_here, n_row, block_rows, channels).transpose(1, 2, 0, 3)
    early = n_row // 2
    raw_pieces = [lax.dynamic_index_in_dim(raw_chunks, row_index, 0, keepdims=False)]
    for shift in range(1, n_row):
        if shift == early + 1:
            product_sent, raw_chunks = lax.optimization_barrier((product_sent, raw_chunks))
        piece = lax.dynamic_index_in_dim(raw_chunks, (row_index + shift) % n_row, 0, keepdims=False)
        raw_pieces.append(
            lax.ppermute(piece, "row", perm=[(r, (r + shift) % n_row) for r in range(n_row)])
        )
    sources = (row_index - jnp.arange(n_row, dtype=jnp.int32)) % n_row
    raw_got = jnp.take(jnp.stack(raw_pieces, axis=0), sources, axis=0)
    own_pair = raw_got.transpose(1, 0, 2, 3).reshape(block_rows, block_cols, channels)
    product_got = lax.all_to_all(
        product_sent.reshape(device_count, -1, lanes), ("row", "col"), 0, 0, tiled=True
    )
    product_sum = product_got.reshape(channels, block_rows, block_cols).transpose(1, 2, 0)
    normed_own = layer_norm(own_pair).astype(jnp.bfloat16)
    gate_values = jax.nn.sigmoid(
        jnp.dot(normed_own.reshape(-1, channels), tri_gate, preferred_element_type=jnp.float32)
    ).reshape(block_rows, block_cols, channels)
    centered = layer_norm(product_sum).astype(jnp.bfloat16)
    update_tri = jnp.dot(
        centered.reshape(-1, channels), tri_output, preferred_element_type=jnp.float32
    ).reshape(block_rows, block_cols, channels)
    return (own_pair.astype(jnp.float32) + gate_values * update_tri).astype(jnp.bfloat16)


def solution(mesh):
    return jax.shard_map(
        shards,
        mesh=mesh,
        in_specs=(
            P(("row", "col"), None, None),
            P(),
            P(),
            P(),
            P(),
            P(),
            P(),
            P(),
            P(),
            P(),
            P(),
            P(),
            P(),
            P(),
        ),
        out_specs=P("row", "col", None),
        check_vma=False,
    )
```

```python
import jax
import jax.numpy as jnp
from jax import lax
from jax.sharding import PartitionSpec as P


def layer_norm(values):
    values = values.astype(jnp.float32)
    center = values - jnp.mean(values, axis=-1, keepdims=True)
    spread = jnp.mean(center * center, axis=-1, keepdims=True)
    return center * lax.rsqrt(spread + 1e-05)


def tile_rows(positions, tile_table, length):
    tile_count = tile_table.shape[0]
    tile_width = length // tile_count
    onehot = (positions[:, None] // tile_width == jnp.arange(tile_count)[None, :]).astype(
        jnp.float32
    )
    picked = jnp.dot(onehot, tile_table.astype(jnp.float32))
    spread_out = jnp.broadcast_to(picked[:, :, None], (positions.shape[0], tile_count, tile_width))
    return spread_out.reshape(positions.shape[0], length) > 0.5


def tile_pairs(row_pos, col_pos, tile_table, length):
    tile_count = tile_table.shape[0]
    tile_width = length // tile_count
    row_hot = (row_pos[:, None] // tile_width == jnp.arange(tile_count)[None, :]).astype(
        jnp.float32
    )
    col_hot = (col_pos[:, None] // tile_width == jnp.arange(tile_count)[None, :]).astype(
        jnp.float32
    )
    return jnp.dot(jnp.dot(row_hot, tile_table.astype(jnp.float32)), col_hot.T)


def attend_lines(
    queries,
    key_rows,
    value_rows,
    gate_pre,
    bias_all,
    key_ok,
    chain_ids,
    chain_add,
    line_dim,
    flipped,
):
    length = queries.shape[1 - line_dim]
    head_count = queries.shape[2]
    head_size = queries.shape[3]
    width_all = head_count * head_size
    query_rows = min(128, length)
    blocks = length // query_rows
    scaling = head_size ** (-0.5)
    spec_q = "lqhd" if line_dim == 0 else "qlhd"
    spec_k = "lkhd" if line_dim == 0 else "klhd"
    usable = key_ok[:, None, None, :]
    if flipped:
        bias_all = bias_all.transpose(0, 2, 1)
    same_all = (chain_ids[:, None] == chain_ids[None, :]).astype(jnp.float32)
    bias_all = bias_all + chain_add[:, None, None] * same_all[None]

    def one_block(offset):
        query_block = lax.dynamic_slice_in_dim(queries, offset, query_rows, 1 - line_dim)
        scores = (
            jnp.einsum(
                f"{spec_q},{spec_k}->lhqk",
                query_block,
                key_rows,
                preferred_element_type=jnp.float32,
            )
            * scaling
        )
        bias_block = lax.dynamic_slice_in_dim(bias_all, offset, query_rows, 1)
        scores = scores + bias_block[None]
        scores = jnp.where(usable, scores, -1000000000.0)
        row_peak = jnp.max(scores, axis=-1, keepdims=True)
        weights = jnp.exp(scores - row_peak)
        attention = (weights / jnp.sum(weights, axis=-1, keepdims=True)).astype(jnp.bfloat16)
        mixed_rows = jnp.einsum(
            f"lhqk,{spec_k}->{spec_q}", attention, value_rows, preferred_element_type=jnp.float32
        )
        mixed_rows = mixed_rows.reshape(mixed_rows.shape[:2] + (width_all,))
        gate_block = lax.dynamic_slice_in_dim(gate_pre, offset, query_rows, 1 - line_dim)
        return (mixed_rows * jax.nn.sigmoid(gate_block)).astype(jnp.bfloat16)

    if blocks == 1:
        return one_block(0)
    outputs = lax.map(one_block, jnp.arange(blocks, dtype=jnp.int32) * query_rows)
    if line_dim == 0:
        outputs = outputs.transpose(1, 0, 2, 3)
    return outputs.reshape(gate_pre.shape[:2] + (width_all,))


def tri_acts(normed, weights, allowed):
    channels = normed.shape[-1]
    projected = jnp.dot(normed.reshape(-1, channels), weights, preferred_element_type=jnp.float32)
    projected = projected.reshape(normed.shape[0], normed.shape[1], 2 * channels)
    return (
        jax.nn.sigmoid(projected[..., channels:]) * projected[..., :channels] * allowed[..., None]
    ).astype(jnp.bfloat16)


def gather_lines(piece):
    device_count = lax.axis_size("row") * lax.axis_size("col")
    sent = jnp.broadcast_to(piece[None], (device_count,) + piece.shape)
    got = lax.all_to_all(sent, ("row", "col"), 0, 0, tiled=True)
    heads, rows_here, length = piece.shape
    return got.transpose(1, 0, 2, 3).reshape(heads, device_count * rows_here, length)


def shards(
    pair_rep,
    tile_mask,
    chain_ids,
    chain_bias,
    row_project,
    row_bias_proj,
    row_output,
    col_project,
    col_bias_proj,
    col_output,
    tri_left,
    tri_right,
    tri_gate,
    tri_output,
):
    n_row = lax.axis_size("row")
    n_col = lax.axis_size("col")
    device_count = n_row * n_col
    rows_here, length, channels = pair_rep.shape
    head_count = row_bias_proj.shape[1]
    head_size = channels // head_count
    row_index = lax.axis_index("row")
    col_index = lax.axis_index("col")
    device_index = row_index * n_col + col_index
    block_rows = length // n_row
    block_cols = length // n_col
    local_lines = device_index * rows_here + jnp.arange(rows_here, dtype=jnp.int32)
    local_cols = col_index * block_cols + row_index * rows_here + jnp.arange(rows_here, dtype=jnp.int32)
    normed = layer_norm(pair_rep).astype(jnp.bfloat16)
    flat_rows = normed.reshape(rows_here * length, channels)
    bias_rows = jnp.dot(flat_rows, row_bias_proj, preferred_element_type=jnp.float32)
    bias_rows = bias_rows.reshape(rows_here, length, head_count).transpose(2, 0, 1)
    bias_all = gather_lines(bias_rows)
    projected = jnp.dot(flat_rows, row_project, preferred_element_type=jnp.float32).reshape(
        rows_here, length, 4 * channels
    )
    qkv_rows = (
        projected[..., : 3 * channels]
        .astype(jnp.bfloat16)
        .reshape(rows_here, length, 3, head_count, head_size)
    )
    key_ok = tile_rows(local_lines, tile_mask, length)
    mixed_rows = attend_lines(
        qkv_rows[:, :, 0],
        qkv_rows[:, :, 1],
        qkv_rows[:, :, 2],
        projected[..., 3 * channels :],
        bias_all,
        key_ok,
        chain_ids,
        chain_bias[0],
        0,
        False,
    )
    update = jnp.dot(
        mixed_rows.reshape(-1, channels), row_output, preferred_element_type=jnp.float32
    ).reshape(rows_here, length, channels)
    first_pair = (pair_rep.astype(jnp.float32) + update).astype(jnp.bfloat16)
    normed_first = layer_norm(first_pair).astype(jnp.bfloat16)
    bias_next = jnp.dot(
        normed_first.reshape(-1, channels), col_bias_proj, preferred_element_type=jnp.float32
    )
    bias_next = bias_next.reshape(rows_here, length, head_count).transpose(2, 0, 1)
    lanes = 128
    pair_chunks = (
        first_pair.reshape(rows_here, n_col, n_row, rows_here, channels)
        .transpose(2, 1, 0, 3, 4)
        .reshape(device_count, rows_here * rows_here * channels // lanes, lanes)
    )
    bias_high = bias_next.astype(jnp.bfloat16)
    bias_low = (bias_next - bias_high.astype(jnp.float32)).astype(jnp.bfloat16)
    bias_words = jnp.stack([bias_high, bias_low], axis=0).reshape(1, -1, lanes)
    bias_chunks = jnp.broadcast_to(bias_words, (device_count,) + bias_words.shape[1:])
    merged = lax.all_to_all(
        jnp.concatenate([pair_chunks, bias_chunks], axis=1), ("row", "col"), 0, 0, tiled=True
    )
    pair_rows = pair_chunks.shape[1]
    columns = (
        merged[:, :pair_rows]
        .reshape(device_count, rows_here, rows_here, channels)
        .transpose(2, 0, 1, 3)
        .reshape(rows_here, length, channels)
    )
    bias_got = (
        merged[:, pair_rows:]
        .reshape(device_count, 2, head_count, rows_here, length)
        .astype(jnp.float32)
    )
    bias_cols = (
        (bias_got[:, 0] + bias_got[:, 1])
        .transpose(1, 0, 2, 3)
        .reshape(head_count, length, length)
    )
    normed_cols = layer_norm(columns).astype(jnp.bfloat16)
    projected_cols = jnp.dot(
        normed_cols.reshape(-1, channels), col_project, preferred_element_type=jnp.float32
    ).reshape(rows_here, length, 4 * channels)
    qkv_cols = (
        projected_cols[..., : 3 * channels]
        .astype(jnp.bfloat16)
        .reshape(rows_here, length, 3, head_count, head_size)
    )
    col_ok = tile_rows(local_cols, tile_mask.T, length)
    mixed_cols = attend_lines(
        qkv_cols[:, :, 0],
        qkv_cols[:, :, 1],
        qkv_cols[:, :, 2],
        projected_cols[..., 3 * channels :],
        bias_cols,
        col_ok,
        chain_ids,
        chain_bias[1],
        0,
        True,
    )
    update_cols = jnp.dot(
        mixed_cols.reshape(-1, channels), col_output, preferred_element_type=jnp.float32
    ).reshape(rows_here, length, channels)
    second_pair = (columns.astype(jnp.float32) + update_cols).astype(jnp.bfloat16)
    normed_second = layer_norm(second_pair).astype(jnp.bfloat16)
    edge_mask = tile_pairs(local_cols, jnp.arange(length, dtype=jnp.int32), tile_mask.T, length)
    both = jnp.dot(
        normed_second.reshape(-1, channels),
        jnp.concatenate([tri_left, tri_right], axis=1),
        preferred_element_type=jnp.float32,
    ).reshape(normed_second.shape[:2] + (4 * channels,))
    left_all, right_all = (
        (
            jax.nn.sigmoid(half[..., channels:]) * half[..., :channels] * edge_mask[..., None]
        ).astype(jnp.bfloat16)
        for half in (both[..., : 2 * channels], both[..., 2 * channels :])
    )
    channels_here = channels // device_count
    edges = jnp.stack([left_all, right_all], axis=0).transpose(3, 0, 1, 2)
    edges_got = lax.all_to_all(edges, ("row", "col"), 0, 2, tiled=True)
    product_part = jnp.einsum(
        "cki,ckj->cij",
        edges_got[:, 0],
        edges_got[:, 1],
        preferred_element_type=jnp.float32,
    )
    product_sent = (
        product_part.reshape(channels_here, n_row, block_rows, n_col, block_cols)
        .transpose(1, 3, 0, 2, 4)
        .reshape(device_count, channels_here, block_rows, block_cols)
    )
    raw_chunks = second_pair.reshape(rows_here, n_row, block_rows, channels).transpose(1, 2, 0, 3)
    early = n_row - 3
    raw_pieces = [lax.dynamic_index_in_dim(raw_chunks, row_index, 0, keepdims=False)]
    for shift in range(1, n_row):
        if shift == early + 1:
            product_sent, raw_chunks = lax.optimization_barrier((product_sent, raw_chunks))
        piece = lax.dynamic_index_in_dim(raw_chunks, (row_index + shift) % n_row, 0, keepdims=False)
        raw_pieces.append(
            lax.ppermute(piece, "row", perm=[(r, (r + shift) % n_row) for r in range(n_row)])
        )
    sources = (row_index - jnp.arange(n_row, dtype=jnp.int32)) % n_row
    raw_got = jnp.take(jnp.stack(raw_pieces, axis=0), sources, axis=0)
    own_pair = raw_got.transpose(1, 0, 2, 3).reshape(block_rows, block_cols, channels)
    product_got = lax.all_to_all(
        product_sent.reshape(device_count, -1, lanes), ("row", "col"), 0, 0, tiled=True
    )
    product_sum = product_got.reshape(channels, block_rows, block_cols).transpose(1, 2, 0)
    normed_own = layer_norm(own_pair).astype(jnp.bfloat16)
    gate_values = jax.nn.sigmoid(
        jnp.dot(normed_own.reshape(-1, channels), tri_gate, preferred_element_type=jnp.float32)
    ).reshape(block_rows, block_cols, channels)
    centered = layer_norm(product_sum).astype(jnp.bfloat16)
    update_tri = jnp.dot(
        centered.reshape(-1, channels), tri_output, preferred_element_type=jnp.float32
    ).reshape(block_rows, block_cols, channels)
    return (own_pair.astype(jnp.float32) + gate_values * update_tri).astype(jnp.bfloat16)


def solution(mesh):
    return jax.shard_map(
        shards,
        mesh=mesh,
        in_specs=(
            P(("row", "col"), None, None),
            P(),
            P(),
            P(),
            P(),
            P(),
            P(),
            P(),
            P(),
            P(),
            P(),
            P(),
            P(),
            P(),
        ),
        out_specs=P("row", "col", None),
        check_vma=False,
    )
```

```python
import jax
import jax.numpy as jnp
from jax import lax
from jax.sharding import PartitionSpec as P


def layer_norm(values):
    values = values.astype(jnp.float32)
    center = values - jnp.mean(values, axis=-1, keepdims=True)
    spread = jnp.mean(center * center, axis=-1, keepdims=True)
    return center * lax.rsqrt(spread + 1e-05)


def tile_rows(positions, tile_table, length):
    tile_count = tile_table.shape[0]
    tile_width = length // tile_count
    onehot = (positions[:, None] // tile_width == jnp.arange(tile_count)[None, :]).astype(
        jnp.float32
    )
    picked = jnp.dot(onehot, tile_table.astype(jnp.float32))
    spread_out = jnp.broadcast_to(picked[:, :, None], (positions.shape[0], tile_count, tile_width))
    return spread_out.reshape(positions.shape[0], length) > 0.5


def tile_pairs(row_pos, col_pos, tile_table, length):
    tile_count = tile_table.shape[0]
    tile_width = length // tile_count
    row_hot = (row_pos[:, None] // tile_width == jnp.arange(tile_count)[None, :]).astype(
        jnp.float32
    )
    col_hot = (col_pos[:, None] // tile_width == jnp.arange(tile_count)[None, :]).astype(
        jnp.float32
    )
    return jnp.dot(jnp.dot(row_hot, tile_table.astype(jnp.float32)), col_hot.T)


def attend_lines(
    queries,
    key_rows,
    value_rows,
    gate_pre,
    bias_all,
    key_ok,
    chain_ids,
    chain_add,
    line_dim,
    flipped,
):
    length = queries.shape[1 - line_dim]
    head_count = queries.shape[2]
    head_size = queries.shape[3]
    width_all = head_count * head_size
    query_rows = min(128, length)
    blocks = length // query_rows
    scaling = head_size ** (-0.5)
    spec_q = "lqhd" if line_dim == 0 else "qlhd"
    spec_k = "lkhd" if line_dim == 0 else "klhd"
    usable = key_ok[:, None, None, :]
    if flipped:
        bias_all = bias_all.transpose(0, 2, 1)
    same_all = (chain_ids[:, None] == chain_ids[None, :]).astype(jnp.float32)
    bias_all = bias_all + chain_add[:, None, None] * same_all[None]

    def one_block(offset):
        query_block = lax.dynamic_slice_in_dim(queries, offset, query_rows, 1 - line_dim)
        scores = (
            jnp.einsum(
                f"{spec_q},{spec_k}->lhqk",
                query_block,
                key_rows,
                preferred_element_type=jnp.float32,
            )
            * scaling
        )
        bias_block = lax.dynamic_slice_in_dim(bias_all, offset, query_rows, 1)
        scores = scores + bias_block[None]
        scores = jnp.where(usable, scores, -1000000000.0)
        row_peak = jnp.max(scores, axis=-1, keepdims=True)
        weights = jnp.exp(scores - row_peak)
        attention = (weights / jnp.sum(weights, axis=-1, keepdims=True)).astype(jnp.bfloat16)
        mixed_rows = jnp.einsum(
            f"lhqk,{spec_k}->{spec_q}", attention, value_rows, preferred_element_type=jnp.float32
        )
        mixed_rows = mixed_rows.reshape(mixed_rows.shape[:2] + (width_all,))
        gate_block = lax.dynamic_slice_in_dim(gate_pre, offset, query_rows, 1 - line_dim)
        return (mixed_rows * jax.nn.sigmoid(gate_block)).astype(jnp.bfloat16)

    if blocks == 1:
        return one_block(0)
    outputs = lax.map(one_block, jnp.arange(blocks, dtype=jnp.int32) * query_rows)
    if line_dim == 0:
        outputs = outputs.transpose(1, 0, 2, 3)
    return outputs.reshape(gate_pre.shape[:2] + (width_all,))


def tri_acts(normed, weights, allowed):
    channels = normed.shape[-1]
    projected = jnp.dot(normed.reshape(-1, channels), weights, preferred_element_type=jnp.float32)
    projected = projected.reshape(normed.shape[0], normed.shape[1], 2 * channels)
    return (
        jax.nn.sigmoid(projected[..., channels:]) * projected[..., :channels] * allowed[..., None]
    ).astype(jnp.bfloat16)


def gather_lines(piece):
    device_count = lax.axis_size("row") * lax.axis_size("col")
    sent = jnp.broadcast_to(piece[None], (device_count,) + piece.shape)
    got = lax.all_to_all(sent, ("row", "col"), 0, 0, tiled=True)
    heads, rows_here, length = piece.shape
    return got.transpose(1, 0, 2, 3).reshape(heads, device_count * rows_here, length)


def shards(
    pair_rep,
    tile_mask,
    chain_ids,
    chain_bias,
    row_project,
    row_bias_proj,
    row_output,
    col_project,
    col_bias_proj,
    col_output,
    tri_left,
    tri_right,
    tri_gate,
    tri_output,
):
    n_row = lax.axis_size("row")
    n_col = lax.axis_size("col")
    device_count = n_row * n_col
    rows_here, length, channels = pair_rep.shape
    head_count = row_bias_proj.shape[1]
    head_size = channels // head_count
    row_index = lax.axis_index("row")
    col_index = lax.axis_index("col")
    device_index = row_index * n_col + col_index
    block_rows = length // n_row
    block_cols = length // n_col
    local_lines = device_index * rows_here + jnp.arange(rows_here, dtype=jnp.int32)
    local_cols = col_index * block_cols + row_index * rows_here + jnp.arange(rows_here, dtype=jnp.int32)
    normed = layer_norm(pair_rep).astype(jnp.bfloat16)
    flat_rows = normed.reshape(rows_here * length, channels)
    bias_rows = jnp.dot(flat_rows, row_bias_proj, preferred_element_type=jnp.float32)
    bias_rows = bias_rows.reshape(rows_here, length, head_count).transpose(2, 0, 1)
    bias_all = gather_lines(bias_rows)
    projected = jnp.dot(flat_rows, row_project, preferred_element_type=jnp.float32).reshape(
        rows_here, length, 4 * channels
    )
    qkv_rows = (
        projected[..., : 3 * channels]
        .astype(jnp.bfloat16)
        .reshape(rows_here, length, 3, head_count, head_size)
    )
    key_ok = tile_rows(local_lines, tile_mask, length)
    mixed_rows = attend_lines(
        qkv_rows[:, :, 0],
        qkv_rows[:, :, 1],
        qkv_rows[:, :, 2],
        projected[..., 3 * channels :],
        bias_all,
        key_ok,
        chain_ids,
        chain_bias[0],
        0,
        False,
    )
    update = jnp.dot(
        mixed_rows.reshape(-1, channels), row_output, preferred_element_type=jnp.float32
    ).reshape(rows_here, length, channels)
    first_pair = (pair_rep.astype(jnp.float32) + update).astype(jnp.bfloat16)
    normed_first = layer_norm(first_pair).astype(jnp.bfloat16)
    bias_next = jnp.dot(
        normed_first.reshape(-1, channels), col_bias_proj, preferred_element_type=jnp.float32
    )
    bias_next = bias_next.reshape(rows_here, length, head_count).transpose(2, 0, 1)
    lanes = 128
    pair_chunks = (
        first_pair.reshape(rows_here, n_col, n_row, rows_here, channels)
        .transpose(2, 1, 0, 3, 4)
        .reshape(device_count, rows_here * rows_here * channels // lanes, lanes)
    )
    bias_high = bias_next.astype(jnp.bfloat16)
    bias_low = (bias_next - bias_high.astype(jnp.float32)).astype(jnp.bfloat16)
    bias_words = jnp.stack([bias_high, bias_low], axis=0).reshape(1, -1, lanes)
    bias_chunks = jnp.broadcast_to(bias_words, (device_count,) + bias_words.shape[1:])
    merged = lax.all_to_all(
        jnp.concatenate([pair_chunks, bias_chunks], axis=1), ("row", "col"), 0, 0, tiled=True
    )
    pair_rows = pair_chunks.shape[1]
    columns = (
        merged[:, :pair_rows]
        .reshape(device_count, rows_here, rows_here, channels)
        .transpose(2, 0, 1, 3)
        .reshape(rows_here, length, channels)
    )
    bias_got = (
        merged[:, pair_rows:]
        .reshape(device_count, 2, head_count, rows_here, length)
        .astype(jnp.float32)
    )
    bias_cols = (
        (bias_got[:, 0] + bias_got[:, 1])
        .transpose(1, 0, 2, 3)
        .reshape(head_count, length, length)
    )
    normed_cols = layer_norm(columns).astype(jnp.bfloat16)
    projected_cols = jnp.dot(
        normed_cols.reshape(-1, channels), col_project, preferred_element_type=jnp.float32
    ).reshape(rows_here, length, 4 * channels)
    qkv_cols = (
        projected_cols[..., : 3 * channels]
        .astype(jnp.bfloat16)
        .reshape(rows_here, length, 3, head_count, head_size)
    )
    col_ok = tile_rows(local_cols, tile_mask.T, length)
    mixed_cols = attend_lines(
        qkv_cols[:, :, 0],
        qkv_cols[:, :, 1],
        qkv_cols[:, :, 2],
        projected_cols[..., 3 * channels :],
        bias_cols,
        col_ok,
        chain_ids,
        chain_bias[1],
        0,
        True,
    )
    update_cols = jnp.dot(
        mixed_cols.reshape(-1, channels), col_output, preferred_element_type=jnp.float32
    ).reshape(rows_here, length, channels)
    second_pair = (columns.astype(jnp.float32) + update_cols).astype(jnp.bfloat16)
    normed_second = layer_norm(second_pair).astype(jnp.bfloat16)
    edge_mask = tile_pairs(local_cols, jnp.arange(length, dtype=jnp.int32), tile_mask.T, length)
    both = jnp.dot(
        normed_second.reshape(-1, channels),
        jnp.concatenate([tri_left, tri_right], axis=1),
        preferred_element_type=jnp.float32,
    ).reshape(normed_second.shape[:2] + (4 * channels,))
    left_all, right_all = (
        (
            jax.nn.sigmoid(half[..., channels:]) * half[..., :channels] * edge_mask[..., None]
        ).astype(jnp.bfloat16)
        for half in (both[..., : 2 * channels], both[..., 2 * channels :])
    )
    channels_here = channels // device_count
    edges = jnp.stack([left_all, right_all], axis=0).transpose(3, 0, 1, 2)
    edges_got = lax.all_to_all(edges, ("row", "col"), 0, 2, tiled=True)
    product_part = jnp.einsum(
        "cki,ckj->cij",
        edges_got[:, 0],
        edges_got[:, 1],
        preferred_element_type=jnp.float32,
    )
    product_sent = (
        product_part.reshape(channels_here, n_row, block_rows, n_col, block_cols)
        .transpose(1, 3, 0, 2, 4)
        .reshape(device_count, channels_here, block_rows, block_cols)
    )
    raw_chunks = second_pair.reshape(rows_here, n_row, block_rows, channels).transpose(1, 2, 0, 3)
    early = n_row // 2
    raw_pieces = [lax.dynamic_index_in_dim(raw_chunks, row_index, 0, keepdims=False)]
    for shift in range(1, n_row):
        if shift == early + 1:
            product_sent, raw_chunks = lax.optimization_barrier((product_sent, raw_chunks))
        piece = lax.dynamic_index_in_dim(raw_chunks, (row_index + shift) % n_row, 0, keepdims=False)
        raw_pieces.append(
            lax.ppermute(piece, "row", perm=[(r, (r + shift) % n_row) for r in range(n_row)])
        )
    doubled = jnp.stack(raw_pieces[::-1] + raw_pieces[::-1], axis=0)
    raw_got = lax.dynamic_slice_in_dim(doubled, (n_row - 1 - row_index) % n_row, n_row, 0)
    own_pair = raw_got.transpose(1, 0, 2, 3).reshape(block_rows, block_cols, channels)
    product_got = lax.all_to_all(
        product_sent.reshape(device_count, -1, lanes), ("row", "col"), 0, 0, tiled=True
    )
    product_sum = product_got.reshape(channels, block_rows, block_cols).transpose(1, 2, 0)
    normed_own = layer_norm(own_pair).astype(jnp.bfloat16)
    gate_values = jax.nn.sigmoid(
        jnp.dot(normed_own.reshape(-1, channels), tri_gate, preferred_element_type=jnp.float32)
    ).reshape(block_rows, block_cols, channels)
    centered = layer_norm(product_sum).astype(jnp.bfloat16)
    update_tri = jnp.dot(
        centered.reshape(-1, channels), tri_output, preferred_element_type=jnp.float32
    ).reshape(block_rows, block_cols, channels)
    return (own_pair.astype(jnp.float32) + gate_values * update_tri).astype(jnp.bfloat16)


def solution(mesh):
    return jax.shard_map(
        shards,
        mesh=mesh,
        in_specs=(
            P(("row", "col"), None, None),
            P(),
            P(),
            P(),
            P(),
            P(),
            P(),
            P(),
            P(),
            P(),
            P(),
            P(),
            P(),
            P(),
        ),
        out_specs=P("row", "col", None),
        check_vma=False,
    )
```

```python
import jax
import jax.numpy as jnp
from jax import lax
from jax.sharding import PartitionSpec as P


def layer_norm(values):
    values = values.astype(jnp.float32)
    center = values - jnp.mean(values, axis=-1, keepdims=True)
    spread = jnp.mean(center * center, axis=-1, keepdims=True)
    return center * lax.rsqrt(spread + 1e-05)


def tile_rows(positions, tile_table, length):
    tile_count = tile_table.shape[0]
    tile_width = length // tile_count
    onehot = (positions[:, None] // tile_width == jnp.arange(tile_count)[None, :]).astype(
        jnp.float32
    )
    picked = jnp.dot(onehot, tile_table.astype(jnp.float32))
    spread_out = jnp.broadcast_to(picked[:, :, None], (positions.shape[0], tile_count, tile_width))
    return spread_out.reshape(positions.shape[0], length) > 0.5


def tile_pairs(row_pos, col_pos, tile_table, length):
    tile_count = tile_table.shape[0]
    tile_width = length // tile_count
    row_hot = (row_pos[:, None] // tile_width == jnp.arange(tile_count)[None, :]).astype(
        jnp.float32
    )
    col_hot = (col_pos[:, None] // tile_width == jnp.arange(tile_count)[None, :]).astype(
        jnp.float32
    )
    return jnp.dot(jnp.dot(row_hot, tile_table.astype(jnp.float32)), col_hot.T)


def attend_lines(
    queries,
    key_rows,
    value_rows,
    gate_pre,
    bias_all,
    key_ok,
    chain_ids,
    chain_add,
    line_dim,
    flipped,
):
    length = queries.shape[1 - line_dim]
    head_count = queries.shape[2]
    head_size = queries.shape[3]
    width_all = head_count * head_size
    query_rows = min(128, length)
    blocks = length // query_rows
    scaling = head_size ** (-0.5)
    spec_q = "lqhd" if line_dim == 0 else "qlhd"
    spec_k = "lkhd" if line_dim == 0 else "klhd"
    usable = key_ok[:, None, None, :]
    if flipped:
        bias_all = bias_all.transpose(0, 2, 1)
    same_all = (chain_ids[:, None] == chain_ids[None, :]).astype(jnp.float32)
    bias_all = bias_all + chain_add[:, None, None] * same_all[None]

    def one_block(offset):
        query_block = lax.dynamic_slice_in_dim(queries, offset, query_rows, 1 - line_dim)
        scores = (
            jnp.einsum(
                f"{spec_q},{spec_k}->lhqk",
                query_block,
                key_rows,
                preferred_element_type=jnp.float32,
            )
            * scaling
        )
        bias_block = lax.dynamic_slice_in_dim(bias_all, offset, query_rows, 1)
        scores = scores + bias_block[None]
        scores = jnp.where(usable, scores, -1000000000.0)
        row_peak = jnp.max(scores, axis=-1, keepdims=True)
        weights = jnp.exp(scores - row_peak)
        attention = (weights / jnp.sum(weights, axis=-1, keepdims=True)).astype(jnp.bfloat16)
        mixed_rows = jnp.einsum(
            f"lhqk,{spec_k}->{spec_q}", attention, value_rows, preferred_element_type=jnp.float32
        )
        mixed_rows = mixed_rows.reshape(mixed_rows.shape[:2] + (width_all,))
        gate_block = lax.dynamic_slice_in_dim(gate_pre, offset, query_rows, 1 - line_dim)
        return (mixed_rows * jax.nn.sigmoid(gate_block)).astype(jnp.bfloat16)

    if blocks == 1:
        return one_block(0)
    outputs = lax.map(one_block, jnp.arange(blocks, dtype=jnp.int32) * query_rows)
    if line_dim == 0:
        outputs = outputs.transpose(1, 0, 2, 3)
    return outputs.reshape(gate_pre.shape[:2] + (width_all,))


def tri_acts(normed, weights, allowed):
    channels = normed.shape[-1]
    projected = jnp.dot(normed.reshape(-1, channels), weights, preferred_element_type=jnp.float32)
    projected = projected.reshape(normed.shape[0], normed.shape[1], 2 * channels)
    return (
        jax.nn.sigmoid(projected[..., channels:]) * projected[..., :channels] * allowed[..., None]
    ).astype(jnp.bfloat16)


def gather_lines(piece):
    device_count = lax.axis_size("row") * lax.axis_size("col")
    sent = jnp.broadcast_to(piece[None], (device_count,) + piece.shape)
    got = lax.all_to_all(sent, ("row", "col"), 0, 0, tiled=True)
    heads, rows_here, length = piece.shape
    return got.transpose(1, 0, 2, 3).reshape(heads, device_count * rows_here, length)


def shards(
    pair_rep,
    tile_mask,
    chain_ids,
    chain_bias,
    row_project,
    row_bias_proj,
    row_output,
    col_project,
    col_bias_proj,
    col_output,
    tri_left,
    tri_right,
    tri_gate,
    tri_output,
):
    n_row = lax.axis_size("row")
    n_col = lax.axis_size("col")
    device_count = n_row * n_col
    rows_here, length, channels = pair_rep.shape
    head_count = row_bias_proj.shape[1]
    head_size = channels // head_count
    row_index = lax.axis_index("row")
    col_index = lax.axis_index("col")
    device_index = row_index * n_col + col_index
    block_rows = length // n_row
    block_cols = length // n_col
    local_lines = device_index * rows_here + jnp.arange(rows_here, dtype=jnp.int32)
    local_cols = col_index * block_cols + row_index * rows_here + jnp.arange(rows_here, dtype=jnp.int32)
    normed = layer_norm(pair_rep).astype(jnp.bfloat16)
    flat_rows = normed.reshape(rows_here * length, channels)
    bias_rows = jnp.dot(flat_rows, row_bias_proj, preferred_element_type=jnp.float32)
    bias_rows = bias_rows.reshape(rows_here, length, head_count).transpose(2, 0, 1)
    bias_all = gather_lines(bias_rows)
    projected = jnp.dot(flat_rows, row_project, preferred_element_type=jnp.float32).reshape(
        rows_here, length, 4 * channels
    )
    qkv_rows = (
        projected[..., : 3 * channels]
        .astype(jnp.bfloat16)
        .reshape(rows_here, length, 3, head_count, head_size)
    )
    key_ok = tile_rows(local_lines, tile_mask, length)
    mixed_rows = attend_lines(
        qkv_rows[:, :, 0],
        qkv_rows[:, :, 1],
        qkv_rows[:, :, 2],
        projected[..., 3 * channels :],
        bias_all,
        key_ok,
        chain_ids,
        chain_bias[0],
        0,
        False,
    )
    update = jnp.dot(
        mixed_rows.reshape(-1, channels), row_output, preferred_element_type=jnp.float32
    ).reshape(rows_here, length, channels)
    first_pair = (pair_rep.astype(jnp.float32) + update).astype(jnp.bfloat16)
    normed_first = layer_norm(first_pair).astype(jnp.bfloat16)
    bias_next = jnp.dot(
        normed_first.reshape(-1, channels), col_bias_proj, preferred_element_type=jnp.float32
    )
    bias_next = bias_next.reshape(rows_here, length, head_count).transpose(2, 0, 1)
    lanes = 128
    pair_chunks = (
        first_pair.reshape(rows_here, n_col, n_row, rows_here, channels)
        .transpose(2, 1, 0, 3, 4)
        .reshape(device_count, rows_here * rows_here * channels // lanes, lanes)
    )
    bias_high = bias_next.astype(jnp.bfloat16)
    bias_low = (bias_next - bias_high.astype(jnp.float32)).astype(jnp.bfloat16)
    bias_words = jnp.stack([bias_high, bias_low], axis=0).reshape(1, -1, lanes)
    bias_chunks = jnp.broadcast_to(bias_words, (device_count,) + bias_words.shape[1:])
    merged = lax.all_to_all(
        jnp.concatenate([pair_chunks, bias_chunks], axis=1), ("row", "col"), 0, 0, tiled=True
    )
    pair_rows = pair_chunks.shape[1]
    columns = (
        merged[:, :pair_rows]
        .reshape(device_count, rows_here, rows_here, channels)
        .transpose(2, 0, 1, 3)
        .reshape(rows_here, length, channels)
    )
    bias_got = (
        merged[:, pair_rows:]
        .reshape(device_count, 2, head_count, rows_here, length)
        .astype(jnp.float32)
    )
    bias_cols = (
        (bias_got[:, 0] + bias_got[:, 1])
        .transpose(1, 0, 2, 3)
        .reshape(head_count, length, length)
    )
    normed_cols = layer_norm(columns).astype(jnp.bfloat16)
    projected_cols = jnp.dot(
        normed_cols.reshape(-1, channels), col_project, preferred_element_type=jnp.float32
    ).reshape(rows_here, length, 4 * channels)
    qkv_cols = (
        projected_cols[..., : 3 * channels]
        .astype(jnp.bfloat16)
        .reshape(rows_here, length, 3, head_count, head_size)
    )
    col_ok = tile_rows(local_cols, tile_mask.T, length)
    mixed_cols = attend_lines(
        qkv_cols[:, :, 0],
        qkv_cols[:, :, 1],
        qkv_cols[:, :, 2],
        projected_cols[..., 3 * channels :],
        bias_cols,
        col_ok,
        chain_ids,
        chain_bias[1],
        0,
        True,
    )
    update_cols = jnp.dot(
        mixed_cols.reshape(-1, channels), col_output, preferred_element_type=jnp.float32
    ).reshape(rows_here, length, channels)
    second_pair = (columns.astype(jnp.float32) + update_cols).astype(jnp.bfloat16)
    normed_second = layer_norm(second_pair).astype(jnp.bfloat16)
    edge_mask = tile_pairs(local_cols, jnp.arange(length, dtype=jnp.int32), tile_mask.T, length)
    both = jnp.dot(
        normed_second.reshape(-1, channels),
        jnp.concatenate([tri_left, tri_right], axis=1),
        preferred_element_type=jnp.float32,
    ).reshape(normed_second.shape[:2] + (4 * channels,))
    left_all, right_all = (
        (
            jax.nn.sigmoid(half[..., channels:]) * half[..., :channels] * edge_mask[..., None]
        ).astype(jnp.bfloat16)
        for half in (both[..., : 2 * channels], both[..., 2 * channels :])
    )
    channels_here = channels // device_count
    edges = jnp.stack([left_all, right_all], axis=0).transpose(3, 0, 1, 2)
    edges_got = lax.all_to_all(edges, ("row", "col"), 0, 2, tiled=True)
    product_part = jnp.einsum(
        "cki,ckj->cij",
        edges_got[:, 0],
        edges_got[:, 1],
        preferred_element_type=jnp.float32,
    )
    product_sent = (
        product_part.reshape(channels_here, n_row, block_rows, n_col, block_cols)
        .transpose(1, 3, 0, 2, 4)
        .reshape(device_count, channels_here, block_rows, block_cols)
    )
    raw_chunks = second_pair.reshape(rows_here, n_row, block_rows, channels).transpose(1, 2, 0, 3)
    early = n_row // 4
    raw_pieces = [lax.dynamic_index_in_dim(raw_chunks, row_index, 0, keepdims=False)]
    for shift in range(1, n_row):
        if shift == early + 1:
            product_sent, raw_chunks = lax.optimization_barrier((product_sent, raw_chunks))
        piece = lax.dynamic_index_in_dim(raw_chunks, (row_index + shift) % n_row, 0, keepdims=False)
        raw_pieces.append(
            lax.ppermute(piece, "row", perm=[(r, (r + shift) % n_row) for r in range(n_row)])
        )
    sources = (row_index - jnp.arange(n_row, dtype=jnp.int32)) % n_row
    raw_got = jnp.take(jnp.stack(raw_pieces, axis=0), sources, axis=0)
    own_pair = raw_got.transpose(1, 0, 2, 3).reshape(block_rows, block_cols, channels)
    product_got = lax.all_to_all(
        product_sent.reshape(device_count, -1, lanes), ("row", "col"), 0, 0, tiled=True
    )
    product_sum = product_got.reshape(channels, block_rows, block_cols).transpose(1, 2, 0)
    normed_own = layer_norm(own_pair).astype(jnp.bfloat16)
    gate_values = jax.nn.sigmoid(
        jnp.dot(normed_own.reshape(-1, channels), tri_gate, preferred_element_type=jnp.float32)
    ).reshape(block_rows, block_cols, channels)
    centered = layer_norm(product_sum).astype(jnp.bfloat16)
    update_tri = jnp.dot(
        centered.reshape(-1, channels), tri_output, preferred_element_type=jnp.float32
    ).reshape(block_rows, block_cols, channels)
    return (own_pair.astype(jnp.float32) + gate_values * update_tri).astype(jnp.bfloat16)


def solution(mesh):
    return jax.shard_map(
        shards,
        mesh=mesh,
        in_specs=(
            P(("row", "col"), None, None),
            P(),
            P(),
            P(),
            P(),
            P(),
            P(),
            P(),
            P(),
            P(),
            P(),
            P(),
            P(),
            P(),
        ),
        out_specs=P("row", "col", None),
        check_vma=False,
    )
```
